32 devices in a mesh: group: 2 (over y), row: 16 (over z, x, core).
Axes of the slice: x: 2, y: 2, z: 4, core: 2. Of those that a mesh axis runs over, the one named last changes fastest.
Arguments:
- image: bfloat16 [128, 256, 256], P(('group', 'row')), parts along dimension 0, may hold values from -6 to 6
- tissue: int32 [32, 2], P(('group', 'row')), parts along dimension 0, may hold values from 0 to 1, as said below
- kernel: float32 [7, 7, 256], replicated, may hold values from -0.875 to 0.875
- ln_gain: float32 [256], replicated, may hold values from 0.5 to 1.5
- w_in: bfloat16 [256, 1024], replicated, may hold values from -0.375 to 0.375
- w_out: bfloat16 [1024, 256], replicated, may hold values from -0.1875 to 0.1875
- layer_scale: float32 [256], replicated, may hold values from 0.5 to 1.5
- cotangent: bfloat16 [128, 256, 256], P(('group', 'row')), parts along dimension 0, may hold values from -6 to 6
Outputs:
- block_out: bfloat16 [128, 256, 256], P(('group', 'row')), parts along dimension 0
- grad_image: bfloat16 [128, 256, 256], P(('group', 'row')), parts along dimension 0
- grad_w_in: float32 [512, 1024], P(('group', 'row')), parts along dimension 0
- grad_w_out: float32 [2048, 256], P(('group', 'row')), parts along dimension 0
- small_grads: float32 [102, 256], P('group'), parts along dimension 0
The draws below stay inside these ranges and needn't reach their ends.
There are 2 independent parts, one for each index of `group`. The reference program is written for one: setup_inputs(seed, part) draws one part's arguments, and reference() takes and returns one part's arrays. A program takes and returns all parts, laid end to end along the dimension named above; an argument that names none is the same for every part. Nothing has to cross between parts.
Inputs may be any that keep to these rules, and one draw needn't show every extreme that they name: 1 marks a tile of 4 x 128 positions that holds tissue, 0 one without. Among the 2 tiles of the 4 rows of one device, at least one is 0 and at least one is 1.
All inputs are finite; a program needn't handle non-finite values.
Results may differ from the reference program's by a relative error of at most 0.0063.
Values may be sent and summed in bfloat16 or wider, within the bound.
No kernel may reach another device: no remote copies, remote signals or barrier semaphores. Data moves between devices by JAX's collectives and lax.ppermute only.
A program may use at most 64 MiB of HBM per device.

```python
import jax
import jax.numpy as jnp
from jax import lax

C = 256
FF = 1024
KERNEL = 7
TILE_ROWS = 4
TILE_COLS = 128
ROWS_DEV = 4
COLS = 256
ROWS = 64


def draw_tissue(key, part):
    tile_rows = ROWS // TILE_ROWS
    tile_cols = COLS // TILE_COLS
    device_blocks = ROWS // ROWS_DEV
    tiles_dev = ROWS_DEV // TILE_ROWS * tile_cols
    emptied = max(1, tiles_dev // 4)
    ballots = jax.random.randint(jax.random.fold_in(key, 11), (tile_rows, tile_cols), 0, 100)
    ceiling = 25 + jnp.arange(tile_rows, dtype=jnp.int32) * 45 // tile_rows
    marked = (ballots < ceiling[:, None]).astype(jnp.int32)
    scores = jax.random.randint(jax.random.fold_in(key, 23), (device_blocks, tiles_dev), 0, 1048576)
    scores = scores * tiles_dev + jnp.arange(tiles_dev, dtype=jnp.int32)[None, :]
    order = jnp.argsort(scores, axis=1)
    ranks = jnp.argsort(order, axis=1).astype(jnp.int32)
    keep = (ranks >= emptied).astype(jnp.int32)
    forced = (ranks == tiles_dev - 1).astype(jnp.int32)
    marked = jnp.maximum(marked.reshape(device_blocks, tiles_dev) * keep, forced)
    return marked.reshape(tile_rows, tile_cols)


def shard_levels(own_key, dims, cuts, smallest, largest):
    def one(dim, parts):
        heights = jax.random.uniform(jax.random.fold_in(jax.random.fold_in(own_key, 6), dim), (parts,), jnp.float32, smallest / len(cuts), largest / len(cuts))
        return jnp.repeat(jnp.exp(heights), dims[dim] // parts).reshape((-1,) + (1,) * (len(dims) - dim - 1))

    level = one(*cuts[0])
    for cut in cuts[1:]:
        level = level * one(*cut)
    return level


def bell_draw(rng, shape, scale, bound, shards=(), kind=jnp.bfloat16):
    drawn = jax.random.normal(rng, shape, jnp.float32) * scale
    if len(shards) > 0:
        drawn = shard_levels(rng, shape, shards, -0.22, 0.18) * drawn
    return jnp.clip(drawn, min=-bound, max=bound).astype(kind)


def setup_inputs(seed: int = 0, part: int = 0) -> dict:
    streams_of = jax.random.split(jax.random.key(seed), 9)
    own_keys = jax.random.split(jax.random.fold_in(streams_of[8], part), 9)
    image = bell_draw(own_keys[0], (ROWS, COLS, C), 1.0, 6.0, ((0, 16),))
    tissue = draw_tissue(jax.random.fold_in(jax.random.fold_in(streams_of[8], part), 71), part)
    kernel = bell_draw(streams_of[2], (KERNEL, KERNEL, C), (KERNEL * KERNEL) ** -0.5, 0.875, (), jnp.float32)
    ln_gain = jnp.clip(jax.random.uniform(streams_of[3], (C,), jnp.float32, 0.5, 1.5), 0.5, 1.5)
    w_in = bell_draw(streams_of[4], (C, FF), C ** -0.5, 0.375)
    w_out = bell_draw(streams_of[5], (FF, C), FF ** -0.5, 0.1875)
    layer_scale = jnp.clip(jax.random.uniform(streams_of[6], (C,), jnp.float32, 0.5, 1.5), 0.5, 1.5)
    cotangent = bell_draw(own_keys[7], (ROWS, COLS, C), 1.0, 6.0, ((0, 16),))
    return {"image": image, "tissue": tissue, "kernel": kernel, "ln_gain": ln_gain, "w_in": w_in, "w_out": w_out, "layer_scale": layer_scale, "cotangent": cotangent}


EPSILON = 1e-06
ROOT_TWO_PI = 0.7978845608028654
CUBIC_TERM = 0.044715

def gelu_value(inputs):
    tangent = jnp.tanh(ROOT_TWO_PI * (inputs + CUBIC_TERM * inputs * inputs * inputs))
    return 0.5 * inputs * (1.0 + tangent)

def gelu_slope(inputs):
    tangent = jnp.tanh(ROOT_TWO_PI * (inputs + CUBIC_TERM * inputs * inputs * inputs))
    return 0.5 * (1.0 + tangent) + 0.5 * inputs * (1.0 - tangent * tangent) * ROOT_TWO_PI * (1.0 + 3.0 * CUBIC_TERM * inputs * inputs)

def depthwise(padded, kernel, image_rows, image_cols):
    total = jnp.zeros((image_rows, image_cols, kernel.shape[-1]), jnp.float32)
    for row_tap in range(KERNEL):
        for col_tap in range(KERNEL):
            total = total + padded[row_tap:row_tap + image_rows, col_tap:col_tap + image_cols] * kernel[row_tap, col_tap]
    return total

def kernel_terms(padded, grads, image_rows, image_cols):
    collected = []
    for row_tap in range(KERNEL):
        for col_tap in range(KERNEL):
            collected.append(lax.optimization_barrier(jnp.sum(padded[row_tap:row_tap + image_rows, col_tap:col_tap + image_cols] * grads, axis=(0, 1))))
    return jnp.stack(collected)

def reference(image, tissue, kernel, ln_gain, w_in, w_out, layer_scale, cotangent):
    image_rows, image_cols, channels = image.shape
    hidden = w_in.shape[1]
    half_width = KERNEL // 2
    padded = jnp.pad(image.astype(jnp.float32), ((half_width, half_width), (half_width, half_width), (0, 0)))
    filtered = depthwise(padded, kernel, image_rows, image_cols)
    centre = lax.optimization_barrier(jnp.mean(filtered, axis=-1, keepdims=True))
    centered = filtered - centre
    inv_std = lax.rsqrt(lax.optimization_barrier(jnp.mean(centered * centered, axis=-1, keepdims=True)) + EPSILON)
    standard = centered * inv_std
    normed = (standard * ln_gain).astype(jnp.bfloat16)
    tissue_at = jnp.repeat(jnp.repeat(tissue, TILE_ROWS, axis=0), TILE_COLS, axis=1).astype(jnp.float32)[:, :, None]
    upstream = cotangent.astype(jnp.float32)
    grad_out = (tissue_at * layer_scale * upstream).astype(jnp.bfloat16)
    blocks = image_rows // TILE_ROWS
    normed_blocks = normed.reshape(blocks, TILE_ROWS * image_cols, channels)
    grad_blocks = grad_out.reshape(blocks, TILE_ROWS * image_cols, channels)

    def block_step(totals, record):
        grad_in_sum, grad_out_sum = totals
        normed_blk, grad_blk = record
        pre_act = jnp.dot(normed_blk, w_in, preferred_element_type=jnp.float32)
        activation = gelu_value(pre_act).astype(jnp.bfloat16)
        branch = jnp.dot(activation, w_out, preferred_element_type=jnp.float32)
        grad_act = jnp.dot(grad_blk, w_out.T, preferred_element_type=jnp.float32)
        grad_pre = (grad_act * gelu_slope(pre_act)).astype(jnp.bfloat16)
        grad_norm = jnp.dot(grad_pre, w_in.T, preferred_element_type=jnp.float32)
        grad_in_sum = grad_in_sum + jnp.dot(normed_blk.T, grad_pre, preferred_element_type=jnp.float32)
        grad_out_sum = grad_out_sum + jnp.dot(activation.T, grad_blk, preferred_element_type=jnp.float32)
        return ((grad_in_sum, grad_out_sum), (branch, grad_norm))
    start_totals = (jnp.zeros((channels, hidden), jnp.float32), jnp.zeros((hidden, channels), jnp.float32))
    (grad_w_in, grad_w_out), (branch_blocks, norm_blocks) = lax.scan(block_step, start_totals, (normed_blocks, grad_blocks))
    branch = branch_blocks.reshape(image_rows, image_cols, channels)
    grad_norm = norm_blocks.reshape(image_rows, image_cols, channels)
    block_out = (image.astype(jnp.float32) + tissue_at * layer_scale * branch).astype(jnp.bfloat16)
    scale_grad = lax.optimization_barrier(jnp.sum(tissue_at * branch * upstream, axis=(0, 1)))
    gain_grad = lax.optimization_barrier(jnp.sum(grad_norm * standard, axis=(0, 1)))
    grad_std = grad_norm * ln_gain
    grad_conv = (inv_std * (grad_std - lax.optimization_barrier(jnp.mean(grad_std, axis=-1, keepdims=True)) - standard * lax.optimization_barrier(jnp.mean(grad_std * standard, axis=-1, keepdims=True)))).astype(jnp.bfloat16)
    grad_float = grad_conv.astype(jnp.float32)
    kernel_grad = kernel_terms(padded, grad_float, image_rows, image_cols)
    small_grads = jnp.concatenate([kernel_grad, gain_grad[None], scale_grad[None]], axis=0)
    grad_padded = jnp.pad(grad_float, ((half_width, half_width), (half_width, half_width), (0, 0)))
    conv_back = depthwise(grad_padded, kernel[::-1, ::-1], image_rows, image_cols)
    grad_image = (upstream + conv_back).astype(jnp.bfloat16)
    return (block_out, grad_image, grad_w_in, grad_w_out, small_grads)
```

```python
import jax
import jax.numpy as jnp
from jax import lax
from jax.sharding import PartitionSpec as P

KERNEL = 7
TILE_ROWS = 4
TILE_COLS = 128


EPSILON = 1e-06
ROOT_TWO_PI = 0.7978845608028654
CUBIC_TERM = 0.044715


def padded_2(block, sides, width):
    for axis, dim in sides:
        count = lax.axis_size(axis)
        forward = [(i, i + 1) for i in range(count - 1)]
        backward = [(target, source) for source, target in forward]
        low = lax.ppermute(
            lax.slice_in_dim(block, block.shape[dim] - width, None, axis=dim), axis, forward
        )
        high = lax.ppermute(lax.slice_in_dim(block, 0, width, axis=dim), axis, backward)
        block = jnp.concatenate([low, block, high], axis=dim)
    return block


def halving_reduce(blocks, whole, axis):
    count = lax.axis_size(axis)
    steps = count.bit_length() - 1
    if (1 << steps) != count:
        return lax.psum_scatter(blocks, axis, scatter_dimension=0, tiled=True), lax.psum(whole, axis)
    me = lax.axis_index(axis)
    for step in range(steps):
        bit = (me >> step) & 1
        pairs = [(i, i ^ (1 << step)) for i in range(count)]
        halves = blocks.reshape(blocks.shape[0] // 2, 2, -1)
        keep = lax.dynamic_index_in_dim(halves, bit, axis=1, keepdims=False)
        give = lax.dynamic_index_in_dim(halves, 1 - bit, axis=1, keepdims=False)
        got, got_whole = lax.ppermute((give, whole), axis, pairs)
        blocks = keep + got
        whole = whole + got_whole
    return blocks, whole


def gelu_value(inputs):
    tangent = jnp.tanh(ROOT_TWO_PI * (inputs + CUBIC_TERM * inputs * inputs * inputs))
    return 0.5 * inputs * (1.0 + tangent)


def gelu_slope(inputs):
    tangent = jnp.tanh(ROOT_TWO_PI * (inputs + CUBIC_TERM * inputs * inputs * inputs))
    return 0.5 * (1.0 + tangent) + 0.5 * inputs * (1.0 - tangent * tangent) * ROOT_TWO_PI * (
        1.0 + 3.0 * CUBIC_TERM * inputs * inputs
    )


def depthwise(padded, kernel, image_rows, image_cols):
    total = jnp.zeros((image_rows, image_cols, kernel.shape[-1]), jnp.float32)
    for row_tap in range(KERNEL):
        for col_tap in range(KERNEL):
            total = (
                total
                + padded[row_tap : row_tap + image_rows, col_tap : col_tap + image_cols]
                * kernel[row_tap, col_tap]
            )
    return total


def kernel_terms(padded, grads, image_rows, image_cols):
    collected = []
    for row_tap in range(KERNEL):
        for col_tap in range(KERNEL):
            collected.append(
                jnp.sum(
                    padded[row_tap : row_tap + image_rows, col_tap : col_tap + image_cols] * grads,
                    axis=(0, 1),
                )
            )
    return jnp.stack(collected)


def shards(image, tissue, kernel, ln_gain, w_in, w_out, layer_scale, cotangent):
    half_width = KERNEL // 2
    image_rows, image_cols, channels = image.shape
    hidden = w_in.shape[1]
    tile_size = TILE_ROWS * TILE_COLS

    def to_tiles(values):
        depth_last = values.shape[-1]
        values = values.reshape(
            image_rows // TILE_ROWS, TILE_ROWS, image_cols // TILE_COLS, TILE_COLS, depth_last
        )
        return values.transpose(0, 2, 1, 3, 4).reshape(-1, tile_size, depth_last)

    def from_tiles(values):
        depth_last = values.shape[-1]
        values = values.reshape(
            image_rows // TILE_ROWS, image_cols // TILE_COLS, TILE_ROWS, TILE_COLS, depth_last
        )
        return values.transpose(0, 2, 1, 3, 4).reshape(image_rows, image_cols, depth_last)

    extended = padded_2(image, (("row", 0),), half_width)
    padded = jnp.pad(extended.astype(jnp.float32), ((0, 0), (half_width, half_width), (0, 0)))
    filtered = depthwise(padded, kernel, image_rows, image_cols)
    centre = jnp.mean(filtered, axis=-1, keepdims=True)
    centered = filtered - centre
    inv_std = lax.rsqrt(jnp.mean(centered * centered, axis=-1, keepdims=True) + EPSILON)
    standard = centered * inv_std
    normed = (standard * ln_gain).astype(jnp.bfloat16)
    tissue_at = jnp.repeat(jnp.repeat(tissue, TILE_ROWS, axis=0), TILE_COLS, axis=1).astype(
        jnp.float32
    )[:, :, None]
    upstream = cotangent.astype(jnp.float32)
    grad_out = (tissue_at * layer_scale * upstream).astype(jnp.bfloat16)
    normed_tiles = to_tiles(normed)
    grad_tiles = to_tiles(grad_out)
    has_tissue = tissue.reshape(-1)

    def tile_work(normed_blk, grad_blk):
        pre_act = jnp.dot(normed_blk, w_in, preferred_element_type=jnp.float32)
        activation = gelu_value(pre_act).astype(jnp.bfloat16)
        branch = jnp.dot(activation, w_out, preferred_element_type=jnp.float32)
        grad_act = jnp.dot(grad_blk, w_out.T, preferred_element_type=jnp.float32)
        grad_pre = (grad_act * gelu_slope(pre_act)).astype(jnp.bfloat16)
        grad_norm = jnp.dot(grad_pre, w_in.T, preferred_element_type=jnp.float32)
        return (activation, branch, grad_pre, grad_norm)

    def per_tile(record):
        return tile_work(record[0], record[1])

    act_tiles, branch_tiles, pre_tiles, norm_tiles = lax.map(
        per_tile, (normed_tiles, grad_tiles, has_tissue)
    )
    normed_flat = normed_tiles.reshape(-1, channels)
    grad_flat = grad_tiles.reshape(-1, channels)
    act_flat = act_tiles.reshape(-1, hidden)
    pre_flat = pre_tiles.reshape(-1, hidden)
    partial_in = lax.dot_general(
        normed_flat, pre_flat, (((0,), (0,)), ((), ())), preferred_element_type=jnp.float32
    )
    partial_out = lax.dot_general(
        act_flat, grad_flat, (((0,), (0,)), ((), ())), preferred_element_type=jnp.float32
    )
    branch = from_tiles(branch_tiles)
    grad_norm = from_tiles(norm_tiles)
    block_out = (image.astype(jnp.float32) + tissue_at * layer_scale * branch).astype(jnp.bfloat16)
    scale_grad = jnp.sum(tissue_at * branch * upstream, axis=(0, 1))
    gain_grad = jnp.sum(grad_norm * standard, axis=(0, 1))
    grad_std = grad_norm * ln_gain
    grad_conv = (
        inv_std
        * (
            grad_std
            - jnp.mean(grad_std, axis=-1, keepdims=True)
            - standard * jnp.mean(grad_std * standard, axis=-1, keepdims=True)
        )
    ).astype(jnp.bfloat16)
    grad_float = grad_conv.astype(jnp.float32)
    kernel_grad = kernel_terms(padded, grad_float, image_rows, image_cols)
    packed = jnp.concatenate([kernel_grad, gain_grad[None], scale_grad[None]], axis=0)
    count = lax.axis_size("row")
    merged = jnp.concatenate(
        [partial_in.reshape(count, -1), partial_out.reshape(count, -1)], axis=1
    )
    owned, small_grads = halving_reduce(merged, packed, "row")
    split_at = partial_in.size // count
    grad_w_in = owned[0, :split_at].reshape(-1, hidden)
    grad_w_out = owned[0, split_at:].reshape(-1, channels)
    grad_ext = padded_2(grad_conv, (("row", 0),), half_width)
    grad_padded = jnp.pad(grad_ext.astype(jnp.float32), ((0, 0), (half_width, half_width), (0, 0)))
    conv_back = depthwise(grad_padded, kernel[::-1, ::-1], image_rows, image_cols)
    grad_image = (upstream + conv_back).astype(jnp.bfloat16)
    return (block_out, grad_image, grad_w_in, grad_w_out, small_grads)


def solution(mesh):
    placed = (
        P(("group", "row"), None, None),
        P(("group", "row"), None),
        P(),
        P(),
        P(),
        P(),
        P(),
        P(("group", "row"), None, None),
    )
    return jax.shard_map(
        shards,
        mesh=mesh,
        in_specs=placed,
        out_specs=(
            P(("group", "row"), None, None),
            P(("group", "row"), None, None),
            P(("group", "row"), None),
            P(("group", "row"), None),
            P("group", None),
        ),
        check_vma=False,
    )
```

```python
import jax
import jax.numpy as jnp
from jax import lax
from jax.sharding import PartitionSpec as P

KERNEL = 7
TILE_ROWS = 4
TILE_COLS = 128


EPSILON = 1e-06
ROOT_TWO_PI = 0.7978845608028654
CUBIC_TERM = 0.044715


def padded_2(block, sides, width):
    for axis, dim in sides:
        count = lax.axis_size(axis)
        forward = [(i, i + 1) for i in range(count - 1)]
        backward = [(target, source) for source, target in forward]
        low = lax.ppermute(
            lax.slice_in_dim(block, block.shape[dim] - width, None, axis=dim), axis, forward
        )
        high = lax.ppermute(lax.slice_in_dim(block, 0, width, axis=dim), axis, backward)
        block = jnp.concatenate([low, block, high], axis=dim)
    return block


def bit_reversed(values, count, steps):
    rest = values.shape[1:]
    values = values.reshape((2,) * steps + (values.shape[0] // count,) + rest)
    order = tuple(reversed(range(steps))) + tuple(range(steps, values.ndim))
    return values.transpose(order).reshape((-1,) + rest)


def halving_reduce(parts, whole, axis):
    count = lax.axis_size(axis)
    steps = count.bit_length() - 1
    if (1 << steps) != count:
        owned = [lax.psum_scatter(p, axis, scatter_dimension=0, tiled=True) for p in parts]
        return owned, lax.psum(whole, axis)
    me = lax.axis_index(axis)
    parts = [bit_reversed(p, count, steps) for p in parts]
    for step in range(steps):
        bit = (me >> step) & 1
        pairs = [(i, i ^ (1 << step)) for i in range(count)]
        keeps, gives = [], []
        for p in parts:
            half = p.shape[0] // 2
            keeps.append(lax.dynamic_slice_in_dim(p, bit * half, half, axis=0))
            gives.append(lax.dynamic_slice_in_dim(p, (1 - bit) * half, half, axis=0))
        got, got_whole = lax.ppermute((gives, whole), axis, pairs)
        parts = [k + g for k, g in zip(keeps, got)]
        whole = whole + got_whole
    return parts, whole


def gelu_value(inputs):
    tangent = jnp.tanh(ROOT_TWO_PI * (inputs + CUBIC_TERM * inputs * inputs * inputs))
    return 0.5 * inputs * (1.0 + tangent)


def gelu_slope(inputs):
    tangent = jnp.tanh(ROOT_TWO_PI * (inputs + CUBIC_TERM * inputs * inputs * inputs))
    return 0.5 * (1.0 + tangent) + 0.5 * inputs * (1.0 - tangent * tangent) * ROOT_TWO_PI * (
        1.0 + 3.0 * CUBIC_TERM * inputs * inputs
    )


def depthwise(padded, kernel, image_rows, image_cols):
    total = jnp.zeros((image_rows, image_cols, kernel.shape[-1]), jnp.float32)
    for row_tap in range(KERNEL):
        for col_tap in range(KERNEL):
            total = (
                total
                + padded[row_tap : row_tap + image_rows, col_tap : col_tap + image_cols]
                * kernel[row_tap, col_tap]
            )
    return total


def kernel_terms(padded, grads, image_rows, image_cols):
    collected = []
    for row_tap in range(KERNEL):
        for col_tap in range(KERNEL):
            collected.append(
                jnp.sum(
                    padded[row_tap : row_tap + image_rows, col_tap : col_tap + image_cols] * grads,
                    axis=(0, 1),
                )
            )
    return jnp.stack(collected)


def shards(image, tissue, kernel, ln_gain, w_in, w_out, layer_scale, cotangent):
    half_width = KERNEL // 2
    image_rows, image_cols, channels = image.shape
    hidden = w_in.shape[1]
    tile_size = TILE_ROWS * TILE_COLS

    def to_tiles(values):
        depth_last = values.shape[-1]
        values = values.reshape(
            image_rows // TILE_ROWS, TILE_ROWS, image_cols // TILE_COLS, TILE_COLS, depth_last
        )
        return values.transpose(0, 2, 1, 3, 4).reshape(-1, tile_size, depth_last)

    def from_tiles(values):
        depth_last = values.shape[-1]
        values = values.reshape(
            image_rows // TILE_ROWS, image_cols // TILE_COLS, TILE_ROWS, TILE_COLS, depth_last
        )
        return values.transpose(0, 2, 1, 3, 4).reshape(image_rows, image_cols, depth_last)

    extended = padded_2(image, (("row", 0),), half_width)
    padded = jnp.pad(extended.astype(jnp.float32), ((0, 0), (half_width, half_width), (0, 0)))
    filtered = depthwise(padded, kernel, image_rows, image_cols)
    centre = jnp.mean(filtered, axis=-1, keepdims=True)
    centered = filtered - centre
    inv_std = lax.rsqrt(jnp.mean(centered * centered, axis=-1, keepdims=True) + EPSILON)
    standard = centered * inv_std
    normed = (standard * ln_gain).astype(jnp.bfloat16)
    tissue_at = jnp.repeat(jnp.repeat(tissue, TILE_ROWS, axis=0), TILE_COLS, axis=1).astype(
        jnp.float32
    )[:, :, None]
    upstream = cotangent.astype(jnp.float32)
    grad_out = (tissue_at * layer_scale * upstream).astype(jnp.bfloat16)
    normed_tiles = to_tiles(normed)
    grad_tiles = to_tiles(grad_out)
    has_tissue = tissue.reshape(-1)

    def tile_work(normed_blk, grad_blk):
        pre_act = jnp.dot(normed_blk, w_in, preferred_element_type=jnp.float32)
        activation = gelu_value(pre_act).astype(jnp.bfloat16)
        branch = jnp.dot(activation, w_out, preferred_element_type=jnp.float32)
        grad_act = jnp.dot(grad_blk, w_out.T, preferred_element_type=jnp.float32)
        grad_pre = (grad_act * gelu_slope(pre_act)).astype(jnp.bfloat16)
        grad_norm = jnp.dot(grad_pre, w_in.T, preferred_element_type=jnp.float32)
        return (activation, branch, grad_pre, grad_norm)

    def per_tile(record):
        return tile_work(record[0], record[1])

    act_tiles, branch_tiles, pre_tiles, norm_tiles = lax.map(
        per_tile, (normed_tiles, grad_tiles, has_tissue)
    )
    normed_flat = normed_tiles.reshape(-1, channels)
    grad_flat = grad_tiles.reshape(-1, channels)
    act_flat = act_tiles.reshape(-1, hidden)
    pre_flat = pre_tiles.reshape(-1, hidden)
    partial_in = lax.dot_general(
        normed_flat, pre_flat, (((0,), (0,)), ((), ())), preferred_element_type=jnp.float32
    )
    partial_out = lax.dot_general(
        act_flat, grad_flat, (((0,), (0,)), ((), ())), preferred_element_type=jnp.float32
    )
    branch = from_tiles(branch_tiles)
    grad_norm = from_tiles(norm_tiles)
    block_out = (image.astype(jnp.float32) + tissue_at * layer_scale * branch).astype(jnp.bfloat16)
    scale_grad = jnp.sum(tissue_at * branch * upstream, axis=(0, 1))
    gain_grad = jnp.sum(grad_norm * standard, axis=(0, 1))
    grad_std = grad_norm * ln_gain
    grad_conv = (
        inv_std
        * (
            grad_std
            - jnp.mean(grad_std, axis=-1, keepdims=True)
            - standard * jnp.mean(grad_std * standard, axis=-1, keepdims=True)
        )
    ).astype(jnp.bfloat16)
    grad_float = grad_conv.astype(jnp.float32)
    kernel_grad = kernel_terms(padded, grad_float, image_rows, image_cols)
    packed = jnp.concatenate([kernel_grad, gain_grad[None], scale_grad[None]], axis=0)
    (grad_w_in, grad_w_out), small_grads = halving_reduce([partial_in, partial_out], packed, "row")
    grad_ext = padded_2(grad_conv, (("row", 0),), half_width)
    grad_padded = jnp.pad(grad_ext.astype(jnp.float32), ((0, 0), (half_width, half_width), (0, 0)))
    conv_back = depthwise(grad_padded, kernel[::-1, ::-1], image_rows, image_cols)
    grad_image = (upstream + conv_back).astype(jnp.bfloat16)
    return (block_out, grad_image, grad_w_in, grad_w_out, small_grads)


def solution(mesh):
    placed = (
        P(("group", "row"), None, None),
        P(("group", "row"), None),
        P(),
        P(),
        P(),
        P(),
        P(),
        P(("group", "row"), None, None),
    )
    return jax.shard_map(
        shards,
        mesh=mesh,
        in_specs=placed,
        out_specs=(
            P(("group", "row"), None, None),
            P(("group", "row"), None, None),
            P(("group", "row"), None),
            P(("group", "row"), None),
            P("group", None),
        ),
        check_vma=False,
    )
```

```python
import jax
import jax.numpy as jnp
from jax import lax
from jax.sharding import PartitionSpec as P

KERNEL = 7
TILE_ROWS = 4
TILE_COLS = 128


EPSILON = 1e-06
ROOT_TWO_PI = 0.7978845608028654
CUBIC_TERM = 0.044715


def padded_2(block, sides, width):
    for axis, dim in sides:
        count = lax.axis_size(axis)
        forward = [(i, i + 1) for i in range(count - 1)]
        backward = [(target, source) for source, target in forward]
        low = lax.ppermute(
            lax.slice_in_dim(block, block.shape[dim] - width, None, axis=dim), axis, forward
        )
        high = lax.ppermute(lax.slice_in_dim(block, 0, width, axis=dim), axis, backward)
        block = jnp.concatenate([low, block, high], axis=dim)
    return block


def bit_reversed(values, count, steps):
    rest = values.shape[1:]
    values = values.reshape((2,) * steps + (values.shape[0] // count,) + rest)
    order = tuple(reversed(range(steps))) + tuple(range(steps, values.ndim))
    return values.transpose(order).reshape((-1,) + rest)


def halving_reduce(parts, whole, axis):
    count = lax.axis_size(axis)
    steps = count.bit_length() - 1
    if (1 << steps) != count:
        owned = [lax.psum_scatter(p, axis, scatter_dimension=0, tiled=True) for p in parts]
        return owned, lax.psum(whole, axis)
    me = lax.axis_index(axis)
    parts = [bit_reversed(p, count, steps) for p in parts]
    for step in range(steps):
        bit = (me >> step) & 1
        pairs = [(i, i ^ (1 << step)) for i in range(count)]
        keeps, gives = [], []
        for p in parts:
            half = p.shape[0] // 2
            keeps.append(lax.dynamic_slice_in_dim(p, bit * half, half, axis=0))
            gives.append(lax.dynamic_slice_in_dim(p, (1 - bit) * half, half, axis=0))
        got, got_whole = lax.ppermute((gives, whole), axis, pairs)
        parts = [k + g for k, g in zip(keeps, got)]
        whole = whole + got_whole
    return parts, whole


def gelu_value(inputs):
    tangent = jnp.tanh(ROOT_TWO_PI * (inputs + CUBIC_TERM * inputs * inputs * inputs))
    return 0.5 * inputs * (1.0 + tangent)


def gelu_slope(inputs):
    tangent = jnp.tanh(ROOT_TWO_PI * (inputs + CUBIC_TERM * inputs * inputs * inputs))
    return 0.5 * (1.0 + tangent) + 0.5 * inputs * (1.0 - tangent * tangent) * ROOT_TWO_PI * (
        1.0 + 3.0 * CUBIC_TERM * inputs * inputs
    )


def depthwise(padded, kernel, image_rows, image_cols):
    total = jnp.zeros((image_rows, image_cols, kernel.shape[-1]), jnp.float32)
    for row_tap in range(KERNEL):
        for col_tap in range(KERNEL):
            total = (
                total
                + padded[row_tap : row_tap + image_rows, col_tap : col_tap + image_cols]
                * kernel[row_tap, col_tap]
            )
    return total


def kernel_terms(padded, grads, image_rows, image_cols):
    collected = []
    for row_tap in range(KERNEL):
        for col_tap in range(KERNEL):
            collected.append(
                jnp.sum(
                    padded[row_tap : row_tap + image_rows, col_tap : col_tap + image_cols] * grads,
                    axis=(0, 1),
                )
            )
    return jnp.stack(collected)


def shards(image, tissue, kernel, ln_gain, w_in, w_out, layer_scale, cotangent):
    half_width = KERNEL // 2
    image_rows, image_cols, channels = image.shape
    hidden = w_in.shape[1]
    span = TILE_COLS + 2 * half_width

    first_col = jnp.argmax(tissue.reshape(-1)).astype(jnp.int32) * TILE_COLS
    extended = padded_2(image, (("row", 0),), half_width)
    padded = jnp.pad(extended, ((0, 0), (half_width, half_width), (0, 0)))
    window = lax.dynamic_slice_in_dim(padded, first_col, span, axis=1).astype(jnp.float32)
    filtered = depthwise(window, kernel, image_rows, TILE_COLS)
    centre = jnp.mean(filtered, axis=-1, keepdims=True)
    centered = filtered - centre
    inv_std = lax.rsqrt(jnp.mean(centered * centered, axis=-1, keepdims=True) + EPSILON)
    standard = centered * inv_std
    normed = (standard * ln_gain).astype(jnp.bfloat16)
    upstream = lax.dynamic_slice_in_dim(cotangent, first_col, TILE_COLS, axis=1).astype(jnp.float32)
    grad_out = (1.0 * layer_scale * upstream).astype(jnp.bfloat16)

    normed_flat = normed.reshape(-1, channels)
    grad_flat = grad_out.reshape(-1, channels)
    pre_act = jnp.dot(normed_flat, w_in, preferred_element_type=jnp.float32)
    act_flat = gelu_value(pre_act).astype(jnp.bfloat16)
    branch = jnp.dot(act_flat, w_out, preferred_element_type=jnp.float32)
    grad_act = jnp.dot(grad_flat, w_out.T, preferred_element_type=jnp.float32)
    pre_flat = (grad_act * gelu_slope(pre_act)).astype(jnp.bfloat16)
    grad_norm = jnp.dot(pre_flat, w_in.T, preferred_element_type=jnp.float32)
    partial_in = lax.dot_general(
        normed_flat, pre_flat, (((0,), (0,)), ((), ())), preferred_element_type=jnp.float32
    )
    partial_out = lax.dot_general(
        act_flat, grad_flat, (((0,), (0,)), ((), ())), preferred_element_type=jnp.float32
    )
    branch = branch.reshape(image_rows, TILE_COLS, channels)
    grad_norm = grad_norm.reshape(image_rows, TILE_COLS, channels)
    image_tile = lax.dynamic_slice_in_dim(image, first_col, TILE_COLS, axis=1)
    out_tile = (image_tile.astype(jnp.float32) + 1.0 * layer_scale * branch).astype(jnp.bfloat16)
    block_out = lax.dynamic_update_slice_in_dim(image, out_tile, first_col, axis=1)
    scale_grad = jnp.sum(1.0 * branch * upstream, axis=(0, 1))
    gain_grad = jnp.sum(grad_norm * standard, axis=(0, 1))
    grad_std = grad_norm * ln_gain
    grad_tile = (
        inv_std
        * (
            grad_std
            - jnp.mean(grad_std, axis=-1, keepdims=True)
            - standard * jnp.mean(grad_std * standard, axis=-1, keepdims=True)
        )
    ).astype(jnp.bfloat16)
    kernel_grad = kernel_terms(window, grad_tile.astype(jnp.float32), image_rows, TILE_COLS)
    packed = jnp.concatenate([kernel_grad, gain_grad[None], scale_grad[None]], axis=0)
    (grad_w_in, grad_w_out), small_grads = halving_reduce([partial_in, partial_out], packed, "row")
    grad_conv = lax.dynamic_update_slice_in_dim(
        jnp.zeros_like(image), grad_tile, first_col, axis=1
    )
    grad_ext = padded_2(grad_conv, (("row", 0),), half_width)
    grad_padded = jnp.pad(grad_ext.astype(jnp.float32), ((0, 0), (half_width, half_width), (0, 0)))
    conv_back = depthwise(grad_padded, kernel[::-1, ::-1], image_rows, image_cols)
    grad_image = (cotangent.astype(jnp.float32) + conv_back).astype(jnp.bfloat16)
    return (block_out, grad_image, grad_w_in, grad_w_out, small_grads)


def solution(mesh):
    placed = (
        P(("group", "row"), None, None),
        P(("group", "row"), None),
        P(),
        P(),
        P(),
        P(),
        P(),
        P(("group", "row"), None, None),
    )
    return jax.shard_map(
        shards,
        mesh=mesh,
        in_specs=placed,
        out_specs=(
            P(("group", "row"), None, None),
            P(("group", "row"), None, None),
            P(("group", "row"), None),
            P(("group", "row"), None),
            P("group", None),
        ),
        check_vma=False,
    )
```

```python
import jax
import jax.numpy as jnp
from jax import lax
from jax.sharding import PartitionSpec as P

KERNEL = 7
TILE_ROWS = 4
TILE_COLS = 128


EPSILON = 1e-06
ROOT_TWO_PI = 0.7978845608028654
CUBIC_TERM = 0.044715


def padded_2(block, sides, width):
    for axis, dim in sides:
        count = lax.axis_size(axis)
        forward = [(i, i + 1) for i in range(count - 1)]
        backward = [(target, source) for source, target in forward]
        low = lax.ppermute(
            lax.slice_in_dim(block, block.shape[dim] - width, None, axis=dim), axis, forward
        )
        high = lax.ppermute(lax.slice_in_dim(block, 0, width, axis=dim), axis, backward)
        block = jnp.concatenate([low, block, high], axis=dim)
    return block


def bit_reversed(values, count, steps):
    rest = values.shape[1:]
    values = values.reshape((2,) * steps + (values.shape[0] // count,) + rest)
    order = tuple(reversed(range(steps))) + tuple(range(steps, values.ndim))
    return values.transpose(order).reshape((-1,) + rest)


def halving_reduce(parts, whole, axis):
    count = lax.axis_size(axis)
    steps = count.bit_length() - 1
    if (1 << steps) != count:
        owned = [lax.psum_scatter(p, axis, scatter_dimension=0, tiled=True) for p in parts]
        return owned, lax.psum(whole, axis)
    me = lax.axis_index(axis)
    parts = [bit_reversed(p, count, steps) for p in parts]
    for step in range(steps):
        bit = (me >> step) & 1
        pairs = [(i, i ^ (1 << step)) for i in range(count)]
        keeps, gives = [], []
        for p in parts:
            half = p.shape[0] // 2
            keeps.append(lax.dynamic_slice_in_dim(p, bit * half, half, axis=0))
            gives.append(lax.dynamic_slice_in_dim(p, (1 - bit) * half, half, axis=0))
        got = lax.ppermute(jnp.concatenate(gives + [whole], axis=0), axis, pairs)
        parts, offset = [], 0
        for k in keeps:
            parts.append(k + got[offset : offset + k.shape[0]])
            offset += k.shape[0]
        whole = whole + got[offset:]
    return parts, whole


def gelu_value(inputs):
    tangent = jnp.tanh(ROOT_TWO_PI * (inputs + CUBIC_TERM * inputs * inputs * inputs))
    return 0.5 * inputs * (1.0 + tangent)


def gelu_slope(inputs):
    tangent = jnp.tanh(ROOT_TWO_PI * (inputs + CUBIC_TERM * inputs * inputs * inputs))
    return 0.5 * (1.0 + tangent) + 0.5 * inputs * (1.0 - tangent * tangent) * ROOT_TWO_PI * (
        1.0 + 3.0 * CUBIC_TERM * inputs * inputs
    )


def depthwise(padded, kernel, image_rows, image_cols):
    total = jnp.zeros((image_rows, image_cols, kernel.shape[-1]), jnp.float32)
    for row_tap in range(KERNEL):
        for col_tap in range(KERNEL):
            total = (
                total
                + padded[row_tap : row_tap + image_rows, col_tap : col_tap + image_cols]
                * kernel[row_tap, col_tap]
            )
    return total


def kernel_terms(padded, grads, image_rows, image_cols):
    collected = []
    for row_tap in range(KERNEL):
        for col_tap in range(KERNEL):
            collected.append(
                jnp.sum(
                    padded[row_tap : row_tap + image_rows, col_tap : col_tap + image_cols] * grads,
                    axis=(0, 1),
                )
            )
    return jnp.stack(collected)


def shards(image, tissue, kernel, ln_gain, w_in, w_out, layer_scale, cotangent):
    half_width = KERNEL // 2
    image_rows, image_cols, channels = image.shape
    hidden = w_in.shape[1]
    span = TILE_COLS + 2 * half_width

    first_col = jnp.argmax(tissue.reshape(-1)).astype(jnp.int32) * TILE_COLS
    extended = padded_2(image, (("row", 0),), half_width)
    padded = jnp.pad(extended, ((0, 0), (half_width, half_width), (0, 0)))
    window = lax.dynamic_slice_in_dim(padded, first_col, span, axis=1).astype(jnp.float32)
    filtered = depthwise(window, kernel, image_rows, TILE_COLS)
    centre = jnp.mean(filtered, axis=-1, keepdims=True)
    centered = filtered - centre
    inv_std = lax.rsqrt(jnp.mean(centered * centered, axis=-1, keepdims=True) + EPSILON)
    standard = centered * inv_std
    normed = (standard * ln_gain).astype(jnp.bfloat16)
    upstream = lax.dynamic_slice_in_dim(cotangent, first_col, TILE_COLS, axis=1).astype(jnp.float32)
    grad_out = (1.0 * layer_scale * upstream).astype(jnp.bfloat16)

    normed_flat = normed.reshape(-1, channels)
    grad_flat = grad_out.reshape(-1, channels)
    pre_act = jnp.dot(normed_flat, w_in, preferred_element_type=jnp.float32)
    act_flat = gelu_value(pre_act).astype(jnp.bfloat16)
    branch = jnp.dot(act_flat, w_out, preferred_element_type=jnp.float32)
    grad_act = jnp.dot(grad_flat, w_out.T, preferred_element_type=jnp.float32)
    pre_flat = (grad_act * gelu_slope(pre_act)).astype(jnp.bfloat16)
    grad_norm = jnp.dot(pre_flat, w_in.T, preferred_element_type=jnp.float32)
    partial_in = lax.dot_general(
        normed_flat, pre_flat, (((0,), (0,)), ((), ())), preferred_element_type=jnp.float32
    )
    partial_out = lax.dot_general(
        act_flat, grad_flat, (((0,), (0,)), ((), ())), preferred_element_type=jnp.float32
    )
    branch = branch.reshape(image_rows, TILE_COLS, channels)
    grad_norm = grad_norm.reshape(image_rows, TILE_COLS, channels)
    image_tile = lax.dynamic_slice_in_dim(image, first_col, TILE_COLS, axis=1)
    out_tile = (image_tile.astype(jnp.float32) + 1.0 * layer_scale * branch).astype(jnp.bfloat16)
    block_out = lax.dynamic_update_slice_in_dim(image, out_tile, first_col, axis=1)
    scale_grad = jnp.sum(1.0 * branch * upstream, axis=(0, 1))
    gain_grad = jnp.sum(grad_norm * standard, axis=(0, 1))
    grad_std = grad_norm * ln_gain
    grad_tile = (
        inv_std
        * (
            grad_std
            - jnp.mean(grad_std, axis=-1, keepdims=True)
            - standard * jnp.mean(grad_std * standard, axis=-1, keepdims=True)
        )
    ).astype(jnp.bfloat16)
    kernel_grad = kernel_terms(window, grad_tile.astype(jnp.float32), image_rows, TILE_COLS)
    packed = jnp.concatenate([kernel_grad, gain_grad[None], scale_grad[None]], axis=0)
    (owned_in, grad_w_out), small_grads = halving_reduce(
        [partial_in.reshape(-1, channels), partial_out], packed, "row"
    )
    grad_w_in = owned_in.reshape(-1, hidden)
    grad_conv = lax.dynamic_update_slice_in_dim(
        jnp.zeros_like(image), grad_tile, first_col, axis=1
    )
    grad_ext = padded_2(grad_conv, (("row", 0),), half_width)
    grad_padded = jnp.pad(grad_ext.astype(jnp.float32), ((0, 0), (half_width, half_width), (0, 0)))
    conv_back = depthwise(grad_padded, kernel[::-1, ::-1], image_rows, image_cols)
    grad_image = (cotangent.astype(jnp.float32) + conv_back).astype(jnp.bfloat16)
    return (block_out, grad_image, grad_w_in, grad_w_out, small_grads)


def solution(mesh):
    placed = (
        P(("group", "row"), None, None),
        P(("group", "row"), None),
        P(),
        P(),
        P(),
        P(),
        P(),
        P(("group", "row"), None, None),
    )
    return jax.shard_map(
        shards,
        mesh=mesh,
        in_specs=placed,
        out_specs=(
            P(("group", "row"), None, None),
            P(("group", "row"), None, None),
            P(("group", "row"), None),
            P(("group", "row"), None),
            P("group", None),
        ),
        check_vma=False,
    )
```

```python
import jax
import jax.numpy as jnp
from jax import lax
from jax.sharding import PartitionSpec as P

KERNEL = 7
TILE_ROWS = 4
TILE_COLS = 128


EPSILON = 1e-06
ROOT_TWO_PI = 0.7978845608028654
CUBIC_TERM = 0.044715


def padded_2(block, sides, width):
    for axis, dim in sides:
        count = lax.axis_size(axis)
        forward = [(i, i + 1) for i in range(count - 1)]
        backward = [(target, source) for source, target in forward]
        low = lax.ppermute(
            lax.slice_in_dim(block, block.shape[dim] - width, None, axis=dim), axis, forward
        )
        high = lax.ppermute(lax.slice_in_dim(block, 0, width, axis=dim), axis, backward)
        block = jnp.concatenate([low, block, high], axis=dim)
    return block


def bit_reversed(values, count, steps):
    rest = values.shape[1:]
    values = values.reshape((2,) * steps + (values.shape[0] // count,) + rest)
    order = tuple(reversed(range(steps))) + tuple(range(steps, values.ndim))
    return values.transpose(order).reshape((-1,) + rest)


def halving_reduce(parts, whole, axis):
    count = lax.axis_size(axis)
    steps = count.bit_length() - 1
    if (1 << steps) != count:
        owned = [lax.psum_scatter(p, axis, scatter_dimension=0, tiled=True) for p in parts]
        return owned, lax.psum(whole, axis)
    me = lax.axis_index(axis)
    parts = [bit_reversed(p, count, steps) for p in parts]
    for step in range(steps):
        bit = (me >> step) & 1
        pairs = [(i, i ^ (1 << step)) for i in range(count)]
        keeps, gives = [], []
        for p in parts:
            half = p.shape[0] // 2
            keeps.append(lax.dynamic_slice_in_dim(p, bit * half, half, axis=0))
            gives.append(lax.dynamic_slice_in_dim(p, (1 - bit) * half, half, axis=0))
        got, got_whole = lax.ppermute((gives, whole), axis, pairs)
        parts = [k + g for k, g in zip(keeps, got)]
        whole = whole + got_whole
    return parts, whole


def exchange_reduce(parts, whole, axis):
    count = lax.axis_size(axis)
    blocks = [p.reshape((count, p.shape[0] // count) + p.shape[1:]) for p in parts]
    copies = jnp.broadcast_to(whole[None], (count,) + whole.shape)
    arrived = [
        lax.all_to_all(b, axis, split_axis=0, concat_axis=0, tiled=False)
        for b in blocks + [copies]
    ]
    summed = [jnp.sum(a, axis=0) for a in arrived]
    return summed[:-1], summed[-1]


def gelu_value(inputs):
    tangent = jnp.tanh(ROOT_TWO_PI * (inputs + CUBIC_TERM * inputs * inputs * inputs))
    return 0.5 * inputs * (1.0 + tangent)


def gelu_slope(inputs):
    tangent = jnp.tanh(ROOT_TWO_PI * (inputs + CUBIC_TERM * inputs * inputs * inputs))
    return 0.5 * (1.0 + tangent) + 0.5 * inputs * (1.0 - tangent * tangent) * ROOT_TWO_PI * (
        1.0 + 3.0 * CUBIC_TERM * inputs * inputs
    )


def depthwise(padded, kernel, image_rows, image_cols):
    total = jnp.zeros((image_rows, image_cols, kernel.shape[-1]), jnp.float32)
    for row_tap in range(KERNEL):
        for col_tap in range(KERNEL):
            total = (
                total
                + padded[row_tap : row_tap + image_rows, col_tap : col_tap + image_cols]
                * kernel[row_tap, col_tap]
            )
    return total


def kernel_terms(padded, grads, image_rows, image_cols):
    collected = []
    for row_tap in range(KERNEL):
        for col_tap in range(KERNEL):
            collected.append(
                jnp.sum(
                    padded[row_tap : row_tap + image_rows, col_tap : col_tap + image_cols] * grads,
                    axis=(0, 1),
                )
            )
    return jnp.stack(collected)


def shards(image, tissue, kernel, ln_gain, w_in, w_out, layer_scale, cotangent):
    half_width = KERNEL // 2
    image_rows, image_cols, channels = image.shape
    hidden = w_in.shape[1]
    span = TILE_COLS + 2 * half_width

    first_col = jnp.argmax(tissue.reshape(-1)).astype(jnp.int32) * TILE_COLS
    extended = padded_2(image, (("row", 0),), half_width)
    padded = jnp.pad(extended, ((0, 0), (half_width, half_width), (0, 0)))
    window = lax.dynamic_slice_in_dim(padded, first_col, span, axis=1).astype(jnp.float32)
    filtered = depthwise(window, kernel, image_rows, TILE_COLS)
    centre = jnp.mean(filtered, axis=-1, keepdims=True)
    centered = filtered - centre
    inv_std = lax.rsqrt(jnp.mean(centered * centered, axis=-1, keepdims=True) + EPSILON)
    standard = centered * inv_std
    normed = (standard * ln_gain).astype(jnp.bfloat16)
    upstream = lax.dynamic_slice_in_dim(cotangent, first_col, TILE_COLS, axis=1).astype(jnp.float32)
    grad_out = (1.0 * layer_scale * upstream).astype(jnp.bfloat16)

    normed_flat = normed.reshape(-1, channels)
    grad_flat = grad_out.reshape(-1, channels)
    pre_act = jnp.dot(normed_flat, w_in, preferred_element_type=jnp.float32)
    act_flat = gelu_value(pre_act).astype(jnp.bfloat16)
    branch = jnp.dot(act_flat, w_out, preferred_element_type=jnp.float32)
    grad_act = jnp.dot(grad_flat, w_out.T, preferred_element_type=jnp.float32)
    pre_flat = (grad_act * gelu_slope(pre_act)).astype(jnp.bfloat16)
    grad_norm = jnp.dot(pre_flat, w_in.T, preferred_element_type=jnp.float32)
    partial_in = lax.dot_general(
        normed_flat, pre_flat, (((0,), (0,)), ((), ())), preferred_element_type=jnp.float32
    )
    partial_out = lax.dot_general(
        act_flat, grad_flat, (((0,), (0,)), ((), ())), preferred_element_type=jnp.float32
    )
    branch = branch.reshape(image_rows, TILE_COLS, channels)
    grad_norm = grad_norm.reshape(image_rows, TILE_COLS, channels)
    image_tile = lax.dynamic_slice_in_dim(image, first_col, TILE_COLS, axis=1)
    out_tile = (image_tile.astype(jnp.float32) + 1.0 * layer_scale * branch).astype(jnp.bfloat16)
    block_out = lax.dynamic_update_slice_in_dim(image, out_tile, first_col, axis=1)
    scale_grad = jnp.sum(1.0 * branch * upstream, axis=(0, 1))
    gain_grad = jnp.sum(grad_norm * standard, axis=(0, 1))
    grad_std = grad_norm * ln_gain
    grad_tile = (
        inv_std
        * (
            grad_std
            - jnp.mean(grad_std, axis=-1, keepdims=True)
            - standard * jnp.mean(grad_std * standard, axis=-1, keepdims=True)
        )
    ).astype(jnp.bfloat16)
    kernel_grad = kernel_terms(window, grad_tile.astype(jnp.float32), image_rows, TILE_COLS)
    packed = jnp.concatenate([kernel_grad, gain_grad[None], scale_grad[None]], axis=0)
    (grad_w_in, grad_w_out), small_grads = exchange_reduce([partial_in, partial_out], packed, "row")
    grad_conv = lax.dynamic_update_slice_in_dim(
        jnp.zeros_like(image), grad_tile, first_col, axis=1
    )
    grad_ext = padded_2(grad_conv, (("row", 0),), half_width)
    grad_padded = jnp.pad(grad_ext.astype(jnp.float32), ((0, 0), (half_width, half_width), (0, 0)))
    conv_back = depthwise(grad_padded, kernel[::-1, ::-1], image_rows, image_cols)
    grad_image = (cotangent.astype(jnp.float32) + conv_back).astype(jnp.bfloat16)
    return (block_out, grad_image, grad_w_in, grad_w_out, small_grads)


def solution(mesh):
    placed = (
        P(("group", "row"), None, None),
        P(("group", "row"), None),
        P(),
        P(),
        P(),
        P(),
        P(),
        P(("group", "row"), None, None),
    )
    return jax.shard_map(
        shards,
        mesh=mesh,
        in_specs=placed,
        out_specs=(
            P(("group", "row"), None, None),
            P(("group", "row"), None, None),
            P(("group", "row"), None),
            P(("group", "row"), None),
            P("group", None),
        ),
        check_vma=False,
    )
```

```python
import jax
import jax.numpy as jnp
from jax import lax
from jax.sharding import PartitionSpec as P

KERNEL = 7
TILE_ROWS = 4
TILE_COLS = 128


EPSILON = 1e-06
ROOT_TWO_PI = 0.7978845608028654
CUBIC_TERM = 0.044715


def padded_2(block, sides, width):
    for axis, dim in sides:
        count = lax.axis_size(axis)
        forward = [(i, i + 1) for i in range(count - 1)]
        backward = [(target, source) for source, target in forward]
        low = lax.ppermute(
            lax.slice_in_dim(block, block.shape[dim] - width, None, axis=dim), axis, forward
        )
        high = lax.ppermute(lax.slice_in_dim(block, 0, width, axis=dim), axis, backward)
        block = jnp.concatenate([low, block, high], axis=dim)
    return block


def bit_reversed(values, count, steps, axis):
    shape = values.shape
    values = values.reshape(shape[:axis] + (2,) * steps + (shape[axis] // count,) + shape[axis + 1 :])
    order = (
        tuple(range(axis))
        + tuple(axis + steps - 1 - i for i in range(steps))
        + tuple(range(axis + steps, values.ndim))
    )
    return values.transpose(order).reshape(shape)


def halving_reduce(quartered, rows, whole, axis):
    count = lax.axis_size(axis)
    steps = count.bit_length() - 1
    if (1 << steps) != count:
        return (
            lax.psum_scatter(quartered, axis, scatter_dimension=1, tiled=True),
            lax.psum_scatter(rows, axis, scatter_dimension=0, tiled=True),
            lax.psum(whole, axis),
        )
    me = lax.axis_index(axis)
    quartered = bit_reversed(quartered, count, steps, 1)
    rows = bit_reversed(rows, count, steps, 0)
    quarters, width = quartered.shape[0], quartered.shape[2]
    for step in range(steps):
        bit = (me >> step) & 1
        pairs = [(i, i ^ (1 << step)) for i in range(count)]
        half_q = quartered.shape[1] // 2
        half_r = rows.shape[0] // 2
        keep_q = lax.dynamic_slice_in_dim(quartered, bit * half_q, half_q, axis=1)
        give_q = lax.dynamic_slice_in_dim(quartered, (1 - bit) * half_q, half_q, axis=1)
        keep_r = lax.dynamic_slice_in_dim(rows, bit * half_r, half_r, axis=0)
        give_r = lax.dynamic_slice_in_dim(rows, (1 - bit) * half_r, half_r, axis=0)
        sent = jnp.concatenate([give_q.reshape(-1, width), give_r, whole], axis=0)
        got = lax.ppermute(sent, axis, pairs)
        cut_q = quarters * half_q
        quartered = keep_q + got[:cut_q].reshape(quarters, half_q, width)
        rows = keep_r + got[cut_q : cut_q + half_r]
        whole = whole + got[cut_q + half_r :]
    return quartered, rows, whole


def gelu_value(inputs):
    tangent = jnp.tanh(ROOT_TWO_PI * (inputs + CUBIC_TERM * inputs * inputs * inputs))
    return 0.5 * inputs * (1.0 + tangent)


def gelu_slope(inputs):
    tangent = jnp.tanh(ROOT_TWO_PI * (inputs + CUBIC_TERM * inputs * inputs * inputs))
    return 0.5 * (1.0 + tangent) + 0.5 * inputs * (1.0 - tangent * tangent) * ROOT_TWO_PI * (
        1.0 + 3.0 * CUBIC_TERM * inputs * inputs
    )


def depthwise(padded, kernel, image_rows, image_cols):
    total = jnp.zeros((image_rows, image_cols, kernel.shape[-1]), jnp.float32)
    for row_tap in range(KERNEL):
        for col_tap in range(KERNEL):
            total = (
                total
                + padded[row_tap : row_tap + image_rows, col_tap : col_tap + image_cols]
                * kernel[row_tap, col_tap]
            )
    return total


def kernel_terms(padded, grads, image_rows, image_cols):
    collected = []
    for row_tap in range(KERNEL):
        for col_tap in range(KERNEL):
            collected.append(
                jnp.sum(
                    padded[row_tap : row_tap + image_rows, col_tap : col_tap + image_cols] * grads,
                    axis=(0, 1),
                )
            )
    return jnp.stack(collected)


def shards(image, tissue, kernel, ln_gain, w_in, w_out, layer_scale, cotangent):
    half_width = KERNEL // 2
    image_rows, image_cols, channels = image.shape
    hidden = w_in.shape[1]
    span = TILE_COLS + 2 * half_width

    first_col = jnp.argmax(tissue.reshape(-1)).astype(jnp.int32) * TILE_COLS
    extended = padded_2(image, (("row", 0),), half_width)
    padded = jnp.pad(extended, ((0, 0), (half_width, half_width), (0, 0)))
    window = lax.dynamic_slice_in_dim(padded, first_col, span, axis=1).astype(jnp.float32)
    filtered = depthwise(window, kernel, image_rows, TILE_COLS)
    centre = jnp.mean(filtered, axis=-1, keepdims=True)
    centered = filtered - centre
    inv_std = lax.rsqrt(jnp.mean(centered * centered, axis=-1, keepdims=True) + EPSILON)
    standard = centered * inv_std
    normed = (standard * ln_gain).astype(jnp.bfloat16)
    upstream = lax.dynamic_slice_in_dim(cotangent, first_col, TILE_COLS, axis=1).astype(jnp.float32)
    grad_out = (1.0 * layer_scale * upstream).astype(jnp.bfloat16)

    normed_flat = normed.reshape(-1, channels)
    grad_flat = grad_out.reshape(-1, channels)
    pre_act = jnp.dot(normed_flat, w_in, preferred_element_type=jnp.float32)
    act_flat = gelu_value(pre_act).astype(jnp.bfloat16)
    branch = jnp.dot(act_flat, w_out, preferred_element_type=jnp.float32)
    grad_act = jnp.dot(grad_flat, w_out.T, preferred_element_type=jnp.float32)
    pre_flat = (grad_act * gelu_slope(pre_act)).astype(jnp.bfloat16)
    grad_norm = jnp.dot(pre_flat, w_in.T, preferred_element_type=jnp.float32)
    quarters = hidden // channels
    partial_in = jnp.stack(
        [
            lax.dot_general(
                normed_flat,
                pre_flat[:, q * channels : (q + 1) * channels],
                (((0,), (0,)), ((), ())),
                preferred_element_type=jnp.float32,
            )
            for q in range(quarters)
        ]
    )
    partial_out = lax.dot_general(
        act_flat, grad_flat, (((0,), (0,)), ((), ())), preferred_element_type=jnp.float32
    )
    branch = branch.reshape(image_rows, TILE_COLS, channels)
    grad_norm = grad_norm.reshape(image_rows, TILE_COLS, channels)
    image_tile = lax.dynamic_slice_in_dim(image, first_col, TILE_COLS, axis=1)
    out_tile = (image_tile.astype(jnp.float32) + 1.0 * layer_scale * branch).astype(jnp.bfloat16)
    block_out = lax.dynamic_update_slice_in_dim(image, out_tile, first_col, axis=1)
    scale_grad = jnp.sum(1.0 * branch * upstream, axis=(0, 1))
    gain_grad = jnp.sum(grad_norm * standard, axis=(0, 1))
    grad_std = grad_norm * ln_gain
    grad_tile = (
        inv_std
        * (
            grad_std
            - jnp.mean(grad_std, axis=-1, keepdims=True)
            - standard * jnp.mean(grad_std * standard, axis=-1, keepdims=True)
        )
    ).astype(jnp.bfloat16)
    kernel_grad = kernel_terms(window, grad_tile.astype(jnp.float32), image_rows, TILE_COLS)
    packed = jnp.concatenate([kernel_grad, gain_grad[None], scale_grad[None]], axis=0)
    owned_in, grad_w_out, small_grads = halving_reduce(partial_in, partial_out, packed, "row")
    grad_w_in = owned_in.transpose(1, 0, 2).reshape(-1, hidden)
    grad_conv = lax.dynamic_update_slice_in_dim(
        jnp.zeros_like(image), grad_tile, first_col, axis=1
    )
    grad_ext = padded_2(grad_conv, (("row", 0),), half_width)
    grad_padded = jnp.pad(grad_ext.astype(jnp.float32), ((0, 0), (half_width, half_width), (0, 0)))
    conv_back = depthwise(grad_padded, kernel[::-1, ::-1], image_rows, image_cols)
    grad_image = (cotangent.astype(jnp.float32) + conv_back).astype(jnp.bfloat16)
    return (block_out, grad_image, grad_w_in, grad_w_out, small_grads)


def solution(mesh):
    placed = (
        P(("group", "row"), None, None),
        P(("group", "row"), None),
        P(),
        P(),
        P(),
        P(),
        P(),
        P(("group", "row"), None, None),
    )
    return jax.shard_map(
        shards,
        mesh=mesh,
        in_specs=placed,
        out_specs=(
            P(("group", "row"), None, None),
            P(("group", "row"), None, None),
            P(("group", "row"), None),
            P(("group", "row"), None),
            P("group", None),
        ),
        check_vma=False,
    )
```

```python
import jax
import jax.numpy as jnp
from jax import lax
from jax.sharding import PartitionSpec as P

KERNEL = 7
TILE_ROWS = 4
TILE_COLS = 128


EPSILON = 1e-06
ROOT_TWO_PI = 0.7978845608028654
CUBIC_TERM = 0.044715


def padded_2(block, sides, width):
    for axis, dim in sides:
        count = lax.axis_size(axis)
        forward = [(i, i + 1) for i in range(count - 1)]
        backward = [(target, source) for source, target in forward]
        low = lax.ppermute(
            lax.slice_in_dim(block, block.shape[dim] - width, None, axis=dim), axis, forward
        )
        high = lax.ppermute(lax.slice_in_dim(block, 0, width, axis=dim), axis, backward)
        block = jnp.concatenate([low, block, high], axis=dim)
    return block


def bit_reversed(values, count, steps):
    rest = values.shape[1:]
    values = values.reshape((2,) * steps + (values.shape[0] // count,) + rest)
    order = tuple(reversed(range(steps))) + tuple(range(steps, values.ndim))
    return values.transpose(order).reshape((-1,) + rest)


def halving_reduce(parts, whole, axis):
    count = lax.axis_size(axis)
    steps = count.bit_length() - 1
    if (1 << steps) != count:
        owned = [lax.psum_scatter(p, axis, scatter_dimension=0, tiled=True) for p in parts]
        return owned, lax.psum(whole, axis)
    me = lax.axis_index(axis)
    parts = [bit_reversed(p, count, steps) for p in parts]
    for step in range(steps):
        bit = (me >> step) & 1
        pairs = [(i, i ^ (1 << step)) for i in range(count)]
        keeps, gives = [], []
        for p in parts:
            half = p.shape[0] // 2
            keeps.append(lax.dynamic_slice_in_dim(p, bit * half, half, axis=0))
            gives.append(lax.dynamic_slice_in_dim(p, (1 - bit) * half, half, axis=0))
        if step > 0:
            gives = [g.astype(jnp.bfloat16) for g in gives]
        got, got_whole = lax.ppermute((gives, whole), axis, pairs)
        parts = [k + g.astype(jnp.float32) for k, g in zip(keeps, got)]
        whole = whole + got_whole
    return parts, whole


def gelu_value(inputs):
    tangent = jnp.tanh(ROOT_TWO_PI * (inputs + CUBIC_TERM * inputs * inputs * inputs))
    return 0.5 * inputs * (1.0 + tangent)


def gelu_slope(inputs):
    tangent = jnp.tanh(ROOT_TWO_PI * (inputs + CUBIC_TERM * inputs * inputs * inputs))
    return 0.5 * (1.0 + tangent) + 0.5 * inputs * (1.0 - tangent * tangent) * ROOT_TWO_PI * (
        1.0 + 3.0 * CUBIC_TERM * inputs * inputs
    )


def depthwise(padded, kernel, image_rows, image_cols):
    total = jnp.zeros((image_rows, image_cols, kernel.shape[-1]), jnp.float32)
    for row_tap in range(KERNEL):
        for col_tap in range(KERNEL):
            total = (
                total
                + padded[row_tap : row_tap + image_rows, col_tap : col_tap + image_cols]
                * kernel[row_tap, col_tap]
            )
    return total


def kernel_terms(padded, grads, image_rows, image_cols):
    collected = []
    for row_tap in range(KERNEL):
        for col_tap in range(KERNEL):
            collected.append(
                jnp.sum(
                    padded[row_tap : row_tap + image_rows, col_tap : col_tap + image_cols] * grads,
                    axis=(0, 1),
                )
            )
    return jnp.stack(collected)


def shards(image, tissue, kernel, ln_gain, w_in, w_out, layer_scale, cotangent):
    half_width = KERNEL // 2
    image_rows, image_cols, channels = image.shape
    hidden = w_in.shape[1]
    span = TILE_COLS + 2 * half_width

    first_col = jnp.argmax(tissue.reshape(-1)).astype(jnp.int32) * TILE_COLS
    extended = padded_2(image, (("row", 0),), half_width)
    padded = jnp.pad(extended, ((0, 0), (half_width, half_width), (0, 0)))
    window = lax.dynamic_slice_in_dim(padded, first_col, span, axis=1).astype(jnp.float32)
    filtered = depthwise(window, kernel, image_rows, TILE_COLS)
    centre = jnp.mean(filtered, axis=-1, keepdims=True)
    centered = filtered - centre
    inv_std = lax.rsqrt(jnp.mean(centered * centered, axis=-1, keepdims=True) + EPSILON)
    standard = centered * inv_std
    normed = (standard * ln_gain).astype(jnp.bfloat16)
    upstream = lax.dynamic_slice_in_dim(cotangent, first_col, TILE_COLS, axis=1).astype(jnp.float32)
    grad_out = (1.0 * layer_scale * upstream).astype(jnp.bfloat16)

    normed_flat = normed.reshape(-1, channels)
    grad_flat = grad_out.reshape(-1, channels)
    pre_act = jnp.dot(normed_flat, w_in, preferred_element_type=jnp.float32)
    act_flat = gelu_value(pre_act).astype(jnp.bfloat16)
    branch = jnp.dot(act_flat, w_out, preferred_element_type=jnp.float32)
    grad_act = jnp.dot(grad_flat, w_out.T, preferred_element_type=jnp.float32)
    pre_flat = (grad_act * gelu_slope(pre_act)).astype(jnp.bfloat16)
    grad_norm = jnp.dot(pre_flat, w_in.T, preferred_element_type=jnp.float32)
    partial_in = lax.dot_general(
        normed_flat, pre_flat, (((0,), (0,)), ((), ())), preferred_element_type=jnp.float32
    )
    partial_out = lax.dot_general(
        act_flat, grad_flat, (((0,), (0,)), ((), ())), preferred_element_type=jnp.float32
    )
    branch = branch.reshape(image_rows, TILE_COLS, channels)
    grad_norm = grad_norm.reshape(image_rows, TILE_COLS, channels)
    image_tile = lax.dynamic_slice_in_dim(image, first_col, TILE_COLS, axis=1)
    out_tile = (image_tile.astype(jnp.float32) + 1.0 * layer_scale * branch).astype(jnp.bfloat16)
    block_out = lax.dynamic_update_slice_in_dim(image, out_tile, first_col, axis=1)
    scale_grad = jnp.sum(1.0 * branch * upstream, axis=(0, 1))
    gain_grad = jnp.sum(grad_norm * standard, axis=(0, 1))
    grad_std = grad_norm * ln_gain
    grad_tile = (
        inv_std
        * (
            grad_std
            - jnp.mean(grad_std, axis=-1, keepdims=True)
            - standard * jnp.mean(grad_std * standard, axis=-1, keepdims=True)
        )
    ).astype(jnp.bfloat16)
    kernel_grad = kernel_terms(window, grad_tile.astype(jnp.float32), image_rows, TILE_COLS)
    packed = jnp.concatenate([kernel_grad, gain_grad[None], scale_grad[None]], axis=0)
    (grad_w_in, grad_w_out), small_grads = halving_reduce([partial_in, partial_out], packed, "row")
    grad_conv = lax.dynamic_update_slice_in_dim(
        jnp.zeros_like(image), grad_tile, first_col, axis=1
    )
    grad_ext = padded_2(grad_conv, (("row", 0),), half_width)
    grad_padded = jnp.pad(grad_ext.astype(jnp.float32), ((0, 0), (half_width, half_width), (0, 0)))
    conv_back = depthwise(grad_padded, kernel[::-1, ::-1], image_rows, image_cols)
    grad_image = (cotangent.astype(jnp.float32) + conv_back).astype(jnp.bfloat16)
    return (block_out, grad_image, grad_w_in, grad_w_out, small_grads)


def solution(mesh):
    placed = (
        P(("group", "row"), None, None),
        P(("group", "row"), None),
        P(),
        P(),
        P(),
        P(),
        P(),
        P(("group", "row"), None, None),
    )
    return jax.shard_map(
        shards,
        mesh=mesh,
        in_specs=placed,
        out_specs=(
            P(("group", "row"), None, None),
            P(("group", "row"), None, None),
            P(("group", "row"), None),
            P(("group", "row"), None),
            P("group", None),
        ),
        check_vma=False,
    )
```

```python
import jax
import jax.numpy as jnp
from jax import lax
from jax.sharding import PartitionSpec as P

KERNEL = 7
TILE_ROWS = 4
TILE_COLS = 128


EPSILON = 1e-06
ROOT_TWO_PI = 0.7978845608028654
CUBIC_TERM = 0.044715


def padded_2(block, sides, width):
    for axis, dim in sides:
        count = lax.axis_size(axis)
        forward = [(i, i + 1) for i in range(count - 1)]
        backward = [(target, source) for source, target in forward]
        low = lax.ppermute(
            lax.slice_in_dim(block, block.shape[dim] - width, None, axis=dim), axis, forward
        )
        high = lax.ppermute(lax.slice_in_dim(block, 0, width, axis=dim), axis, backward)
        block = jnp.concatenate([low, block, high], axis=dim)
    return block


def bit_reversed(values, count, steps):
    rest = values.shape[1:]
    values = values.reshape((2,) * steps + (values.shape[0] // count,) + rest)
    order = tuple(reversed(range(steps))) + tuple(range(steps, values.ndim))
    return values.transpose(order).reshape((-1,) + rest)


def halving_reduce(parts, whole, axis):
    count = lax.axis_size(axis)
    steps = count.bit_length() - 1
    if (1 << steps) != count:
        owned = [lax.psum_scatter(p, axis, scatter_dimension=0, tiled=True) for p in parts]
        return owned, lax.psum(whole, axis)
    me = lax.axis_index(axis)
    parts = [bit_reversed(p, count, steps) for p in parts]
    for step in range(steps):
        bit = (me >> step) & 1
        pairs = [(i, i ^ (1 << step)) for i in range(count)]
        keeps, gives = [], []
        for p in parts:
            half = p.shape[0] // 2
            keeps.append(lax.dynamic_slice_in_dim(p, bit * half, half, axis=0))
            gives.append(lax.dynamic_slice_in_dim(p, (1 - bit) * half, half, axis=0))
        if step > 0:
            gives = [g.astype(jnp.bfloat16) for g in gives]
        got, got_whole = lax.ppermute((gives, whole), axis, pairs)
        parts = [k + g.astype(jnp.float32) for k, g in zip(keeps, got)]
        whole = whole + got_whole
    return parts, whole


def halo_rows(block, axis, width):
    count = lax.axis_size(axis)
    forward = [(i, i + 1) for i in range(count - 1)]
    backward = [(target, source) for source, target in forward]
    low = lax.ppermute(lax.slice_in_dim(block, block.shape[0] - width, None, axis=0), axis, forward)
    high = lax.ppermute(lax.slice_in_dim(block, 0, width, axis=0), axis, backward)
    return low, high


def gelu_value(inputs):
    tangent = jnp.tanh(ROOT_TWO_PI * (inputs + CUBIC_TERM * inputs * inputs * inputs))
    return 0.5 * inputs * (1.0 + tangent)


def gelu_slope(inputs):
    tangent = jnp.tanh(ROOT_TWO_PI * (inputs + CUBIC_TERM * inputs * inputs * inputs))
    return 0.5 * (1.0 + tangent) + 0.5 * inputs * (1.0 - tangent * tangent) * ROOT_TWO_PI * (
        1.0 + 3.0 * CUBIC_TERM * inputs * inputs
    )


def depthwise(padded, kernel, image_rows, image_cols):
    total = jnp.zeros((image_rows, image_cols, kernel.shape[-1]), jnp.float32)
    for row_tap in range(KERNEL):
        for col_tap in range(KERNEL):
            total = (
                total
                + padded[row_tap : row_tap + image_rows, col_tap : col_tap + image_cols]
                * kernel[row_tap, col_tap]
            )
    return total


def kernel_terms(padded, grads, image_rows, image_cols):
    collected = []
    for row_tap in range(KERNEL):
        for col_tap in range(KERNEL):
            collected.append(
                jnp.sum(
                    padded[row_tap : row_tap + image_rows, col_tap : col_tap + image_cols] * grads,
                    axis=(0, 1),
                )
            )
    return jnp.stack(collected)


def shards(image, tissue, kernel, ln_gain, w_in, w_out, layer_scale, cotangent):
    half_width = KERNEL // 2
    image_rows, image_cols, channels = image.shape
    hidden = w_in.shape[1]
    span = TILE_COLS + 2 * half_width

    first_col = jnp.argmax(tissue.reshape(-1)).astype(jnp.int32) * TILE_COLS
    extended = padded_2(image, (("row", 0),), half_width)
    padded = jnp.pad(extended, ((0, 0), (half_width, half_width), (0, 0)))
    window = lax.dynamic_slice_in_dim(padded, first_col, span, axis=1).astype(jnp.float32)
    filtered = depthwise(window, kernel, image_rows, TILE_COLS)
    centre = jnp.mean(filtered, axis=-1, keepdims=True)
    centered = filtered - centre
    inv_std = lax.rsqrt(jnp.mean(centered * centered, axis=-1, keepdims=True) + EPSILON)
    standard = centered * inv_std
    normed = (standard * ln_gain).astype(jnp.bfloat16)
    upstream = lax.dynamic_slice_in_dim(cotangent, first_col, TILE_COLS, axis=1).astype(jnp.float32)
    grad_out = (1.0 * layer_scale * upstream).astype(jnp.bfloat16)

    normed_flat = normed.reshape(-1, channels)
    grad_flat = grad_out.reshape(-1, channels)
    pre_act = jnp.dot(normed_flat, w_in, preferred_element_type=jnp.float32)
    act_flat = gelu_value(pre_act).astype(jnp.bfloat16)
    branch = jnp.dot(act_flat, w_out, preferred_element_type=jnp.float32)
    grad_act = jnp.dot(grad_flat, w_out.T, preferred_element_type=jnp.float32)
    pre_flat = (grad_act * gelu_slope(pre_act)).astype(jnp.bfloat16)
    grad_norm = jnp.dot(pre_flat, w_in.T, preferred_element_type=jnp.float32)
    partial_in = lax.dot_general(
        normed_flat, pre_flat, (((0,), (0,)), ((), ())), preferred_element_type=jnp.float32
    )
    partial_out = lax.dot_general(
        act_flat, grad_flat, (((0,), (0,)), ((), ())), preferred_element_type=jnp.float32
    )
    branch = branch.reshape(image_rows, TILE_COLS, channels)
    grad_norm = grad_norm.reshape(image_rows, TILE_COLS, channels)
    image_tile = lax.dynamic_slice_in_dim(image, first_col, TILE_COLS, axis=1)
    out_tile = (image_tile.astype(jnp.float32) + 1.0 * layer_scale * branch).astype(jnp.bfloat16)
    block_out = lax.dynamic_update_slice_in_dim(image, out_tile, first_col, axis=1)
    scale_grad = jnp.sum(1.0 * branch * upstream, axis=(0, 1))
    gain_grad = jnp.sum(grad_norm * standard, axis=(0, 1))
    grad_std = grad_norm * ln_gain
    grad_tile = (
        inv_std
        * (
            grad_std
            - jnp.mean(grad_std, axis=-1, keepdims=True)
            - standard * jnp.mean(grad_std * standard, axis=-1, keepdims=True)
        )
    ).astype(jnp.bfloat16)
    kernel_grad = kernel_terms(window, grad_tile.astype(jnp.float32), image_rows, TILE_COLS)
    packed = jnp.concatenate([kernel_grad, gain_grad[None], scale_grad[None]], axis=0)
    (grad_w_in, grad_w_out), small_grads = halving_reduce([partial_in, partial_out], packed, "row")
    flipped = kernel[::-1, ::-1]
    tile_padded = jnp.pad(
        grad_tile.astype(jnp.float32),
        ((half_width, half_width), (2 * half_width, 2 * half_width), (0, 0)),
    )
    own = depthwise(tile_padded, flipped, image_rows, span)
    own_full = lax.dynamic_update_slice_in_dim(
        jnp.zeros((image_rows, image_cols + 2 * half_width, channels), jnp.float32),
        own,
        first_col,
        axis=1,
    )[:, half_width : half_width + image_cols]
    grad_conv = lax.dynamic_update_slice_in_dim(
        jnp.zeros_like(image), grad_tile, first_col, axis=1
    )
    low, high = halo_rows(grad_conv, "row", half_width)
    edge = ((0, 0), (half_width, half_width), (0, 0))
    low = jnp.pad(low.astype(jnp.float32), edge)
    high = jnp.pad(high.astype(jnp.float32), edge)
    halo_out = []
    for out_row in range(image_rows):
        total = jnp.zeros((image_cols, channels), jnp.float32)
        for row_tap in range(KERNEL):
            source = out_row + row_tap
            if source < half_width:
                line = low[source]
            elif source >= half_width + image_rows:
                line = high[source - half_width - image_rows]
            else:
                continue
            for col_tap in range(KERNEL):
                total = total + line[col_tap : col_tap + image_cols] * flipped[row_tap, col_tap]
        halo_out.append(total)
    conv_back = own_full + jnp.stack(halo_out)
    grad_image = (cotangent.astype(jnp.float32) + conv_back).astype(jnp.bfloat16)
    return (block_out, grad_image, grad_w_in, grad_w_out, small_grads)


def solution(mesh):
    placed = (
        P(("group", "row"), None, None),
        P(("group", "row"), None),
        P(),
        P(),
        P(),
        P(),
        P(),
        P(("group", "row"), None, None),
    )
    return jax.shard_map(
        shards,
        mesh=mesh,
        in_specs=placed,
        out_specs=(
            P(("group", "row"), None, None),
            P(("group", "row"), None, None),
            P(("group", "row"), None),
            P(("group", "row"), None),
            P("group", None),
        ),
        check_vma=False,
    )
```

```python
import jax
import jax.numpy as jnp
from jax import lax
from jax.sharding import PartitionSpec as P

KERNEL = 7
TILE_ROWS = 4
TILE_COLS = 128


EPSILON = 1e-06
ROOT_TWO_PI = 0.7978845608028654
CUBIC_TERM = 0.044715


def padded_2(block, sides, width):
    for axis, dim in sides:
        count = lax.axis_size(axis)
        forward = [(i, i + 1) for i in range(count - 1)]
        backward = [(target, source) for source, target in forward]
        low = lax.ppermute(
            lax.slice_in_dim(block, block.shape[dim] - width, None, axis=dim), axis, forward
        )
        high = lax.ppermute(lax.slice_in_dim(block, 0, width, axis=dim), axis, backward)
        block = jnp.concatenate([low, block, high], axis=dim)
    return block


def bit_reversed(values, count, steps):
    rest = values.shape[1:]
    values = values.reshape((2,) * steps + (values.shape[0] // count,) + rest)
    order = tuple(reversed(range(steps))) + tuple(range(steps, values.ndim))
    return values.transpose(order).reshape((-1,) + rest)


def halving_reduce(parts, whole, axis):
    count = lax.axis_size(axis)
    steps = count.bit_length() - 1
    if (1 << steps) != count:
        owned = [lax.psum_scatter(p, axis, scatter_dimension=0, tiled=True) for p in parts]
        return owned, lax.psum(whole, axis)
    me = lax.axis_index(axis)
    parts = [bit_reversed(p, count, steps) for p in parts]
    for step in range(steps):
        bit = (me >> step) & 1
        pairs = [(i, i ^ (1 << step)) for i in range(count)]
        keeps, gives = [], []
        for p in parts:
            half = p.shape[0] // 2
            keeps.append(lax.dynamic_slice_in_dim(p, bit * half, half, axis=0))
            gives.append(lax.dynamic_slice_in_dim(p, (1 - bit) * half, half, axis=0))
        if step > 0:
            gives = [g.astype(jnp.bfloat16) for g in gives]
        got, got_whole = lax.ppermute((gives, whole), axis, pairs)
        parts = [k + g.astype(jnp.float32) for k, g in zip(keeps, got)]
        whole = whole + got_whole
        parts, whole = lax.optimization_barrier((parts, whole))
    return parts, whole


def halo_rows(block, axis, width):
    count = lax.axis_size(axis)
    forward = [(i, i + 1) for i in range(count - 1)]
    backward = [(target, source) for source, target in forward]
    low = lax.ppermute(lax.slice_in_dim(block, block.shape[0] - width, None, axis=0), axis, forward)
    high = lax.ppermute(lax.slice_in_dim(block, 0, width, axis=0), axis, backward)
    return low, high


def gelu_value(inputs):
    tangent = jnp.tanh(ROOT_TWO_PI * (inputs + CUBIC_TERM * inputs * inputs * inputs))
    return 0.5 * inputs * (1.0 + tangent)


def gelu_slope(inputs):
    tangent = jnp.tanh(ROOT_TWO_PI * (inputs + CUBIC_TERM * inputs * inputs * inputs))
    return 0.5 * (1.0 + tangent) + 0.5 * inputs * (1.0 - tangent * tangent) * ROOT_TWO_PI * (
        1.0 + 3.0 * CUBIC_TERM * inputs * inputs
    )


def depthwise(padded, kernel, image_rows, image_cols):
    total = jnp.zeros((image_rows, image_cols, kernel.shape[-1]), jnp.float32)
    for row_tap in range(KERNEL):
        for col_tap in range(KERNEL):
            total = (
                total
                + padded[row_tap : row_tap + image_rows, col_tap : col_tap + image_cols]
                * kernel[row_tap, col_tap]
            )
    return total


def kernel_terms(padded, grads, image_rows, image_cols):
    collected = []
    for row_tap in range(KERNEL):
        for col_tap in range(KERNEL):
            collected.append(
                jnp.sum(
                    padded[row_tap : row_tap + image_rows, col_tap : col_tap + image_cols] * grads,
                    axis=(0, 1),
                )
            )
    return jnp.stack(collected)


def shards(image, tissue, kernel, ln_gain, w_in, w_out, layer_scale, cotangent):
    half_width = KERNEL // 2
    image_rows, image_cols, channels = image.shape
    hidden = w_in.shape[1]
    span = TILE_COLS + 2 * half_width

    first_col = jnp.argmax(tissue.reshape(-1)).astype(jnp.int32) * TILE_COLS
    extended = padded_2(image, (("row", 0),), half_width)
    padded = jnp.pad(extended, ((0, 0), (half_width, half_width), (0, 0)))
    window = lax.dynamic_slice_in_dim(padded, first_col, span, axis=1).astype(jnp.float32)
    filtered = depthwise(window, kernel, image_rows, TILE_COLS)
    centre = jnp.mean(filtered, axis=-1, keepdims=True)
    centered = filtered - centre
    inv_std = lax.rsqrt(jnp.mean(centered * centered, axis=-1, keepdims=True) + EPSILON)
    standard = centered * inv_std
    normed = (standard * ln_gain).astype(jnp.bfloat16)
    upstream = lax.dynamic_slice_in_dim(cotangent, first_col, TILE_COLS, axis=1).astype(jnp.float32)
    grad_out = (1.0 * layer_scale * upstream).astype(jnp.bfloat16)

    normed_flat = normed.reshape(-1, channels)
    grad_flat = grad_out.reshape(-1, channels)
    pre_act = jnp.dot(normed_flat, w_in, preferred_element_type=jnp.float32)
    act_flat = gelu_value(pre_act).astype(jnp.bfloat16)
    branch = jnp.dot(act_flat, w_out, preferred_element_type=jnp.float32)
    grad_act = jnp.dot(grad_flat, w_out.T, preferred_element_type=jnp.float32)
    pre_flat = (grad_act * gelu_slope(pre_act)).astype(jnp.bfloat16)
    grad_norm = jnp.dot(pre_flat, w_in.T, preferred_element_type=jnp.float32)
    partial_in = lax.dot_general(
        normed_flat, pre_flat, (((0,), (0,)), ((), ())), preferred_element_type=jnp.float32
    )
    partial_out = lax.dot_general(
        act_flat, grad_flat, (((0,), (0,)), ((), ())), preferred_element_type=jnp.float32
    )
    branch = branch.reshape(image_rows, TILE_COLS, channels)
    grad_norm = grad_norm.reshape(image_rows, TILE_COLS, channels)
    image_tile = lax.dynamic_slice_in_dim(image, first_col, TILE_COLS, axis=1)
    out_tile = (image_tile.astype(jnp.float32) + 1.0 * layer_scale * branch).astype(jnp.bfloat16)
    block_out = lax.dynamic_update_slice_in_dim(image, out_tile, first_col, axis=1)
    scale_grad = jnp.sum(1.0 * branch * upstream, axis=(0, 1))
    gain_grad = jnp.sum(grad_norm * standard, axis=(0, 1))
    grad_std = grad_norm * ln_gain
    grad_tile = (
        inv_std
        * (
            grad_std
            - jnp.mean(grad_std, axis=-1, keepdims=True)
            - standard * jnp.mean(grad_std * standard, axis=-1, keepdims=True)
        )
    ).astype(jnp.bfloat16)
    kernel_grad = kernel_terms(window, grad_tile.astype(jnp.float32), image_rows, TILE_COLS)
    packed = jnp.concatenate([kernel_grad, gain_grad[None], scale_grad[None]], axis=0)
    (grad_w_in, grad_w_out), small_grads = halving_reduce([partial_in, partial_out], packed, "row")
    flipped = kernel[::-1, ::-1]
    tile_padded = jnp.pad(
        grad_tile.astype(jnp.float32),
        ((half_width, half_width), (2 * half_width, 2 * half_width), (0, 0)),
    )
    own = depthwise(tile_padded, flipped, image_rows, span)
    own_full = lax.dynamic_update_slice_in_dim(
        jnp.zeros((image_rows, image_cols + 2 * half_width, channels), jnp.float32),
        own,
        first_col,
        axis=1,
    )[:, half_width : half_width + image_cols]
    grad_conv = lax.dynamic_update_slice_in_dim(
        jnp.zeros_like(image), grad_tile, first_col, axis=1
    )
    low, high = halo_rows(grad_conv, "row", half_width)
    edge = ((0, 0), (half_width, half_width), (0, 0))
    low = jnp.pad(low.astype(jnp.float32), edge)
    high = jnp.pad(high.astype(jnp.float32), edge)
    halo_out = []
    for out_row in range(image_rows):
        total = jnp.zeros((image_cols, channels), jnp.float32)
        for row_tap in range(KERNEL):
            source = out_row + row_tap
            if source < half_width:
                line = low[source]
            elif source >= half_width + image_rows:
                line = high[source - half_width - image_rows]
            else:
                continue
            for col_tap in range(KERNEL):
                total = total + line[col_tap : col_tap + image_cols] * flipped[row_tap, col_tap]
        halo_out.append(total)
    conv_back = own_full + jnp.stack(halo_out)
    grad_image = (cotangent.astype(jnp.float32) + conv_back).astype(jnp.bfloat16)
    return (block_out, grad_image, grad_w_in, grad_w_out, small_grads)


def solution(mesh):
    placed = (
        P(("group", "row"), None, None),
        P(("group", "row"), None),
        P(),
        P(),
        P(),
        P(),
        P(),
        P(("group", "row"), None, None),
    )
    return jax.shard_map(
        shards,
        mesh=mesh,
        in_specs=placed,
        out_specs=(
            P(("group", "row"), None, None),
            P(("group", "row"), None, None),
            P(("group", "row"), None),
            P(("group", "row"), None),
            P("group", None),
        ),
        check_vma=False,
    )
```

```python
import jax
import jax.numpy as jnp
from jax import lax
from jax.sharding import PartitionSpec as P

KERNEL = 7
TILE_ROWS = 4
TILE_COLS = 128


EPSILON = 1e-06
ROOT_TWO_PI = 0.7978845608028654
CUBIC_TERM = 0.044715


def padded_2(block, sides, width):
    for axis, dim in sides:
        count = lax.axis_size(axis)
        forward = [(i, i + 1) for i in range(count - 1)]
        backward = [(target, source) for source, target in forward]
        low = lax.ppermute(
            lax.slice_in_dim(block, block.shape[dim] - width, None, axis=dim), axis, forward
        )
        high = lax.ppermute(lax.slice_in_dim(block, 0, width, axis=dim), axis, backward)
        block = jnp.concatenate([low, block, high], axis=dim)
    return block


def bit_reversed(values, count, steps, axis):
    shape = values.shape
    values = values.reshape(shape[:axis] + (2,) * steps + (shape[axis] // count,) + shape[axis + 1 :])
    order = (
        tuple(range(axis))
        + tuple(axis + steps - 1 - i for i in range(steps))
        + tuple(range(axis + steps, values.ndim))
    )
    return values.transpose(order).reshape(shape)


def split_pair(values):
    high = values.astype(jnp.bfloat16)
    low = (values - high.astype(jnp.float32)).astype(jnp.bfloat16)
    return high, low


def halving_reduce(quartered, rows, whole, axis):
    count = lax.axis_size(axis)
    steps = count.bit_length() - 1
    if (1 << steps) != count:
        return (
            lax.psum_scatter(quartered, axis, scatter_dimension=1, tiled=True),
            lax.psum_scatter(rows, axis, scatter_dimension=0, tiled=True),
            lax.psum(whole, axis),
        )
    me = lax.axis_index(axis)
    quartered = bit_reversed(quartered, count, steps, 1)
    rows = bit_reversed(rows, count, steps, 0)
    quarters, width = quartered.shape[0], quartered.shape[2]
    for step in range(steps):
        bit = (me >> step) & 1
        pairs = [(i, i ^ (1 << step)) for i in range(count)]
        half_q = quartered.shape[1] // 2
        half_r = rows.shape[0] // 2
        keep_q = lax.dynamic_slice_in_dim(quartered, bit * half_q, half_q, axis=1)
        give_q = lax.dynamic_slice_in_dim(quartered, (1 - bit) * half_q, half_q, axis=1)
        keep_r = lax.dynamic_slice_in_dim(rows, bit * half_r, half_r, axis=0)
        give_r = lax.dynamic_slice_in_dim(rows, (1 - bit) * half_r, half_r, axis=0)
        if step == 0:
            got_q, got_r, got_whole = lax.ppermute((give_q, give_r, whole), axis, pairs)
            whole = whole + got_whole
        else:
            high, low = split_pair(whole)
            sent = jnp.concatenate(
                [give_q.astype(jnp.bfloat16).reshape(-1, width), give_r.astype(jnp.bfloat16), high, low],
                axis=0,
            )
            got = lax.ppermute(sent, axis, pairs)
            cut_q = quarters * half_q
            cut_r = cut_q + half_r
            size = whole.shape[0]
            got_q = got[:cut_q].reshape(quarters, half_q, width)
            got_r = got[cut_q:cut_r]
            mine = high.astype(jnp.float32) + low.astype(jnp.float32)
            theirs = got[cut_r : cut_r + size].astype(jnp.float32) + got[cut_r + size :].astype(
                jnp.float32
            )
            whole = mine + theirs
        quartered = keep_q + got_q.astype(jnp.float32)
        rows = keep_r + got_r.astype(jnp.float32)
        quartered, rows, whole = lax.optimization_barrier((quartered, rows, whole))
    return quartered, rows, whole


def halo_rows(block, axis, width):
    count = lax.axis_size(axis)
    forward = [(i, i + 1) for i in range(count - 1)]
    backward = [(target, source) for source, target in forward]
    low = lax.ppermute(lax.slice_in_dim(block, block.shape[0] - width, None, axis=0), axis, forward)
    high = lax.ppermute(lax.slice_in_dim(block, 0, width, axis=0), axis, backward)
    return low, high


def gelu_value(inputs):
    tangent = jnp.tanh(ROOT_TWO_PI * (inputs + CUBIC_TERM * inputs * inputs * inputs))
    return 0.5 * inputs * (1.0 + tangent)


def gelu_slope(inputs):
    tangent = jnp.tanh(ROOT_TWO_PI * (inputs + CUBIC_TERM * inputs * inputs * inputs))
    return 0.5 * (1.0 + tangent) + 0.5 * inputs * (1.0 - tangent * tangent) * ROOT_TWO_PI * (
        1.0 + 3.0 * CUBIC_TERM * inputs * inputs
    )


def depthwise(padded, kernel, image_rows, image_cols):
    total = jnp.zeros((image_rows, image_cols, kernel.shape[-1]), jnp.float32)
    for row_tap in range(KERNEL):
        for col_tap in range(KERNEL):
            total = (
                total
                + padded[row_tap : row_tap + image_rows, col_tap : col_tap + image_cols]
                * kernel[row_tap, col_tap]
            )
    return total


def kernel_terms(padded, grads, image_rows, image_cols):
    collected = []
    for row_tap in range(KERNEL):
        for col_tap in range(KERNEL):
            collected.append(
                jnp.sum(
                    padded[row_tap : row_tap + image_rows, col_tap : col_tap + image_cols] * grads,
                    axis=(0, 1),
                )
            )
    return jnp.stack(collected)


def shards(image, tissue, kernel, ln_gain, w_in, w_out, layer_scale, cotangent):
    half_width = KERNEL // 2
    image_rows, image_cols, channels = image.shape
    hidden = w_in.shape[1]
    span = TILE_COLS + 2 * half_width

    first_col = jnp.argmax(tissue.reshape(-1)).astype(jnp.int32) * TILE_COLS
    extended = padded_2(image, (("row", 0),), half_width)
    padded = jnp.pad(extended, ((0, 0), (half_width, half_width), (0, 0)))
    window = lax.dynamic_slice_in_dim(padded, first_col, span, axis=1).astype(jnp.float32)
    filtered = depthwise(window, kernel, image_rows, TILE_COLS)
    centre = jnp.mean(filtered, axis=-1, keepdims=True)
    centered = filtered - centre
    inv_std = lax.rsqrt(jnp.mean(centered * centered, axis=-1, keepdims=True) + EPSILON)
    standard = centered * inv_std
    normed = (standard * ln_gain).astype(jnp.bfloat16)
    upstream = lax.dynamic_slice_in_dim(cotangent, first_col, TILE_COLS, axis=1).astype(jnp.float32)
    grad_out = (1.0 * layer_scale * upstream).astype(jnp.bfloat16)

    normed_flat = normed.reshape(-1, channels)
    grad_flat = grad_out.reshape(-1, channels)
    pre_act = jnp.dot(normed_flat, w_in, preferred_element_type=jnp.float32)
    act_flat = gelu_value(pre_act).astype(jnp.bfloat16)
    branch = jnp.dot(act_flat, w_out, preferred_element_type=jnp.float32)
    grad_act = jnp.dot(grad_flat, w_out.T, preferred_element_type=jnp.float32)
    pre_flat = (grad_act * gelu_slope(pre_act)).astype(jnp.bfloat16)
    grad_norm = jnp.dot(pre_flat, w_in.T, preferred_element_type=jnp.float32)
    quarters = hidden // channels
    partial_in = jnp.stack(
        [
            lax.dot_general(
                normed_flat,
                pre_flat[:, q * channels : (q + 1) * channels],
                (((0,), (0,)), ((), ())),
                preferred_element_type=jnp.float32,
            )
            for q in range(quarters)
        ]
    )
    partial_out = lax.dot_general(
        act_flat, grad_flat, (((0,), (0,)), ((), ())), preferred_element_type=jnp.float32
    )
    branch = branch.reshape(image_rows, TILE_COLS, channels)
    grad_norm = grad_norm.reshape(image_rows, TILE_COLS, channels)
    image_tile = lax.dynamic_slice_in_dim(image, first_col, TILE_COLS, axis=1)
    out_tile = (image_tile.astype(jnp.float32) + 1.0 * layer_scale * branch).astype(jnp.bfloat16)
    block_out = lax.dynamic_update_slice_in_dim(image, out_tile, first_col, axis=1)
    scale_grad = jnp.sum(1.0 * branch * upstream, axis=(0, 1))
    gain_grad = jnp.sum(grad_norm * standard, axis=(0, 1))
    grad_std = grad_norm * ln_gain
    grad_tile = (
        inv_std
        * (
            grad_std
            - jnp.mean(grad_std, axis=-1, keepdims=True)
            - standard * jnp.mean(grad_std * standard, axis=-1, keepdims=True)
        )
    ).astype(jnp.bfloat16)
    kernel_grad = kernel_terms(window, grad_tile.astype(jnp.float32), image_rows, TILE_COLS)
    packed = jnp.concatenate([kernel_grad, gain_grad[None], scale_grad[None]], axis=0)
    owned_in, grad_w_out, small_grads = halving_reduce(partial_in, partial_out, packed, "row")
    grad_w_in = owned_in.transpose(1, 0, 2).reshape(-1, hidden)
    flipped = kernel[::-1, ::-1]
    tile_padded = jnp.pad(
        grad_tile.astype(jnp.float32),
        ((half_width, half_width), (2 * half_width, 2 * half_width), (0, 0)),
    )
    own = depthwise(tile_padded, flipped, image_rows, span)
    own_full = lax.dynamic_update_slice_in_dim(
        jnp.zeros((image_rows, image_cols + 2 * half_width, channels), jnp.float32),
        own,
        first_col,
        axis=1,
    )[:, half_width : half_width + image_cols]
    grad_conv = lax.dynamic_update_slice_in_dim(
        jnp.zeros_like(image), grad_tile, first_col, axis=1
    )
    low, high = halo_rows(grad_conv, "row", half_width)
    edge = ((0, 0), (half_width, half_width), (0, 0))
    low = jnp.pad(low.astype(jnp.float32), edge)
    high = jnp.pad(high.astype(jnp.float32), edge)
    halo_out = []
    for out_row in range(image_rows):
        total = jnp.zeros((image_cols, channels), jnp.float32)
        for row_tap in range(KERNEL):
            source = out_row + row_tap
            if source < half_width:
                line = low[source]
            elif source >= half_width + image_rows:
                line = high[source - half_width - image_rows]
            else:
                continue
            for col_tap in range(KERNEL):
                total = total + line[col_tap : col_tap + image_cols] * flipped[row_tap, col_tap]
        halo_out.append(total)
    conv_back = own_full + jnp.stack(halo_out)
    grad_image = (cotangent.astype(jnp.float32) + conv_back).astype(jnp.bfloat16)
    return (block_out, grad_image, grad_w_in, grad_w_out, small_grads)


def solution(mesh):
    placed = (
        P(("group", "row"), None, None),
        P(("group", "row"), None),
        P(),
        P(),
        P(),
        P(),
        P(),
        P(("group", "row"), None, None),
    )
    return jax.shard_map(
        shards,
        mesh=mesh,
        in_specs=placed,
        out_specs=(
            P(("group", "row"), None, None),
            P(("group", "row"), None, None),
            P(("group", "row"), None),
            P(("group", "row"), None),
            P("group", None),
        ),
        check_vma=False,
    )
```

```python
import jax
import jax.numpy as jnp
from jax import lax
from jax.sharding import PartitionSpec as P

KERNEL = 7
TILE_ROWS = 4
TILE_COLS = 128


EPSILON = 1e-06
ROOT_TWO_PI = 0.7978845608028654
CUBIC_TERM = 0.044715


def padded_2(block, sides, width):
    for axis, dim in sides:
        count = lax.axis_size(axis)
        forward = [(i, i + 1) for i in range(count - 1)]
        backward = [(target, source) for source, target in forward]
        low = lax.ppermute(
            lax.slice_in_dim(block, block.shape[dim] - width, None, axis=dim), axis, forward
        )
        high = lax.ppermute(lax.slice_in_dim(block, 0, width, axis=dim), axis, backward)
        block = jnp.concatenate([low, block, high], axis=dim)
    return block


def bit_reversed(values, count, steps, axis):
    shape = values.shape
    values = values.reshape(shape[:axis] + (2,) * steps + (shape[axis] // count,) + shape[axis + 1 :])
    order = (
        tuple(range(axis))
        + tuple(axis + steps - 1 - i for i in range(steps))
        + tuple(range(axis + steps, values.ndim))
    )
    return values.transpose(order).reshape(shape)


def split_pair(values):
    high = values.astype(jnp.bfloat16)
    low = (values - high.astype(jnp.float32)).astype(jnp.bfloat16)
    return high, low


def halving_reduce(quartered, rows, whole, axis, riders):
    count = lax.axis_size(axis)
    steps = count.bit_length() - 1
    if (1 << steps) != count:
        return (
            lax.psum_scatter(quartered, axis, scatter_dimension=1, tiled=True),
            lax.psum_scatter(rows, axis, scatter_dimension=0, tiled=True),
            lax.psum(whole, axis),
            riders,
        )
    me = lax.axis_index(axis)
    riders = list(riders)
    quartered = bit_reversed(quartered, count, steps, 1)
    rows = bit_reversed(rows, count, steps, 0)
    quarters, width = quartered.shape[0], quartered.shape[2]
    for step in range(steps):
        bit = (me >> step) & 1
        pairs = [(i, i ^ (1 << step)) for i in range(count)]
        half_q = quartered.shape[1] // 2
        half_r = rows.shape[0] // 2
        keep_q = lax.dynamic_slice_in_dim(quartered, bit * half_q, half_q, axis=1)
        give_q = lax.dynamic_slice_in_dim(quartered, (1 - bit) * half_q, half_q, axis=1)
        keep_r = lax.dynamic_slice_in_dim(rows, bit * half_r, half_r, axis=0)
        give_r = lax.dynamic_slice_in_dim(rows, (1 - bit) * half_r, half_r, axis=0)
        if step == 0:
            got_q, got_r, got_whole = lax.ppermute((give_q, give_r, whole), axis, pairs)
            whole = whole + got_whole
        else:
            high, low = split_pair(whole)
            sent = jnp.concatenate(
                [give_q.astype(jnp.bfloat16).reshape(-1, width), give_r.astype(jnp.bfloat16), high, low],
                axis=0,
            )
            got = lax.ppermute(sent, axis, pairs)
            cut_q = quarters * half_q
            cut_r = cut_q + half_r
            size = whole.shape[0]
            got_q = got[:cut_q].reshape(quarters, half_q, width)
            got_r = got[cut_q:cut_r]
            mine = high.astype(jnp.float32) + low.astype(jnp.float32)
            theirs = got[cut_r : cut_r + size].astype(jnp.float32) + got[cut_r + size :].astype(
                jnp.float32
            )
            whole = mine + theirs
        quartered = keep_q + got_q.astype(jnp.float32)
        rows = keep_r + got_r.astype(jnp.float32)
        if step < len(riders):
            quartered, rows, whole, riders[step] = lax.optimization_barrier(
                (quartered, rows, whole, riders[step])
            )
    return quartered, rows, whole, riders


def halo_rows(block, axis, width):
    count = lax.axis_size(axis)
    forward = [(i, i + 1) for i in range(count - 1)]
    backward = [(target, source) for source, target in forward]
    low = lax.ppermute(lax.slice_in_dim(block, block.shape[0] - width, None, axis=0), axis, forward)
    high = lax.ppermute(lax.slice_in_dim(block, 0, width, axis=0), axis, backward)
    return low, high


def gelu_value(inputs):
    tangent = jnp.tanh(ROOT_TWO_PI * (inputs + CUBIC_TERM * inputs * inputs * inputs))
    return 0.5 * inputs * (1.0 + tangent)


def gelu_slope(inputs):
    tangent = jnp.tanh(ROOT_TWO_PI * (inputs + CUBIC_TERM * inputs * inputs * inputs))
    return 0.5 * (1.0 + tangent) + 0.5 * inputs * (1.0 - tangent * tangent) * ROOT_TWO_PI * (
        1.0 + 3.0 * CUBIC_TERM * inputs * inputs
    )


def depthwise(padded, kernel, image_rows, image_cols):
    total = jnp.zeros((image_rows, image_cols, kernel.shape[-1]), jnp.float32)
    for row_tap in range(KERNEL):
        for col_tap in range(KERNEL):
            total = (
                total
                + padded[row_tap : row_tap + image_rows, col_tap : col_tap + image_cols]
                * kernel[row_tap, col_tap]
            )
    return total


def kernel_terms(padded, grads, image_rows, image_cols):
    collected = []
    for row_tap in range(KERNEL):
        for col_tap in range(KERNEL):
            collected.append(
                jnp.sum(
                    padded[row_tap : row_tap + image_rows, col_tap : col_tap + image_cols] * grads,
                    axis=(0, 1),
                )
            )
    return jnp.stack(collected)


def shards(image, tissue, kernel, ln_gain, w_in, w_out, layer_scale, cotangent):
    half_width = KERNEL // 2
    image_rows, image_cols, channels = image.shape
    hidden = w_in.shape[1]
    span = TILE_COLS + 2 * half_width

    first_col = jnp.argmax(tissue.reshape(-1)).astype(jnp.int32) * TILE_COLS
    extended = padded_2(image, (("row", 0),), half_width)
    padded = jnp.pad(extended, ((0, 0), (half_width, half_width), (0, 0)))
    window = lax.dynamic_slice_in_dim(padded, first_col, span, axis=1).astype(jnp.float32)
    filtered = depthwise(window, kernel, image_rows, TILE_COLS)
    centre = jnp.mean(filtered, axis=-1, keepdims=True)
    centered = filtered - centre
    inv_std = lax.rsqrt(jnp.mean(centered * centered, axis=-1, keepdims=True) + EPSILON)
    standard = centered * inv_std
    normed = (standard * ln_gain).astype(jnp.bfloat16)
    upstream = lax.dynamic_slice_in_dim(cotangent, first_col, TILE_COLS, axis=1).astype(jnp.float32)
    grad_out = (1.0 * layer_scale * upstream).astype(jnp.bfloat16)

    normed_flat = normed.reshape(-1, channels)
    grad_flat = grad_out.reshape(-1, channels)
    pre_act = jnp.dot(normed_flat, w_in, preferred_element_type=jnp.float32)
    act_flat = gelu_value(pre_act).astype(jnp.bfloat16)
    branch = jnp.dot(act_flat, w_out, preferred_element_type=jnp.float32)
    grad_act = jnp.dot(grad_flat, w_out.T, preferred_element_type=jnp.float32)
    pre_flat = (grad_act * gelu_slope(pre_act)).astype(jnp.bfloat16)
    grad_norm = jnp.dot(pre_flat, w_in.T, preferred_element_type=jnp.float32)
    quarters = hidden // channels
    partial_in = jnp.stack(
        [
            lax.dot_general(
                normed_flat,
                pre_flat[:, q * channels : (q + 1) * channels],
                (((0,), (0,)), ((), ())),
                preferred_element_type=jnp.float32,
            )
            for q in range(quarters)
        ]
    )
    partial_out = lax.dot_general(
        act_flat, grad_flat, (((0,), (0,)), ((), ())), preferred_element_type=jnp.float32
    )
    branch = branch.reshape(image_rows, TILE_COLS, channels)
    grad_norm = grad_norm.reshape(image_rows, TILE_COLS, channels)
    image_tile = lax.dynamic_slice_in_dim(image, first_col, TILE_COLS, axis=1)
    out_tile = (image_tile.astype(jnp.float32) + 1.0 * layer_scale * branch).astype(jnp.bfloat16)
    block_out = lax.dynamic_update_slice_in_dim(image, out_tile, first_col, axis=1)
    scale_grad = jnp.sum(1.0 * branch * upstream, axis=(0, 1))
    gain_grad = jnp.sum(grad_norm * standard, axis=(0, 1))
    grad_std = grad_norm * ln_gain
    grad_tile = (
        inv_std
        * (
            grad_std
            - jnp.mean(grad_std, axis=-1, keepdims=True)
            - standard * jnp.mean(grad_std * standard, axis=-1, keepdims=True)
        )
    ).astype(jnp.bfloat16)
    kernel_grad = kernel_terms(window, grad_tile.astype(jnp.float32), image_rows, TILE_COLS)
    packed = jnp.concatenate([kernel_grad, gain_grad[None], scale_grad[None]], axis=0)
    grad_conv = lax.dynamic_update_slice_in_dim(
        jnp.zeros_like(image), grad_tile, first_col, axis=1
    )
    low, high = halo_rows(grad_conv, "row", half_width)
    owned_in, grad_w_out, small_grads, (conv_tile, (low, high)) = halving_reduce(
        partial_in, partial_out, packed, "row", [grad_tile, (low, high)]
    )
    grad_w_in = owned_in.transpose(1, 0, 2).reshape(-1, hidden)
    flipped = kernel[::-1, ::-1]
    tile_padded = jnp.pad(
        conv_tile.astype(jnp.float32),
        ((half_width, half_width), (2 * half_width, 2 * half_width), (0, 0)),
    )
    own = depthwise(tile_padded, flipped, image_rows, span)
    own_full = lax.dynamic_update_slice_in_dim(
        jnp.zeros((image_rows, image_cols + 2 * half_width, channels), jnp.float32),
        own,
        first_col,
        axis=1,
    )[:, half_width : half_width + image_cols]
    edge = ((0, 0), (half_width, half_width), (0, 0))
    low = jnp.pad(low.astype(jnp.float32), edge)
    high = jnp.pad(high.astype(jnp.float32), edge)
    halo_out = []
    for out_row in range(image_rows):
        total = jnp.zeros((image_cols, channels), jnp.float32)
        for row_tap in range(KERNEL):
            source = out_row + row_tap
            if source < half_width:
                line = low[source]
            elif source >= half_width + image_rows:
                line = high[source - half_width - image_rows]
            else:
                continue
            for col_tap in range(KERNEL):
                total = total + line[col_tap : col_tap + image_cols] * flipped[row_tap, col_tap]
        halo_out.append(total)
    conv_back = own_full + jnp.stack(halo_out)
    grad_image = (cotangent.astype(jnp.float32) + conv_back).astype(jnp.bfloat16)
    return (block_out, grad_image, grad_w_in, grad_w_out, small_grads)


def solution(mesh):
    placed = (
        P(("group", "row"), None, None),
        P(("group", "row"), None),
        P(),
        P(),
        P(),
        P(),
        P(),
        P(("group", "row"), None, None),
    )
    return jax.shard_map(
        shards,
        mesh=mesh,
        in_specs=placed,
        out_specs=(
            P(("group", "row"), None, None),
            P(("group", "row"), None, None),
            P(("group", "row"), None),
            P(("group", "row"), None),
            P("group", None),
        ),
        check_vma=False,
    )
```

```python
import jax
import jax.numpy as jnp
from jax import lax
from jax.sharding import PartitionSpec as P

KERNEL = 7
TILE_ROWS = 4
TILE_COLS = 128


EPSILON = 1e-06
ROOT_TWO_PI = 0.7978845608028654
CUBIC_TERM = 0.044715


def padded_2(block, sides, width):
    for axis, dim in sides:
        count = lax.axis_size(axis)
        forward = [(i, i + 1) for i in range(count - 1)]
        backward = [(target, source) for source, target in forward]
        low = lax.ppermute(
            lax.slice_in_dim(block, block.shape[dim] - width, None, axis=dim), axis, forward
        )
        high = lax.ppermute(lax.slice_in_dim(block, 0, width, axis=dim), axis, backward)
        block = jnp.concatenate([low, block, high], axis=dim)
    return block


def bit_reversed(values, count, steps, axis):
    shape = values.shape
    values = values.reshape(shape[:axis] + (2,) * steps + (shape[axis] // count,) + shape[axis + 1 :])
    order = (
        tuple(range(axis))
        + tuple(axis + steps - 1 - i for i in range(steps))
        + tuple(range(axis + steps, values.ndim))
    )
    return values.transpose(order).reshape(shape)


def split_pair(values):
    high = values.astype(jnp.bfloat16)
    low = (values - high.astype(jnp.float32)).astype(jnp.bfloat16)
    return high, low


def halving_reduce(quartered, rows, whole, axis):
    count = lax.axis_size(axis)
    steps = count.bit_length() - 1
    if (1 << steps) != count:
        return (
            lax.psum_scatter(quartered, axis, scatter_dimension=1, tiled=True),
            lax.psum_scatter(rows, axis, scatter_dimension=0, tiled=True),
            lax.psum(whole, axis),
        )
    me = lax.axis_index(axis)
    quartered = bit_reversed(quartered, count, steps, 1)
    rows = bit_reversed(rows, count, steps, 0)
    quarters, width = quartered.shape[0], quartered.shape[2]
    for step in range(steps):
        bit = (me >> step) & 1
        pairs = [(i, i ^ (1 << step)) for i in range(count)]
        half_q = quartered.shape[1] // 2
        half_r = rows.shape[0] // 2
        keep_q = lax.dynamic_slice_in_dim(quartered, bit * half_q, half_q, axis=1)
        give_q = lax.dynamic_slice_in_dim(quartered, (1 - bit) * half_q, half_q, axis=1)
        keep_r = lax.dynamic_slice_in_dim(rows, bit * half_r, half_r, axis=0)
        give_r = lax.dynamic_slice_in_dim(rows, (1 - bit) * half_r, half_r, axis=0)
        if step == 0:
            got_q, got_r, got_whole = lax.ppermute((give_q, give_r, whole), axis, pairs)
            whole = whole + got_whole
        else:
            high, low = split_pair(whole)
            sent = jnp.concatenate(
                [give_q.astype(jnp.bfloat16).reshape(-1, width), give_r.astype(jnp.bfloat16), high, low],
                axis=0,
            )
            got = lax.ppermute(sent, axis, pairs)
            cut_q = quarters * half_q
            cut_r = cut_q + half_r
            size = whole.shape[0]
            got_q = got[:cut_q].reshape(quarters, half_q, width)
            got_r = got[cut_q:cut_r]
            mine = high.astype(jnp.float32) + low.astype(jnp.float32)
            theirs = got[cut_r : cut_r + size].astype(jnp.float32) + got[cut_r + size :].astype(
                jnp.float32
            )
            whole = mine + theirs
        quartered = keep_q + got_q.astype(jnp.float32)
        rows = keep_r + got_r.astype(jnp.float32)
        quartered, rows, whole = lax.optimization_barrier((quartered, rows, whole))
    return quartered, rows, whole


def halo_rows(block, axis, width):
    count = lax.axis_size(axis)
    forward = [(i, i + 1) for i in range(count - 1)]
    backward = [(target, source) for source, target in forward]
    low = lax.ppermute(lax.slice_in_dim(block, block.shape[0] - width, None, axis=0), axis, forward)
    high = lax.ppermute(lax.slice_in_dim(block, 0, width, axis=0), axis, backward)
    return low, high


def row_taps(line_of, kernel, out_rows, out_cols):
    rows = []
    for out_row in range(out_rows):
        total = jnp.zeros((out_cols, kernel.shape[-1]), jnp.float32)
        for row_tap in range(KERNEL):
            line = line_of(out_row + row_tap)
            if line is None:
                continue
            for col_tap in range(KERNEL):
                total = total + line[col_tap : col_tap + out_cols] * kernel[row_tap, col_tap]
        rows.append(total)
    return jnp.stack(rows)


def gelu_value(inputs):
    tangent = jnp.tanh(ROOT_TWO_PI * (inputs + CUBIC_TERM * inputs * inputs * inputs))
    return 0.5 * inputs * (1.0 + tangent)


def gelu_slope(inputs):
    tangent = jnp.tanh(ROOT_TWO_PI * (inputs + CUBIC_TERM * inputs * inputs * inputs))
    return 0.5 * (1.0 + tangent) + 0.5 * inputs * (1.0 - tangent * tangent) * ROOT_TWO_PI * (
        1.0 + 3.0 * CUBIC_TERM * inputs * inputs
    )


def depthwise(padded, kernel, image_rows, image_cols):
    total = jnp.zeros((image_rows, image_cols, kernel.shape[-1]), jnp.float32)
    for row_tap in range(KERNEL):
        for col_tap in range(KERNEL):
            total = (
                total
                + padded[row_tap : row_tap + image_rows, col_tap : col_tap + image_cols]
                * kernel[row_tap, col_tap]
            )
    return total


def kernel_terms(padded, grads, image_rows, image_cols):
    collected = []
    for row_tap in range(KERNEL):
        for col_tap in range(KERNEL):
            collected.append(
                jnp.sum(
                    padded[row_tap : row_tap + image_rows, col_tap : col_tap + image_cols] * grads,
                    axis=(0, 1),
                )
            )
    return jnp.stack(collected)


def shards(image, tissue, kernel, ln_gain, w_in, w_out, layer_scale, cotangent):
    half_width = KERNEL // 2
    image_rows, image_cols, channels = image.shape
    hidden = w_in.shape[1]
    span = TILE_COLS + 2 * half_width

    first_col = jnp.argmax(tissue.reshape(-1)).astype(jnp.int32) * TILE_COLS
    image_low, image_high = halo_rows(image, "row", half_width)
    extended = jnp.concatenate([image_low, image, image_high], axis=0)
    padded = jnp.pad(extended, ((0, 0), (half_width, half_width), (0, 0)))
    window = lax.dynamic_slice_in_dim(padded, first_col, span, axis=1).astype(jnp.float32)
    own_window = lax.dynamic_slice_in_dim(
        jnp.pad(image, ((0, 0), (half_width, half_width), (0, 0))), first_col, span, axis=1
    ).astype(jnp.float32)
    low_window = lax.dynamic_slice_in_dim(
        jnp.pad(image_low, ((0, 0), (half_width, half_width), (0, 0))), first_col, span, axis=1
    ).astype(jnp.float32)
    high_window = lax.dynamic_slice_in_dim(
        jnp.pad(image_high, ((0, 0), (half_width, half_width), (0, 0))), first_col, span, axis=1
    ).astype(jnp.float32)
    own_part = row_taps(
        lambda source: own_window[source - half_width]
        if half_width <= source < half_width + image_rows
        else None,
        kernel,
        image_rows,
        TILE_COLS,
    )
    halo_part = row_taps(
        lambda source: low_window[source]
        if source < half_width
        else (high_window[source - half_width - image_rows] if source >= half_width + image_rows else None),
        kernel,
        image_rows,
        TILE_COLS,
    )
    filtered = own_part + halo_part
    centre = jnp.mean(filtered, axis=-1, keepdims=True)
    centered = filtered - centre
    inv_std = lax.rsqrt(jnp.mean(centered * centered, axis=-1, keepdims=True) + EPSILON)
    standard = centered * inv_std
    normed = (standard * ln_gain).astype(jnp.bfloat16)
    upstream = lax.dynamic_slice_in_dim(cotangent, first_col, TILE_COLS, axis=1).astype(jnp.float32)
    grad_out = (1.0 * layer_scale * upstream).astype(jnp.bfloat16)

    normed_flat = normed.reshape(-1, channels)
    grad_flat = grad_out.reshape(-1, channels)
    pre_act = jnp.dot(normed_flat, w_in, preferred_element_type=jnp.float32)
    act_flat = gelu_value(pre_act).astype(jnp.bfloat16)
    branch = jnp.dot(act_flat, w_out, preferred_element_type=jnp.float32)
    grad_act = jnp.dot(grad_flat, w_out.T, preferred_element_type=jnp.float32)
    pre_flat = (grad_act * gelu_slope(pre_act)).astype(jnp.bfloat16)
    grad_norm = jnp.dot(pre_flat, w_in.T, preferred_element_type=jnp.float32)
    quarters = hidden // channels
    partial_in = jnp.stack(
        [
            lax.dot_general(
                normed_flat,
                pre_flat[:, q * channels : (q + 1) * channels],
                (((0,), (0,)), ((), ())),
                preferred_element_type=jnp.float32,
            )
            for q in range(quarters)
        ]
    )
    partial_out = lax.dot_general(
        act_flat, grad_flat, (((0,), (0,)), ((), ())), preferred_element_type=jnp.float32
    )
    branch = branch.reshape(image_rows, TILE_COLS, channels)
    grad_norm = grad_norm.reshape(image_rows, TILE_COLS, channels)
    image_tile = lax.dynamic_slice_in_dim(image, first_col, TILE_COLS, axis=1)
    out_tile = (image_tile.astype(jnp.float32) + 1.0 * layer_scale * branch).astype(jnp.bfloat16)
    block_out = lax.dynamic_update_slice_in_dim(image, out_tile, first_col, axis=1)
    scale_grad = jnp.sum(1.0 * branch * upstream, axis=(0, 1))
    gain_grad = jnp.sum(grad_norm * standard, axis=(0, 1))
    grad_std = grad_norm * ln_gain
    grad_tile = (
        inv_std
        * (
            grad_std
            - jnp.mean(grad_std, axis=-1, keepdims=True)
            - standard * jnp.mean(grad_std * standard, axis=-1, keepdims=True)
        )
    ).astype(jnp.bfloat16)
    kernel_grad = kernel_terms(window, grad_tile.astype(jnp.float32), image_rows, TILE_COLS)
    packed = jnp.concatenate([kernel_grad, gain_grad[None], scale_grad[None]], axis=0)
    owned_in, grad_w_out, small_grads = halving_reduce(partial_in, partial_out, packed, "row")
    grad_w_in = owned_in.transpose(1, 0, 2).reshape(-1, hidden)
    flipped = kernel[::-1, ::-1]
    tile_padded = jnp.pad(
        grad_tile.astype(jnp.float32),
        ((half_width, half_width), (2 * half_width, 2 * half_width), (0, 0)),
    )
    own = depthwise(tile_padded, flipped, image_rows, span)
    own_full = lax.dynamic_update_slice_in_dim(
        jnp.zeros((image_rows, image_cols + 2 * half_width, channels), jnp.float32),
        own,
        first_col,
        axis=1,
    )[:, half_width : half_width + image_cols]
    grad_conv = lax.dynamic_update_slice_in_dim(
        jnp.zeros_like(image), grad_tile, first_col, axis=1
    )
    low, high = halo_rows(grad_conv, "row", half_width)
    edge = ((0, 0), (half_width, half_width), (0, 0))
    low = jnp.pad(low.astype(jnp.float32), edge)
    high = jnp.pad(high.astype(jnp.float32), edge)
    halo_out = []
    for out_row in range(image_rows):
        total = jnp.zeros((image_cols, channels), jnp.float32)
        for row_tap in range(KERNEL):
            source = out_row + row_tap
            if source < half_width:
                line = low[source]
            elif source >= half_width + image_rows:
                line = high[source - half_width - image_rows]
            else:
                continue
            for col_tap in range(KERNEL):
                total = total + line[col_tap : col_tap + image_cols] * flipped[row_tap, col_tap]
        halo_out.append(total)
    conv_back = own_full + jnp.stack(halo_out)
    grad_image = (cotangent.astype(jnp.float32) + conv_back).astype(jnp.bfloat16)
    return (block_out, grad_image, grad_w_in, grad_w_out, small_grads)


def solution(mesh):
    placed = (
        P(("group", "row"), None, None),
        P(("group", "row"), None),
        P(),
        P(),
        P(),
        P(),
        P(),
        P(("group", "row"), None, None),
    )
    return jax.shard_map(
        shards,
        mesh=mesh,
        in_specs=placed,
        out_specs=(
            P(("group", "row"), None, None),
            P(("group", "row"), None, None),
            P(("group", "row"), None),
            P(("group", "row"), None),
            P("group", None),
        ),
        check_vma=False,
    )
```

```python
import jax
import jax.numpy as jnp
from jax import lax
from jax.sharding import PartitionSpec as P

KERNEL = 7
TILE_ROWS = 4
TILE_COLS = 128


EPSILON = 1e-06
ROOT_TWO_PI = 0.7978845608028654
CUBIC_TERM = 0.044715


def padded_2(block, sides, width):
    for axis, dim in sides:
        count = lax.axis_size(axis)
        forward = [(i, i + 1) for i in range(count - 1)]
        backward = [(target, source) for source, target in forward]
        low = lax.ppermute(
            lax.slice_in_dim(block, block.shape[dim] - width, None, axis=dim), axis, forward
        )
        high = lax.ppermute(lax.slice_in_dim(block, 0, width, axis=dim), axis, backward)
        block = jnp.concatenate([low, block, high], axis=dim)
    return block


def bit_reversed(values, count, steps, axis):
    shape = values.shape
    values = values.reshape(shape[:axis] + (2,) * steps + (shape[axis] // count,) + shape[axis + 1 :])
    order = (
        tuple(range(axis))
        + tuple(axis + steps - 1 - i for i in range(steps))
        + tuple(range(axis + steps, values.ndim))
    )
    return values.transpose(order).reshape(shape)


def split_pair(values):
    high = values.astype(jnp.bfloat16)
    low = (values - high.astype(jnp.float32)).astype(jnp.bfloat16)
    return high, low


def halving_reduce(quartered, rows, whole, axis, rider):
    count = lax.axis_size(axis)
    steps = count.bit_length() - 1
    if (1 << steps) != count:
        return (
            lax.psum_scatter(quartered, axis, scatter_dimension=1, tiled=True),
            lax.psum_scatter(rows, axis, scatter_dimension=0, tiled=True),
            lax.psum(whole, axis),
            rider,
        )
    me = lax.axis_index(axis)
    quartered = bit_reversed(quartered, count, steps, 1)
    rows = bit_reversed(rows, count, steps, 0)
    quarters, width = quartered.shape[0], quartered.shape[2]
    for step in range(steps):
        bit = (me >> step) & 1
        pairs = [(i, i ^ (1 << step)) for i in range(count)]
        half_q = quartered.shape[1] // 2
        half_r = rows.shape[0] // 2
        keep_q = lax.dynamic_slice_in_dim(quartered, bit * half_q, half_q, axis=1)
        give_q = lax.dynamic_slice_in_dim(quartered, (1 - bit) * half_q, half_q, axis=1)
        keep_r = lax.dynamic_slice_in_dim(rows, bit * half_r, half_r, axis=0)
        give_r = lax.dynamic_slice_in_dim(rows, (1 - bit) * half_r, half_r, axis=0)
        if step == 0:
            got_q, got_r, got_whole = lax.ppermute((give_q, give_r, whole), axis, pairs)
            whole = whole + got_whole
        else:
            high, low = split_pair(whole)
            sent = jnp.concatenate(
                [give_q.astype(jnp.bfloat16).reshape(-1, width), give_r.astype(jnp.bfloat16), high, low],
                axis=0,
            )
            got = lax.ppermute(sent, axis, pairs)
            cut_q = quarters * half_q
            cut_r = cut_q + half_r
            size = whole.shape[0]
            got_q = got[:cut_q].reshape(quarters, half_q, width)
            got_r = got[cut_q:cut_r]
            mine = high.astype(jnp.float32) + low.astype(jnp.float32)
            theirs = got[cut_r : cut_r + size].astype(jnp.float32) + got[cut_r + size :].astype(
                jnp.float32
            )
            whole = mine + theirs
        quartered = keep_q + got_q.astype(jnp.float32)
        rows = keep_r + got_r.astype(jnp.float32)
        if step == 0:
            quartered, rows, whole, rider = lax.optimization_barrier((quartered, rows, whole, rider))
        else:
            quartered, rows, whole = lax.optimization_barrier((quartered, rows, whole))
    return quartered, rows, whole, rider


def halo_rows(block, axis, width):
    count = lax.axis_size(axis)
    forward = [(i, i + 1) for i in range(count - 1)]
    backward = [(target, source) for source, target in forward]
    low = lax.ppermute(lax.slice_in_dim(block, block.shape[0] - width, None, axis=0), axis, forward)
    high = lax.ppermute(lax.slice_in_dim(block, 0, width, axis=0), axis, backward)
    return low, high


def gelu_value(inputs):
    tangent = jnp.tanh(ROOT_TWO_PI * (inputs + CUBIC_TERM * inputs * inputs * inputs))
    return 0.5 * inputs * (1.0 + tangent)


def gelu_slope(inputs):
    tangent = jnp.tanh(ROOT_TWO_PI * (inputs + CUBIC_TERM * inputs * inputs * inputs))
    return 0.5 * (1.0 + tangent) + 0.5 * inputs * (1.0 - tangent * tangent) * ROOT_TWO_PI * (
        1.0 + 3.0 * CUBIC_TERM * inputs * inputs
    )


def depthwise(padded, kernel, image_rows, image_cols):
    total = jnp.zeros((image_rows, image_cols, kernel.shape[-1]), jnp.float32)
    for row_tap in range(KERNEL):
        for col_tap in range(KERNEL):
            total = (
                total
                + padded[row_tap : row_tap + image_rows, col_tap : col_tap + image_cols]
                * kernel[row_tap, col_tap]
            )
    return total


def kernel_terms(padded, grads, image_rows, image_cols):
    collected = []
    for row_tap in range(KERNEL):
        for col_tap in range(KERNEL):
            collected.append(
                jnp.sum(
                    padded[row_tap : row_tap + image_rows, col_tap : col_tap + image_cols] * grads,
                    axis=(0, 1),
                )
            )
    return jnp.stack(collected)


def shards(image, tissue, kernel, ln_gain, w_in, w_out, layer_scale, cotangent):
    half_width = KERNEL // 2
    image_rows, image_cols, channels = image.shape
    hidden = w_in.shape[1]
    span = TILE_COLS + 2 * half_width

    first_col = jnp.argmax(tissue.reshape(-1)).astype(jnp.int32) * TILE_COLS
    extended = padded_2(image, (("row", 0),), half_width)
    padded = jnp.pad(extended, ((0, 0), (half_width, half_width), (0, 0)))
    window = lax.dynamic_slice_in_dim(padded, first_col, span, axis=1).astype(jnp.float32)
    filtered = depthwise(window, kernel, image_rows, TILE_COLS)
    centre = jnp.mean(filtered, axis=-1, keepdims=True)
    centered = filtered - centre
    inv_std = lax.rsqrt(jnp.mean(centered * centered, axis=-1, keepdims=True) + EPSILON)
    standard = centered * inv_std
    normed = (standard * ln_gain).astype(jnp.bfloat16)
    upstream = lax.dynamic_slice_in_dim(cotangent, first_col, TILE_COLS, axis=1).astype(jnp.float32)
    grad_out = (1.0 * layer_scale * upstream).astype(jnp.bfloat16)

    normed_flat = normed.reshape(-1, channels)
    grad_flat = grad_out.reshape(-1, channels)
    pre_act = jnp.dot(normed_flat, w_in, preferred_element_type=jnp.float32)
    act_flat = gelu_value(pre_act).astype(jnp.bfloat16)
    branch = jnp.dot(act_flat, w_out, preferred_element_type=jnp.float32)
    grad_act = jnp.dot(grad_flat, w_out.T, preferred_element_type=jnp.float32)
    pre_flat = (grad_act * gelu_slope(pre_act)).astype(jnp.bfloat16)
    grad_norm = jnp.dot(pre_flat, w_in.T, preferred_element_type=jnp.float32)
    quarters = hidden // channels
    partial_in = jnp.stack(
        [
            lax.dot_general(
                normed_flat,
                pre_flat[:, q * channels : (q + 1) * channels],
                (((0,), (0,)), ((), ())),
                preferred_element_type=jnp.float32,
            )
            for q in range(quarters)
        ]
    )
    partial_out = lax.dot_general(
        act_flat, grad_flat, (((0,), (0,)), ((), ())), preferred_element_type=jnp.float32
    )
    branch = branch.reshape(image_rows, TILE_COLS, channels)
    grad_norm = grad_norm.reshape(image_rows, TILE_COLS, channels)
    image_tile = lax.dynamic_slice_in_dim(image, first_col, TILE_COLS, axis=1)
    out_tile = (image_tile.astype(jnp.float32) + 1.0 * layer_scale * branch).astype(jnp.bfloat16)
    block_out = lax.dynamic_update_slice_in_dim(image, out_tile, first_col, axis=1)
    scale_grad = jnp.sum(1.0 * branch * upstream, axis=(0, 1))
    gain_grad = jnp.sum(grad_norm * standard, axis=(0, 1))
    grad_std = grad_norm * ln_gain
    grad_tile = (
        inv_std
        * (
            grad_std
            - jnp.mean(grad_std, axis=-1, keepdims=True)
            - standard * jnp.mean(grad_std * standard, axis=-1, keepdims=True)
        )
    ).astype(jnp.bfloat16)
    kernel_grad = kernel_terms(window, grad_tile.astype(jnp.float32), image_rows, TILE_COLS)
    packed = jnp.concatenate([kernel_grad, gain_grad[None], scale_grad[None]], axis=0)
    owned_in, grad_w_out, small_grads, flipped = halving_reduce(
        partial_in, partial_out, packed, "row", kernel[::-1, ::-1]
    )
    grad_w_in = owned_in.transpose(1, 0, 2).reshape(-1, hidden)
    tile_padded = jnp.pad(
        grad_tile.astype(jnp.float32),
        ((half_width, half_width), (2 * half_width, 2 * half_width), (0, 0)),
    )
    own = depthwise(tile_padded, flipped, image_rows, span)
    own_full = lax.dynamic_update_slice_in_dim(
        jnp.zeros((image_rows, image_cols + 2 * half_width, channels), jnp.float32),
        own,
        first_col,
        axis=1,
    )[:, half_width : half_width + image_cols]
    grad_conv = lax.dynamic_update_slice_in_dim(
        jnp.zeros_like(image), grad_tile, first_col, axis=1
    )
    low, high = halo_rows(grad_conv, "row", half_width)
    edge = ((0, 0), (half_width, half_width), (0, 0))
    low = jnp.pad(low.astype(jnp.float32), edge)
    high = jnp.pad(high.astype(jnp.float32), edge)
    halo_out = []
    for out_row in range(image_rows):
        total = jnp.zeros((image_cols, channels), jnp.float32)
        for row_tap in range(KERNEL):
            source = out_row + row_tap
            if source < half_width:
                line = low[source]
            elif source >= half_width + image_rows:
                line = high[source - half_width - image_rows]
            else:
                continue
            for col_tap in range(KERNEL):
                total = total + line[col_tap : col_tap + image_cols] * flipped[row_tap, col_tap]
        halo_out.append(total)
    conv_back = own_full + jnp.stack(halo_out)
    grad_image = (cotangent.astype(jnp.float32) + conv_back).astype(jnp.bfloat16)
    return (block_out, grad_image, grad_w_in, grad_w_out, small_grads)


def solution(mesh):
    placed = (
        P(("group", "row"), None, None),
        P(("group", "row"), None),
        P(),
        P(),
        P(),
        P(),
        P(),
        P(("group", "row"), None, None),
    )
    return jax.shard_map(
        shards,
        mesh=mesh,
        in_specs=placed,
        out_specs=(
            P(("group", "row"), None, None),
            P(("group", "row"), None, None),
            P(("group", "row"), None),
            P(("group", "row"), None),
            P("group", None),
        ),
        check_vma=False,
    )
```

```python
import jax
import jax.numpy as jnp
from jax import lax
from jax.sharding import PartitionSpec as P

KERNEL = 7
TILE_ROWS = 4
TILE_COLS = 128


EPSILON = 1e-06
ROOT_TWO_PI = 0.7978845608028654
CUBIC_TERM = 0.044715


def padded_2(block, sides, width):
    for axis, dim in sides:
        count = lax.axis_size(axis)
        forward = [(i, i + 1) for i in range(count - 1)]
        backward = [(target, source) for source, target in forward]
        low = lax.ppermute(
            lax.slice_in_dim(block, block.shape[dim] - width, None, axis=dim), axis, forward
        )
        high = lax.ppermute(lax.slice_in_dim(block, 0, width, axis=dim), axis, backward)
        block = jnp.concatenate([low, block, high], axis=dim)
    return block


def bit_reversed(values, count, steps, axis):
    shape = values.shape
    values = values.reshape(shape[:axis] + (2,) * steps + (shape[axis] // count,) + shape[axis + 1 :])
    order = (
        tuple(range(axis))
        + tuple(axis + steps - 1 - i for i in range(steps))
        + tuple(range(axis + steps, values.ndim))
    )
    return values.transpose(order).reshape(shape)


def split_pair(values):
    high = values.astype(jnp.bfloat16)
    low = (values - high.astype(jnp.float32)).astype(jnp.bfloat16)
    return high, low


def halving_reduce(quartered, rows, whole, axis):
    count = lax.axis_size(axis)
    steps = count.bit_length() - 1
    if (1 << steps) != count:
        return (
            lax.psum_scatter(quartered, axis, scatter_dimension=1, tiled=True),
            lax.psum_scatter(rows, axis, scatter_dimension=0, tiled=True),
            lax.psum(whole, axis),
        )
    me = lax.axis_index(axis)
    quartered = bit_reversed(quartered, count, steps, 1)
    rows = bit_reversed(rows, count, steps, 0)
    quarters, width = quartered.shape[0], quartered.shape[2]
    for step in range(steps):
        bit = (me >> step) & 1
        pairs = [(i, i ^ (1 << step)) for i in range(count)]
        half_q = quartered.shape[1] // 2
        half_r = rows.shape[0] // 2
        keep_q = lax.dynamic_slice_in_dim(quartered, bit * half_q, half_q, axis=1)
        give_q = lax.dynamic_slice_in_dim(quartered, (1 - bit) * half_q, half_q, axis=1)
        keep_r = lax.dynamic_slice_in_dim(rows, bit * half_r, half_r, axis=0)
        give_r = lax.dynamic_slice_in_dim(rows, (1 - bit) * half_r, half_r, axis=0)
        if step == 0:
            got_q, got_r, got_whole = lax.ppermute((give_q, give_r, whole), axis, pairs)
            whole = whole + got_whole
        else:
            high, low = split_pair(whole)
            sent = jnp.concatenate(
                [give_q.astype(jnp.bfloat16).reshape(-1, width), give_r.astype(jnp.bfloat16), high, low],
                axis=0,
            )
            got = lax.ppermute(sent, axis, pairs)
            cut_q = quarters * half_q
            cut_r = cut_q + half_r
            size = whole.shape[0]
            got_q = got[:cut_q].reshape(quarters, half_q, width)
            got_r = got[cut_q:cut_r]
            mine = high.astype(jnp.float32) + low.astype(jnp.float32)
            theirs = got[cut_r : cut_r + size].astype(jnp.float32) + got[cut_r + size :].astype(
                jnp.float32
            )
            whole = mine + theirs
        quartered = keep_q + got_q.astype(jnp.float32)
        rows = keep_r + got_r.astype(jnp.float32)
        quartered, rows, whole = lax.optimization_barrier((quartered, rows, whole))
    return quartered, rows, whole


def halo_rows(block, axis, width):
    count = lax.axis_size(axis)
    forward = [(i, i + 1) for i in range(count - 1)]
    backward = [(target, source) for source, target in forward]
    low = lax.ppermute(lax.slice_in_dim(block, block.shape[0] - width, None, axis=0), axis, forward)
    high = lax.ppermute(lax.slice_in_dim(block, 0, width, axis=0), axis, backward)
    return low, high


def gelu_value(inputs):
    tangent = jnp.tanh(ROOT_TWO_PI * (inputs + CUBIC_TERM * inputs * inputs * inputs))
    return 0.5 * inputs * (1.0 + tangent)


def gelu_slope(inputs):
    tangent = jnp.tanh(ROOT_TWO_PI * (inputs + CUBIC_TERM * inputs * inputs * inputs))
    return 0.5 * (1.0 + tangent) + 0.5 * inputs * (1.0 - tangent * tangent) * ROOT_TWO_PI * (
        1.0 + 3.0 * CUBIC_TERM * inputs * inputs
    )


def depthwise(padded, kernel, image_rows, image_cols):
    total = jnp.zeros((image_rows, image_cols, kernel.shape[-1]), jnp.float32)
    for row_tap in range(KERNEL):
        for col_tap in range(KERNEL):
            total = (
                total
                + padded[row_tap : row_tap + image_rows, col_tap : col_tap + image_cols]
                * kernel[row_tap, col_tap]
            )
    return total


def kernel_terms(padded, grads, image_rows, image_cols):
    collected = []
    for row_tap in range(KERNEL):
        for col_tap in range(KERNEL):
            collected.append(
                jnp.sum(
                    padded[row_tap : row_tap + image_rows, col_tap : col_tap + image_cols] * grads,
                    axis=(0, 1),
                )
            )
    return jnp.stack(collected)


def shards(image, tissue, kernel, ln_gain, w_in, w_out, layer_scale, cotangent):
    half_width = KERNEL // 2
    image_rows, image_cols, channels = image.shape
    hidden = w_in.shape[1]
    span = TILE_COLS + 2 * half_width

    first_col = jnp.argmax(tissue.reshape(-1)).astype(jnp.int32) * TILE_COLS
    extended = padded_2(image, (("row", 0),), half_width)
    padded = jnp.pad(extended, ((0, 0), (half_width, half_width), (0, 0)))
    window = lax.dynamic_slice_in_dim(padded, first_col, span, axis=1).astype(jnp.float32)
    filtered = depthwise(window, kernel, image_rows, TILE_COLS)
    centre = jnp.mean(filtered, axis=-1, keepdims=True)
    centered = filtered - centre
    inv_std = lax.rsqrt(jnp.mean(centered * centered, axis=-1, keepdims=True) + EPSILON)
    standard = centered * inv_std
    normed = (standard * ln_gain).astype(jnp.bfloat16)
    upstream = lax.dynamic_slice_in_dim(cotangent, first_col, TILE_COLS, axis=1).astype(jnp.float32)
    grad_out = (1.0 * layer_scale * upstream).astype(jnp.bfloat16)

    normed_flat = normed.reshape(-1, channels)
    grad_flat = grad_out.reshape(-1, channels)
    pre_act = jnp.dot(normed_flat, w_in, preferred_element_type=jnp.float32)
    act_flat = gelu_value(pre_act).astype(jnp.bfloat16)
    branch = jnp.dot(act_flat, w_out, preferred_element_type=jnp.float32)
    grad_act = jnp.dot(grad_flat, w_out.T, preferred_element_type=jnp.float32)
    pre_flat = (grad_act * gelu_slope(pre_act)).astype(jnp.bfloat16)
    grad_norm = jnp.dot(pre_flat, w_in.T, preferred_element_type=jnp.float32)
    quarters = hidden // channels
    partial_in = jnp.stack(
        [
            lax.dot_general(
                normed_flat,
                pre_flat[:, q * channels : (q + 1) * channels],
                (((0,), (0,)), ((), ())),
                preferred_element_type=jnp.float32,
            )
            for q in range(quarters)
        ]
    )
    partial_out = lax.dot_general(
        act_flat, grad_flat, (((0,), (0,)), ((), ())), preferred_element_type=jnp.float32
    )
    branch = branch.reshape(image_rows, TILE_COLS, channels)
    grad_norm = grad_norm.reshape(image_rows, TILE_COLS, channels)
    image_tile = lax.dynamic_slice_in_dim(image, first_col, TILE_COLS, axis=1)
    out_tile = (image_tile.astype(jnp.float32) + 1.0 * layer_scale * branch).astype(jnp.bfloat16)
    block_out = lax.dynamic_update_slice_in_dim(image, out_tile, first_col, axis=1)
    scale_grad = jnp.sum(1.0 * branch * upstream, axis=(0, 1))
    gain_grad = jnp.sum(grad_norm * standard, axis=(0, 1))
    grad_std = grad_norm * ln_gain
    grad_tile = (
        inv_std
        * (
            grad_std
            - jnp.mean(grad_std, axis=-1, keepdims=True)
            - standard * jnp.mean(grad_std * standard, axis=-1, keepdims=True)
        )
    ).astype(jnp.bfloat16)
    kernel_grad = kernel_terms(window, grad_tile.astype(jnp.float32), image_rows, TILE_COLS)
    packed = jnp.concatenate([kernel_grad, gain_grad[None], scale_grad[None]], axis=0)
    owned_in, grad_w_out, small_grads = halving_reduce(partial_in, partial_out, packed, "row")
    grad_w_in = owned_in.transpose(1, 0, 2).reshape(-1, hidden)
    flipped = kernel[::-1, ::-1]
    tile_padded = jnp.pad(
        grad_tile.astype(jnp.float32),
        ((half_width, half_width), (2 * half_width, 2 * half_width), (0, 0)),
    )
    own = depthwise(tile_padded, flipped, image_rows, span)
    tile_index = first_col // TILE_COLS
    own_full = jnp.zeros((image_rows, image_cols, channels), jnp.float32)
    for tile in range(image_cols // TILE_COLS):
        left = tile * TILE_COLS - half_width
        lo, hi = max(left, 0), min(left + span, image_cols)
        placed = jnp.pad(own[:, lo - left : hi - left], ((0, 0), (lo, image_cols - hi), (0, 0)))
        own_full = jnp.where(tile_index == tile, placed, own_full)
    grad_conv = lax.dynamic_update_slice_in_dim(
        jnp.zeros_like(image), grad_tile, first_col, axis=1
    )
    low, high = halo_rows(grad_conv, "row", half_width)
    edge = ((0, 0), (half_width, half_width), (0, 0))
    low = jnp.pad(low, edge)
    high = jnp.pad(high, edge)
    halo_out = []
    for out_row in range(image_rows):
        total = jnp.zeros((image_cols, channels), jnp.float32)
        for row_tap in range(KERNEL):
            source = out_row + row_tap
            if source < half_width:
                line = low[source]
            elif source >= half_width + image_rows:
                line = high[source - half_width - image_rows]
            else:
                continue
            for col_tap in range(KERNEL):
                total = total + line[col_tap : col_tap + image_cols] * flipped[row_tap, col_tap]
        halo_out.append(total)
    conv_back = own_full + jnp.stack(halo_out)
    grad_image = (cotangent.astype(jnp.float32) + conv_back).astype(jnp.bfloat16)
    return (block_out, grad_image, grad_w_in, grad_w_out, small_grads)


def solution(mesh):
    placed = (
        P(("group", "row"), None, None),
        P(("group", "row"), None),
        P(),
        P(),
        P(),
        P(),
        P(),
        P(("group", "row"), None, None),
    )
    return jax.shard_map(
        shards,
        mesh=mesh,
        in_specs=placed,
        out_specs=(
            P(("group", "row"), None, None),
            P(("group", "row"), None, None),
            P(("group", "row"), None),
            P(("group", "row"), None),
            P("group", None),
        ),
        check_vma=False,
    )
```

```python
import jax
import jax.numpy as jnp
from jax import lax
from jax.sharding import PartitionSpec as P

KERNEL = 7
TILE_ROWS = 4
TILE_COLS = 128


EPSILON = 1e-06
ROOT_TWO_PI = 0.7978845608028654
CUBIC_TERM = 0.044715


def padded_2(block, sides, width):
    for axis, dim in sides:
        count = lax.axis_size(axis)
        forward = [(i, i + 1) for i in range(count - 1)]
        backward = [(target, source) for source, target in forward]
        low = lax.ppermute(
            lax.slice_in_dim(block, block.shape[dim] - width, None, axis=dim), axis, forward
        )
        high = lax.ppermute(lax.slice_in_dim(block, 0, width, axis=dim), axis, backward)
        block = jnp.concatenate([low, block, high], axis=dim)
    return block


def bit_reversed(values, count, steps, axis):
    shape = values.shape
    values = values.reshape(shape[:axis] + (2,) * steps + (shape[axis] // count,) + shape[axis + 1 :])
    order = (
        tuple(range(axis))
        + tuple(axis + steps - 1 - i for i in range(steps))
        + tuple(range(axis + steps, values.ndim))
    )
    return values.transpose(order).reshape(shape)


def split_pair(values):
    high = values.astype(jnp.bfloat16)
    low = (values - high.astype(jnp.float32)).astype(jnp.bfloat16)
    return high, low


def halving_reduce(quartered, rows, whole, axis):
    count = lax.axis_size(axis)
    steps = count.bit_length() - 1
    if (1 << steps) != count:
        return (
            lax.psum_scatter(quartered, axis, scatter_dimension=1, tiled=True),
            lax.psum_scatter(rows, axis, scatter_dimension=0, tiled=True),
            lax.psum(whole, axis),
        )
    me = lax.axis_index(axis)
    quartered = bit_reversed(quartered, count, steps, 1)
    rows = bit_reversed(rows, count, steps, 0)
    quarters, width = quartered.shape[0], quartered.shape[2]
    for step in range(steps):
        bit = (me >> step) & 1
        pairs = [(i, i ^ (1 << step)) for i in range(count)]
        half_q = quartered.shape[1] // 2
        half_r = rows.shape[0] // 2
        keep_q = lax.dynamic_slice_in_dim(quartered, bit * half_q, half_q, axis=1)
        give_q = lax.dynamic_slice_in_dim(quartered, (1 - bit) * half_q, half_q, axis=1)
        keep_r = lax.dynamic_slice_in_dim(rows, bit * half_r, half_r, axis=0)
        give_r = lax.dynamic_slice_in_dim(rows, (1 - bit) * half_r, half_r, axis=0)
        if step == 0:
            got_q, got_r, got_whole = lax.ppermute((give_q, give_r, whole), axis, pairs)
            whole = whole + got_whole
        else:
            high, low = split_pair(whole)
            sent = jnp.concatenate(
                [give_q.astype(jnp.bfloat16).reshape(-1, width), give_r.astype(jnp.bfloat16), high, low],
                axis=0,
            )
            got = lax.ppermute(sent, axis, pairs)
            cut_q = quarters * half_q
            cut_r = cut_q + half_r
            size = whole.shape[0]
            got_q = got[:cut_q].reshape(quarters, half_q, width)
            got_r = got[cut_q:cut_r]
            mine = high.astype(jnp.float32) + low.astype(jnp.float32)
            theirs = got[cut_r : cut_r + size].astype(jnp.float32) + got[cut_r + size :].astype(
                jnp.float32
            )
            whole = mine + theirs
        quartered = keep_q + got_q.astype(jnp.float32)
        rows = keep_r + got_r.astype(jnp.float32)
        quartered, rows, whole = lax.optimization_barrier((quartered, rows, whole))
    return quartered, rows, whole


def halo_rows(block, axis, width):
    count = lax.axis_size(axis)
    forward = [(i, i + 1) for i in range(count - 1)]
    backward = [(target, source) for source, target in forward]
    low = lax.ppermute(lax.slice_in_dim(block, block.shape[0] - width, None, axis=0), axis, forward)
    high = lax.ppermute(lax.slice_in_dim(block, 0, width, axis=0), axis, backward)
    return low, high


def gelu_value(inputs):
    tangent = jnp.tanh(ROOT_TWO_PI * (inputs + CUBIC_TERM * inputs * inputs * inputs))
    return 0.5 * inputs * (1.0 + tangent)


def gelu_slope(inputs):
    tangent = jnp.tanh(ROOT_TWO_PI * (inputs + CUBIC_TERM * inputs * inputs * inputs))
    return 0.5 * (1.0 + tangent) + 0.5 * inputs * (1.0 - tangent * tangent) * ROOT_TWO_PI * (
        1.0 + 3.0 * CUBIC_TERM * inputs * inputs
    )


def depthwise(padded, kernel, image_rows, image_cols):
    total = jnp.zeros((image_rows, image_cols, kernel.shape[-1]), jnp.float32)
    for row_tap in range(KERNEL):
        for col_tap in range(KERNEL):
            total = (
                total
                + padded[row_tap : row_tap + image_rows, col_tap : col_tap + image_cols]
                * kernel[row_tap, col_tap]
            )
    return total


def kernel_terms(padded, grads, image_rows, image_cols):
    collected = []
    for row_tap in range(KERNEL):
        for col_tap in range(KERNEL):
            collected.append(
                jnp.sum(
                    padded[row_tap : row_tap + image_rows, col_tap : col_tap + image_cols] * grads,
                    axis=(0, 1),
                )
            )
    return jnp.stack(collected)


def shards(image, tissue, kernel, ln_gain, w_in, w_out, layer_scale, cotangent):
    half_width = KERNEL // 2
    image_rows, image_cols, channels = image.shape
    hidden = w_in.shape[1]
    span = TILE_COLS + 2 * half_width

    first_col = jnp.argmax(tissue.reshape(-1)).astype(jnp.int32) * TILE_COLS
    extended = padded_2(image, (("row", 0),), half_width)
    padded = jnp.pad(extended, ((0, 0), (half_width, half_width), (0, 0)))
    window = lax.dynamic_slice_in_dim(padded, first_col, span, axis=1).astype(jnp.float32)
    filtered = depthwise(window, kernel, image_rows, TILE_COLS)
    centre = jnp.mean(filtered, axis=-1, keepdims=True)
    centered = filtered - centre
    inv_std = lax.rsqrt(jnp.mean(centered * centered, axis=-1, keepdims=True) + EPSILON)
    standard = centered * inv_std
    normed = (standard * ln_gain).astype(jnp.bfloat16)
    upstream = lax.dynamic_slice_in_dim(cotangent, first_col, TILE_COLS, axis=1).astype(jnp.float32)
    grad_out = (1.0 * layer_scale * upstream).astype(jnp.bfloat16)

    normed_flat = normed.reshape(-1, channels)
    grad_flat = grad_out.reshape(-1, channels)
    pre_act = jnp.dot(normed_flat, w_in, preferred_element_type=jnp.float32)
    act_flat = gelu_value(pre_act).astype(jnp.bfloat16)
    branch = jnp.dot(act_flat, w_out, preferred_element_type=jnp.float32)
    grad_act = jnp.dot(grad_flat, w_out.T, preferred_element_type=jnp.float32)
    pre_flat = (grad_act * gelu_slope(pre_act)).astype(jnp.bfloat16)
    grad_norm = jnp.dot(pre_flat, w_in.T, preferred_element_type=jnp.float32)
    quarters = hidden // channels
    positions = pre_flat.shape[0]
    pre_quarters = pre_flat.reshape(positions, quarters, channels).transpose(1, 0, 2)
    normed_copies = jnp.broadcast_to(normed_flat[None], (quarters, positions, channels))
    partial_in = lax.dot_general(
        normed_copies,
        pre_quarters,
        (((1,), (1,)), ((0,), (0,))),
        preferred_element_type=jnp.float32,
    )
    partial_out = lax.dot_general(
        act_flat, grad_flat, (((0,), (0,)), ((), ())), preferred_element_type=jnp.float32
    )
    branch = branch.reshape(image_rows, TILE_COLS, channels)
    grad_norm = grad_norm.reshape(image_rows, TILE_COLS, channels)
    image_tile = lax.dynamic_slice_in_dim(image, first_col, TILE_COLS, axis=1)
    out_tile = (image_tile.astype(jnp.float32) + 1.0 * layer_scale * branch).astype(jnp.bfloat16)
    block_out = lax.dynamic_update_slice_in_dim(image, out_tile, first_col, axis=1)
    scale_grad = jnp.sum(1.0 * branch * upstream, axis=(0, 1))
    gain_grad = jnp.sum(grad_norm * standard, axis=(0, 1))
    grad_std = grad_norm * ln_gain
    grad_tile = (
        inv_std
        * (
            grad_std
            - jnp.mean(grad_std, axis=-1, keepdims=True)
            - standard * jnp.mean(grad_std * standard, axis=-1, keepdims=True)
        )
    ).astype(jnp.bfloat16)
    kernel_grad = kernel_terms(window, grad_tile.astype(jnp.float32), image_rows, TILE_COLS)
    packed = jnp.concatenate([kernel_grad, gain_grad[None], scale_grad[None]], axis=0)
    owned_in, grad_w_out, small_grads = halving_reduce(partial_in, partial_out, packed, "row")
    grad_w_in = owned_in.transpose(1, 0, 2).reshape(-1, hidden)
    flipped = kernel[::-1, ::-1]
    tile_padded = jnp.pad(
        grad_tile.astype(jnp.float32),
        ((half_width, half_width), (2 * half_width, 2 * half_width), (0, 0)),
    )
    own = depthwise(tile_padded, flipped, image_rows, span)
    tile_index = first_col // TILE_COLS
    own_full = jnp.zeros((image_rows, image_cols, channels), jnp.float32)
    for tile in range(image_cols // TILE_COLS):
        left = tile * TILE_COLS - half_width
        lo, hi = max(left, 0), min(left + span, image_cols)
        placed = jnp.pad(own[:, lo - left : hi - left], ((0, 0), (lo, image_cols - hi), (0, 0)))
        own_full = jnp.where(tile_index == tile, placed, own_full)
    grad_conv = lax.dynamic_update_slice_in_dim(
        jnp.zeros_like(image), grad_tile, first_col, axis=1
    )
    low, high = halo_rows(grad_conv, "row", half_width)
    edge = ((0, 0), (half_width, half_width), (0, 0))
    low = jnp.pad(low, edge)
    high = jnp.pad(high, edge)
    halo_out = []
    for out_row in range(image_rows):
        total = jnp.zeros((image_cols, channels), jnp.float32)
        for row_tap in range(KERNEL):
            source = out_row + row_tap
            if source < half_width:
                line = low[source]
            elif source >= half_width + image_rows:
                line = high[source - half_width - image_rows]
            else:
                continue
            for col_tap in range(KERNEL):
                total = total + line[col_tap : col_tap + image_cols] * flipped[row_tap, col_tap]
        halo_out.append(total)
    conv_back = own_full + jnp.stack(halo_out)
    grad_image = (cotangent.astype(jnp.float32) + conv_back).astype(jnp.bfloat16)
    return (block_out, grad_image, grad_w_in, grad_w_out, small_grads)


def solution(mesh):
    placed = (
        P(("group", "row"), None, None),
        P(("group", "row"), None),
        P(),
        P(),
        P(),
        P(),
        P(),
        P(("group", "row"), None, None),
    )
    return jax.shard_map(
        shards,
        mesh=mesh,
        in_specs=placed,
        out_specs=(
            P(("group", "row"), None, None),
            P(("group", "row"), None, None),
            P(("group", "row"), None),
            P(("group", "row"), None),
            P("group", None),
        ),
        check_vma=False,
    )
```

```python
import jax
import jax.numpy as jnp
from jax import lax
from jax.sharding import PartitionSpec as P

KERNEL = 7
TILE_ROWS = 4
TILE_COLS = 128


EPSILON = 1e-06
ROOT_TWO_PI = 0.7978845608028654
CUBIC_TERM = 0.044715


def padded_2(block, sides, width):
    for axis, dim in sides:
        count = lax.axis_size(axis)
        forward = [(i, i + 1) for i in range(count - 1)]
        backward = [(target, source) for source, target in forward]
        low = lax.ppermute(
            lax.slice_in_dim(block, block.shape[dim] - width, None, axis=dim), axis, forward
        )
        high = lax.ppermute(lax.slice_in_dim(block, 0, width, axis=dim), axis, backward)
        block = jnp.concatenate([low, block, high], axis=dim)
    return block


def bit_reversed(values, count, steps, axis):
    shape = values.shape
    values = values.reshape(shape[:axis] + (2,) * steps + (shape[axis] // count,) + shape[axis + 1 :])
    order = (
        tuple(range(axis))
        + tuple(axis + steps - 1 - i for i in range(steps))
        + tuple(range(axis + steps, values.ndim))
    )
    return values.transpose(order).reshape(shape)


def split_pair(values):
    high = values.astype(jnp.bfloat16)
    low = (values - high.astype(jnp.float32)).astype(jnp.bfloat16)
    return high, low


def halving_reduce(quartered, rows, whole, axis):
    count = lax.axis_size(axis)
    steps = count.bit_length() - 1
    if (1 << steps) != count:
        return (
            lax.psum_scatter(quartered, axis, scatter_dimension=1, tiled=True),
            lax.psum_scatter(rows, axis, scatter_dimension=0, tiled=True),
            lax.psum(whole, axis),
        )
    me = lax.axis_index(axis)
    quartered = bit_reversed(quartered, count, steps, 1)
    rows = bit_reversed(rows, count, steps, 0)
    quarters, width = quartered.shape[0], quartered.shape[2]
    for step in range(steps):
        bit = (me >> step) & 1
        pairs = [(i, i ^ (1 << step)) for i in range(count)]
        half_q = quartered.shape[1] // 2
        half_r = rows.shape[0] // 2
        keep_q = lax.dynamic_slice_in_dim(quartered, bit * half_q, half_q, axis=1)
        give_q = lax.dynamic_slice_in_dim(quartered, (1 - bit) * half_q, half_q, axis=1)
        keep_r = lax.dynamic_slice_in_dim(rows, bit * half_r, half_r, axis=0)
        give_r = lax.dynamic_slice_in_dim(rows, (1 - bit) * half_r, half_r, axis=0)
        if step == 0:
            got_q, got_r, got_whole = lax.ppermute((give_q, give_r, whole), axis, pairs)
            whole = whole + got_whole
        else:
            high, low = split_pair(whole)
            sent = jnp.concatenate(
                [give_q.astype(jnp.bfloat16).reshape(-1, width), give_r.astype(jnp.bfloat16), high, low],
                axis=0,
            )
            got = lax.ppermute(sent, axis, pairs)
            cut_q = quarters * half_q
            cut_r = cut_q + half_r
            size = whole.shape[0]
            got_q = got[:cut_q].reshape(quarters, half_q, width)
            got_r = got[cut_q:cut_r]
            mine = high.astype(jnp.float32) + low.astype(jnp.float32)
            theirs = got[cut_r : cut_r + size].astype(jnp.float32) + got[cut_r + size :].astype(
                jnp.float32
            )
            whole = mine + theirs
        quartered = keep_q + got_q.astype(jnp.float32)
        rows = keep_r + got_r.astype(jnp.float32)
        quartered, rows, whole = lax.optimization_barrier((quartered, rows, whole))
    return quartered, rows, whole


def halo_rows(block, axis, width):
    count = lax.axis_size(axis)
    forward = [(i, i + 1) for i in range(count - 1)]
    backward = [(target, source) for source, target in forward]
    low = lax.ppermute(lax.slice_in_dim(block, block.shape[0] - width, None, axis=0), axis, forward)
    high = lax.ppermute(lax.slice_in_dim(block, 0, width, axis=0), axis, backward)
    return low, high


def gelu_value(inputs):
    tangent = jnp.tanh(ROOT_TWO_PI * (inputs + CUBIC_TERM * inputs * inputs * inputs))
    return 0.5 * inputs * (1.0 + tangent)


def gelu_slope(inputs):
    tangent = jnp.tanh(ROOT_TWO_PI * (inputs + CUBIC_TERM * inputs * inputs * inputs))
    return 0.5 * (1.0 + tangent) + 0.5 * inputs * (1.0 - tangent * tangent) * ROOT_TWO_PI * (
        1.0 + 3.0 * CUBIC_TERM * inputs * inputs
    )


def depthwise(padded, kernel, image_rows, image_cols):
    total = jnp.zeros((image_rows, image_cols, kernel.shape[-1]), jnp.float32)
    for row_tap in range(KERNEL):
        for col_tap in range(KERNEL):
            total = (
                total
                + padded[row_tap : row_tap + image_rows, col_tap : col_tap + image_cols]
                * kernel[row_tap, col_tap]
            )
    return total


def kernel_terms(padded, grads, image_rows, image_cols):
    collected = []
    for row_tap in range(KERNEL):
        for col_tap in range(KERNEL):
            collected.append(
                jnp.sum(
                    padded[row_tap : row_tap + image_rows, col_tap : col_tap + image_cols] * grads,
                    axis=(0, 1),
                )
            )
    return jnp.stack(collected)


def shards(image, tissue, kernel, ln_gain, w_in, w_out, layer_scale, cotangent):
    half_width = KERNEL // 2
    image_rows, image_cols, channels = image.shape
    hidden = w_in.shape[1]
    span = TILE_COLS + 2 * half_width

    first_col = jnp.argmax(tissue.reshape(-1)).astype(jnp.int32) * TILE_COLS
    extended = padded_2(image, (("row", 0),), half_width)
    padded = jnp.pad(extended, ((0, 0), (half_width, half_width), (0, 0)))
    window = lax.dynamic_slice_in_dim(padded, first_col, span, axis=1).astype(jnp.float32)
    filtered = depthwise(window, kernel, image_rows, TILE_COLS)
    centre = jnp.mean(filtered, axis=-1, keepdims=True)
    centered = filtered - centre
    inv_std = lax.rsqrt(jnp.mean(centered * centered, axis=-1, keepdims=True) + EPSILON)
    standard = centered * inv_std
    normed = (standard * ln_gain).astype(jnp.bfloat16)
    upstream = lax.dynamic_slice_in_dim(cotangent, first_col, TILE_COLS, axis=1).astype(jnp.float32)
    grad_out = (1.0 * layer_scale * upstream).astype(jnp.bfloat16)

    normed_flat = normed.reshape(-1, channels)
    grad_flat = grad_out.reshape(-1, channels)
    pre_act = jnp.dot(normed_flat, w_in, preferred_element_type=jnp.float32)
    act_flat = gelu_value(pre_act).astype(jnp.bfloat16)
    branch = jnp.dot(act_flat, w_out, preferred_element_type=jnp.float32)
    grad_act = jnp.dot(grad_flat, w_out.T, preferred_element_type=jnp.float32)
    pre_flat = (grad_act * gelu_slope(pre_act)).astype(jnp.bfloat16)
    grad_norm = jnp.dot(pre_flat, w_in.T, preferred_element_type=jnp.float32)
    quarters = hidden // channels
    positions = pre_flat.shape[0]
    pre_quarters = pre_flat.reshape(positions, quarters, channels).transpose(1, 0, 2)
    normed_copies = jnp.broadcast_to(normed_flat[None], (quarters, positions, channels))
    partial_in = lax.dot_general(
        normed_copies,
        pre_quarters,
        (((1,), (1,)), ((0,), (0,))),
        preferred_element_type=jnp.float32,
    )
    partial_out = lax.dot_general(
        act_flat, grad_flat, (((0,), (0,)), ((), ())), preferred_element_type=jnp.float32
    )
    branch = branch.reshape(image_rows, TILE_COLS, channels)
    grad_norm = grad_norm.reshape(image_rows, TILE_COLS, channels)
    image_tile = lax.dynamic_slice_in_dim(image, first_col, TILE_COLS, axis=1)
    out_tile = (image_tile.astype(jnp.float32) + 1.0 * layer_scale * branch).astype(jnp.bfloat16)
    block_out = lax.dynamic_update_slice_in_dim(image, out_tile, first_col, axis=1)
    scale_grad = jnp.sum(1.0 * branch * upstream, axis=(0, 1))
    gain_grad = jnp.sum(grad_norm * standard, axis=(0, 1))
    grad_std = grad_norm * ln_gain
    grad_tile = (
        inv_std
        * (
            grad_std
            - jnp.mean(grad_std, axis=-1, keepdims=True)
            - standard * jnp.mean(grad_std * standard, axis=-1, keepdims=True)
        )
    ).astype(jnp.bfloat16)
    kernel_grad = kernel_terms(window, grad_tile.astype(jnp.float32), image_rows, TILE_COLS)
    packed = jnp.concatenate([kernel_grad, gain_grad[None], scale_grad[None]], axis=0)
    owned_in, grad_w_out, small_grads = halving_reduce(partial_in, partial_out, packed, "row")
    grad_w_in = owned_in.transpose(1, 0, 2).reshape(-1, hidden)
    flipped = kernel[::-1, ::-1]
    tile_padded = jnp.pad(
        grad_tile.astype(jnp.float32),
        ((half_width, half_width), (2 * half_width, 2 * half_width), (0, 0)),
    )
    own = depthwise(tile_padded, flipped, image_rows, span)
    own_full = lax.dynamic_update_slice_in_dim(
        jnp.zeros((image_rows, image_cols + 2 * half_width, channels), jnp.float32),
        own,
        first_col,
        axis=1,
    )[:, half_width : half_width + image_cols]
    grad_conv = lax.dynamic_update_slice_in_dim(
        jnp.zeros_like(image), grad_tile, first_col, axis=1
    )
    low, high = halo_rows(grad_conv, "row", half_width)
    edge = ((0, 0), (half_width, half_width), (0, 0))
    low = jnp.pad(low.astype(jnp.float32), edge)
    high = jnp.pad(high.astype(jnp.float32), edge)
    halo_out = []
    for out_row in range(image_rows):
        total = jnp.zeros((image_cols, channels), jnp.float32)
        for row_tap in range(KERNEL):
            source = out_row + row_tap
            if source < half_width:
                line = low[source]
            elif source >= half_width + image_rows:
                line = high[source - half_width - image_rows]
            else:
                continue
            for col_tap in range(KERNEL):
                total = total + line[col_tap : col_tap + image_cols] * flipped[row_tap, col_tap]
        halo_out.append(total)
    conv_back = own_full + jnp.stack(halo_out)
    grad_image = (cotangent.astype(jnp.float32) + conv_back).astype(jnp.bfloat16)
    return (block_out, grad_image, grad_w_in, grad_w_out, small_grads)


def solution(mesh):
    placed = (
        P(("group", "row"), None, None),
        P(("group", "row"), None),
        P(),
        P(),
        P(),
        P(),
        P(),
        P(("group", "row"), None, None),
    )
    return jax.shard_map(
        shards,
        mesh=mesh,
        in_specs=placed,
        out_specs=(
            P(("group", "row"), None, None),
            P(("group", "row"), None, None),
            P(("group", "row"), None),
            P(("group", "row"), None),
            P("group", None),
        ),
        check_vma=False,
    )
```

```python
import jax
import jax.numpy as jnp
from jax import lax
from jax.sharding import PartitionSpec as P

KERNEL = 7
TILE_ROWS = 4
TILE_COLS = 128


EPSILON = 1e-06
ROOT_TWO_PI = 0.7978845608028654
CUBIC_TERM = 0.044715


def padded_2(block, sides, width):
    for axis, dim in sides:
        count = lax.axis_size(axis)
        forward = [(i, i + 1) for i in range(count - 1)]
        backward = [(target, source) for source, target in forward]
        low = lax.ppermute(
            lax.slice_in_dim(block, block.shape[dim] - width, None, axis=dim), axis, forward
        )
        high = lax.ppermute(lax.slice_in_dim(block, 0, width, axis=dim), axis, backward)
        block = jnp.concatenate([low, block, high], axis=dim)
    return block


def bit_reversed(values, count, steps, axis):
    shape = values.shape
    values = values.reshape(shape[:axis] + (2,) * steps + (shape[axis] // count,) + shape[axis + 1 :])
    order = (
        tuple(range(axis))
        + tuple(axis + steps - 1 - i for i in range(steps))
        + tuple(range(axis + steps, values.ndim))
    )
    return values.transpose(order).reshape(shape)


def split_pair(values):
    high = values.astype(jnp.bfloat16)
    low = (values - high.astype(jnp.float32)).astype(jnp.bfloat16)
    return high, low


def halving_reduce(quartered, rows, whole, axis):
    count = lax.axis_size(axis)
    steps = count.bit_length() - 1
    if (1 << steps) != count:
        return (
            lax.psum_scatter(quartered, axis, scatter_dimension=1, tiled=True),
            lax.psum_scatter(rows, axis, scatter_dimension=0, tiled=True),
            lax.psum(whole, axis),
        )
    me = lax.axis_index(axis)
    quartered = bit_reversed(quartered, count, steps, 1)
    rows = bit_reversed(rows, count, steps, 0)
    quarters, width = quartered.shape[0], quartered.shape[2]
    for step in range(steps):
        bit = (me >> step) & 1
        pairs = [(i, i ^ (1 << step)) for i in range(count)]
        half_q = quartered.shape[1] // 2
        half_r = rows.shape[0] // 2
        keep_q = lax.dynamic_slice_in_dim(quartered, bit * half_q, half_q, axis=1)
        give_q = lax.dynamic_slice_in_dim(quartered, (1 - bit) * half_q, half_q, axis=1)
        keep_r = lax.dynamic_slice_in_dim(rows, bit * half_r, half_r, axis=0)
        give_r = lax.dynamic_slice_in_dim(rows, (1 - bit) * half_r, half_r, axis=0)
        if step == 0:
            got_q, got_r, got_whole = lax.ppermute((give_q, give_r, whole), axis, pairs)
            whole = whole + got_whole
        else:
            high, low = split_pair(whole)
            sent = jnp.concatenate(
                [give_q.astype(jnp.bfloat16).reshape(-1, width), give_r.astype(jnp.bfloat16), high, low],
                axis=0,
            )
            got = lax.ppermute(sent, axis, pairs)
            cut_q = quarters * half_q
            cut_r = cut_q + half_r
            size = whole.shape[0]
            got_q = got[:cut_q].reshape(quarters, half_q, width)
            got_r = got[cut_q:cut_r]
            mine = high.astype(jnp.float32) + low.astype(jnp.float32)
            theirs = got[cut_r : cut_r + size].astype(jnp.float32) + got[cut_r + size :].astype(
                jnp.float32
            )
            whole = mine + theirs
        quartered = keep_q + got_q.astype(jnp.float32)
        rows = keep_r + got_r.astype(jnp.float32)
        quartered, rows, whole = lax.optimization_barrier((quartered, rows, whole))
    return quartered, rows, whole


def halo_rows(block, axis, width):
    count = lax.axis_size(axis)
    forward = [(i, i + 1) for i in range(count - 1)]
    backward = [(target, source) for source, target in forward]
    low = lax.ppermute(lax.slice_in_dim(block, block.shape[0] - width, None, axis=0), axis, forward)
    high = lax.ppermute(lax.slice_in_dim(block, 0, width, axis=0), axis, backward)
    return low, high


def gelu_value(inputs):
    tangent = jnp.tanh(ROOT_TWO_PI * (inputs + CUBIC_TERM * inputs * inputs * inputs))
    return 0.5 * inputs * (1.0 + tangent)


def gelu_slope(inputs):
    tangent = jnp.tanh(ROOT_TWO_PI * (inputs + CUBIC_TERM * inputs * inputs * inputs))
    return 0.5 * (1.0 + tangent) + 0.5 * inputs * (1.0 - tangent * tangent) * ROOT_TWO_PI * (
        1.0 + 3.0 * CUBIC_TERM * inputs * inputs
    )


def depthwise(padded, kernel, image_rows, image_cols):
    total = jnp.zeros((image_rows, image_cols, kernel.shape[-1]), jnp.float32)
    for row_tap in range(KERNEL):
        for col_tap in range(KERNEL):
            total = (
                total
                + padded[row_tap : row_tap + image_rows, col_tap : col_tap + image_cols]
                * kernel[row_tap, col_tap]
            )
    return total


def kernel_terms(padded, grads, image_rows, image_cols):
    collected = []
    for row_tap in range(KERNEL):
        for col_tap in range(KERNEL):
            collected.append(
                jnp.sum(
                    padded[row_tap : row_tap + image_rows, col_tap : col_tap + image_cols] * grads,
                    axis=(0, 1),
                )
            )
    return jnp.stack(collected)


def shards(image, tissue, kernel, ln_gain, w_in, w_out, layer_scale, cotangent):
    half_width = KERNEL // 2
    image_rows, image_cols, channels = image.shape
    hidden = w_in.shape[1]
    span = TILE_COLS + 2 * half_width

    first_col = jnp.argmax(tissue.reshape(-1)).astype(jnp.int32) * TILE_COLS
    extended = padded_2(image, (("row", 0),), half_width)
    padded = jnp.pad(extended, ((0, 0), (half_width, half_width), (0, 0)))
    window = lax.dynamic_slice_in_dim(padded, first_col, span, axis=1).astype(jnp.float32)
    filtered = depthwise(window, kernel, image_rows, TILE_COLS)
    centre = jnp.mean(filtered, axis=-1, keepdims=True)
    centered = filtered - centre
    inv_std = lax.rsqrt(jnp.mean(centered * centered, axis=-1, keepdims=True) + EPSILON)
    standard = centered * inv_std
    normed = (standard * ln_gain).astype(jnp.bfloat16)
    upstream = lax.dynamic_slice_in_dim(cotangent, first_col, TILE_COLS, axis=1).astype(jnp.float32)
    grad_out = (1.0 * layer_scale * upstream).astype(jnp.bfloat16)

    normed_flat = normed.reshape(-1, channels)
    grad_flat = grad_out.reshape(-1, channels)
    pre_act = jnp.dot(normed_flat, w_in, preferred_element_type=jnp.float32)
    act_flat = gelu_value(pre_act).astype(jnp.bfloat16)
    branch = jnp.dot(act_flat, w_out, preferred_element_type=jnp.float32)
    grad_act = jnp.dot(grad_flat, w_out.T, preferred_element_type=jnp.float32)
    pre_flat = (grad_act * gelu_slope(pre_act)).astype(jnp.bfloat16)
    grad_norm = jnp.dot(pre_flat, w_in.T, preferred_element_type=jnp.float32)
    quarters = hidden // channels
    positions = pre_flat.shape[0]
    pre_quarters = pre_flat.reshape(positions, quarters, channels).transpose(1, 0, 2)
    normed_copies = jnp.broadcast_to(normed_flat[None], (quarters, positions, channels))
    partial_in = lax.dot_general(
        normed_copies,
        pre_quarters,
        (((1,), (1,)), ((0,), (0,))),
        preferred_element_type=jnp.float32,
    )
    partial_out = lax.dot_general(
        act_flat, grad_flat, (((0,), (0,)), ((), ())), preferred_element_type=jnp.float32
    )
    branch = branch.reshape(image_rows, TILE_COLS, channels)
    grad_norm = grad_norm.reshape(image_rows, TILE_COLS, channels)
    image_tile = lax.dynamic_slice_in_dim(image, first_col, TILE_COLS, axis=1)
    out_tile = (image_tile.astype(jnp.float32) + 1.0 * layer_scale * branch).astype(jnp.bfloat16)
    block_out = lax.dynamic_update_slice_in_dim(image, out_tile, first_col, axis=1)
    scale_grad = jnp.sum(1.0 * branch * upstream, axis=(0, 1))
    gain_grad = jnp.sum(grad_norm * standard, axis=(0, 1))
    grad_std = grad_norm * ln_gain
    grad_tile = (
        inv_std
        * (
            grad_std
            - jnp.mean(grad_std, axis=-1, keepdims=True)
            - standard * jnp.mean(grad_std * standard, axis=-1, keepdims=True)
        )
    ).astype(jnp.bfloat16)
    kernel_grad = kernel_terms(window, grad_tile.astype(jnp.float32), image_rows, TILE_COLS)
    packed = jnp.concatenate([kernel_grad, gain_grad[None], scale_grad[None]], axis=0)
    owned_in, grad_w_out, small_grads = halving_reduce(partial_in, partial_out, packed, "row")
    grad_w_in = owned_in.transpose(1, 0, 2).reshape(-1, hidden)
    flipped = kernel[::-1, ::-1]
    tile_padded = jnp.pad(
        grad_tile.astype(jnp.float32),
        ((half_width, half_width), (2 * half_width, 2 * half_width), (0, 0)),
    )
    own = depthwise(tile_padded, flipped, image_rows, span)
    own_full = lax.dynamic_update_slice_in_dim(
        jnp.zeros((image_rows, image_cols + 2 * half_width, channels), jnp.float32),
        own,
        first_col,
        axis=1,
    )[:, half_width : half_width + image_cols]
    grad_conv = lax.dynamic_update_slice_in_dim(
        jnp.zeros_like(image), grad_tile, first_col, axis=1
    )
    low, high = halo_rows(grad_conv, "row", half_width)
    edge = ((0, 0), (half_width, half_width), (0, 0))
    low = jnp.pad(low, edge)
    high = jnp.pad(high, edge)
    halo_out = []
    for out_row in range(image_rows):
        total = jnp.zeros((image_cols, channels), jnp.float32)
        for row_tap in range(KERNEL):
            source = out_row + row_tap
            if source < half_width:
                line = low[source]
            elif source >= half_width + image_rows:
                line = high[source - half_width - image_rows]
            else:
                continue
            for col_tap in range(KERNEL):
                total = total + line[col_tap : col_tap + image_cols] * flipped[row_tap, col_tap]
        halo_out.append(total)
    conv_back = own_full + jnp.stack(halo_out)
    grad_image = (cotangent.astype(jnp.float32) + conv_back).astype(jnp.bfloat16)
    return (block_out, grad_image, grad_w_in, grad_w_out, small_grads)


def solution(mesh):
    placed = (
        P(("group", "row"), None, None),
        P(("group", "row"), None),
        P(),
        P(),
        P(),
        P(),
        P(),
        P(("group", "row"), None, None),
    )
    return jax.shard_map(
        shards,
        mesh=mesh,
        in_specs=placed,
        out_specs=(
            P(("group", "row"), None, None),
            P(("group", "row"), None, None),
            P(("group", "row"), None),
            P(("group", "row"), None),
            P("group", None),
        ),
        check_vma=False,
    )
```

```python
import jax
import jax.numpy as jnp
from jax import lax
from jax.sharding import PartitionSpec as P

KERNEL = 7
TILE_ROWS = 4
TILE_COLS = 128


EPSILON = 1e-06
ROOT_TWO_PI = 0.7978845608028654
CUBIC_TERM = 0.044715


def padded_2(block, sides, width):
    for axis, dim in sides:
        count = lax.axis_size(axis)
        forward = [(i, i + 1) for i in range(count - 1)]
        backward = [(target, source) for source, target in forward]
        low = lax.ppermute(
            lax.slice_in_dim(block, block.shape[dim] - width, None, axis=dim), axis, forward
        )
        high = lax.ppermute(lax.slice_in_dim(block, 0, width, axis=dim), axis, backward)
        block = jnp.concatenate([low, block, high], axis=dim)
    return block


def bit_reversed(values, count, steps, axis):
    shape = values.shape
    values = values.reshape(shape[:axis] + (2,) * steps + (shape[axis] // count,) + shape[axis + 1 :])
    order = (
        tuple(range(axis))
        + tuple(axis + steps - 1 - i for i in range(steps))
        + tuple(range(axis + steps, values.ndim))
    )
    return values.transpose(order).reshape(shape)


def split_pair(values):
    high = values.astype(jnp.bfloat16)
    low = (values - high.astype(jnp.float32)).astype(jnp.bfloat16)
    return high, low


def halving_reduce(quartered, rows, whole, axis):
    count = lax.axis_size(axis)
    steps = count.bit_length() - 1
    if (1 << steps) != count:
        return (
            lax.psum_scatter(quartered, axis, scatter_dimension=1, tiled=True),
            lax.psum_scatter(rows, axis, scatter_dimension=0, tiled=True),
            lax.psum(whole, axis),
        )
    me = lax.axis_index(axis)
    quartered = bit_reversed(quartered, count, steps, 1)
    rows = bit_reversed(rows, count, steps, 0)
    quarters, width = quartered.shape[0], quartered.shape[2]
    for step in range(steps):
        bit = (me >> step) & 1
        pairs = [(i, i ^ (1 << step)) for i in range(count)]
        half_q = quartered.shape[1] // 2
        half_r = rows.shape[0] // 2
        keep_q = lax.dynamic_slice_in_dim(quartered, bit * half_q, half_q, axis=1)
        give_q = lax.dynamic_slice_in_dim(quartered, (1 - bit) * half_q, half_q, axis=1)
        keep_r = lax.dynamic_slice_in_dim(rows, bit * half_r, half_r, axis=0)
        give_r = lax.dynamic_slice_in_dim(rows, (1 - bit) * half_r, half_r, axis=0)
        if step == 0:
            got_q, got_r, got_whole = lax.ppermute((give_q, give_r, whole), axis, pairs)
            whole = whole + got_whole
        else:
            high, low = split_pair(whole)
            sent = jnp.concatenate(
                [give_q.astype(jnp.bfloat16).reshape(-1, width), give_r.astype(jnp.bfloat16), high, low],
                axis=0,
            )
            got = lax.ppermute(sent, axis, pairs)
            cut_q = quarters * half_q
            cut_r = cut_q + half_r
            size = whole.shape[0]
            got_q = got[:cut_q].reshape(quarters, half_q, width)
            got_r = got[cut_q:cut_r]
            mine = high.astype(jnp.float32) + low.astype(jnp.float32)
            theirs = got[cut_r : cut_r + size].astype(jnp.float32) + got[cut_r + size :].astype(
                jnp.float32
            )
            whole = mine + theirs
        quartered = keep_q + got_q.astype(jnp.float32)
        rows = keep_r + got_r.astype(jnp.float32)
        quartered, rows, whole = lax.optimization_barrier((quartered, rows, whole))
    return quartered, rows, whole


def halo_rows(block, axis, width):
    count = lax.axis_size(axis)
    forward = [(i, i + 1) for i in range(count - 1)]
    backward = [(target, source) for source, target in forward]
    low = lax.ppermute(lax.slice_in_dim(block, block.shape[0] - width, None, axis=0), axis, forward)
    high = lax.ppermute(lax.slice_in_dim(block, 0, width, axis=0), axis, backward)
    return low, high


def gelu_value(inputs):
    tangent = jnp.tanh(ROOT_TWO_PI * (inputs + CUBIC_TERM * inputs * inputs * inputs))
    return 0.5 * inputs * (1.0 + tangent)


def gelu_slope(inputs):
    tangent = jnp.tanh(ROOT_TWO_PI * (inputs + CUBIC_TERM * inputs * inputs * inputs))
    return 0.5 * (1.0 + tangent) + 0.5 * inputs * (1.0 - tangent * tangent) * ROOT_TWO_PI * (
        1.0 + 3.0 * CUBIC_TERM * inputs * inputs
    )


def depthwise(padded, kernel, image_rows, image_cols):
    total = jnp.zeros((image_rows, image_cols, kernel.shape[-1]), jnp.float32)
    for row_tap in range(KERNEL):
        for col_tap in range(KERNEL):
            total = (
                total
                + padded[row_tap : row_tap + image_rows, col_tap : col_tap + image_cols]
                * kernel[row_tap, col_tap]
            )
    return total


def kernel_terms(padded, grads, image_rows, image_cols):
    collected = []
    for row_tap in range(KERNEL):
        for col_tap in range(KERNEL):
            collected.append(
                jnp.sum(
                    padded[row_tap : row_tap + image_rows, col_tap : col_tap + image_cols] * grads,
                    axis=(0, 1),
                )
            )
    return jnp.stack(collected)


def shards(image, tissue, kernel, ln_gain, w_in, w_out, layer_scale, cotangent):
    half_width = KERNEL // 2
    image_rows, image_cols, channels = image.shape
    hidden = w_in.shape[1]
    span = TILE_COLS + 2 * half_width

    first_col = jnp.argmax(tissue.reshape(-1)).astype(jnp.int32) * TILE_COLS
    extended = padded_2(image, (("row", 0),), half_width)
    padded = jnp.pad(extended, ((0, 0), (half_width, half_width), (0, 0)))
    window = lax.dynamic_slice_in_dim(padded, first_col, span, axis=1).astype(jnp.float32)
    filtered = depthwise(window, kernel, image_rows, TILE_COLS)
    centre = jnp.mean(filtered, axis=-1, keepdims=True)
    centered = filtered - centre
    inv_std = lax.rsqrt(jnp.mean(centered * centered, axis=-1, keepdims=True) + EPSILON)
    standard = centered * inv_std
    normed = (standard * ln_gain).astype(jnp.bfloat16)
    upstream = lax.dynamic_slice_in_dim(cotangent, first_col, TILE_COLS, axis=1).astype(jnp.float32)
    grad_out = (1.0 * layer_scale * upstream).astype(jnp.bfloat16)

    normed_flat = normed.reshape(-1, channels)
    grad_flat = grad_out.reshape(-1, channels)
    pre_act = jnp.dot(normed_flat, w_in, preferred_element_type=jnp.float32)
    act_flat = gelu_value(pre_act).astype(jnp.bfloat16)
    branch = jnp.dot(act_flat, w_out, preferred_element_type=jnp.float32)
    grad_act = jnp.dot(grad_flat, w_out.T, preferred_element_type=jnp.float32)
    pre_flat = (grad_act * gelu_slope(pre_act)).astype(jnp.bfloat16)
    grad_norm = jnp.dot(pre_flat, w_in.T, preferred_element_type=jnp.float32)
    quarters = hidden // channels
    positions = pre_flat.shape[0]
    pre_quarters = pre_flat.reshape(positions, quarters, channels).transpose(1, 0, 2)
    normed_copies = jnp.broadcast_to(normed_flat[None], (quarters, positions, channels))
    partial_in = lax.dot_general(
        normed_copies,
        pre_quarters,
        (((1,), (1,)), ((0,), (0,))),
        preferred_element_type=jnp.float32,
    )
    partial_out = lax.dot_general(
        act_flat, grad_flat, (((0,), (0,)), ((), ())), preferred_element_type=jnp.float32
    )
    branch = branch.reshape(image_rows, TILE_COLS, channels)
    grad_norm = grad_norm.reshape(image_rows, TILE_COLS, channels)
    image_tile = lax.dynamic_slice_in_dim(image, first_col, TILE_COLS, axis=1)
    out_tile = (image_tile.astype(jnp.float32) + 1.0 * layer_scale * branch).astype(jnp.bfloat16)
    block_out = lax.dynamic_update_slice_in_dim(image, out_tile, first_col, axis=1)
    scale_grad = jnp.sum(1.0 * branch * upstream, axis=(0, 1))
    gain_grad = jnp.sum(grad_norm * standard, axis=(0, 1))
    grad_std = grad_norm * ln_gain
    grad_tile = (
        inv_std
        * (
            grad_std
            - jnp.mean(grad_std, axis=-1, keepdims=True)
            - standard * jnp.mean(grad_std * standard, axis=-1, keepdims=True)
        )
    ).astype(jnp.bfloat16)
    kernel_grad = kernel_terms(window, grad_tile.astype(jnp.float32), image_rows, TILE_COLS)
    packed = jnp.concatenate([kernel_grad, gain_grad[None], scale_grad[None]], axis=0)
    owned_in, grad_w_out, small_grads = halving_reduce(partial_in, partial_out, packed, "row")
    grad_w_in = owned_in.transpose(1, 0, 2).reshape(-1, hidden)
    flipped = kernel[::-1, ::-1]
    tile_padded = jnp.pad(
        grad_tile.astype(jnp.float32),
        ((half_width, half_width), (2 * half_width, 2 * half_width), (0, 0)),
    )
    own = depthwise(tile_padded, flipped, image_rows, span)
    tile_index = first_col // TILE_COLS
    own_full = jnp.zeros((image_rows, image_cols, channels), jnp.float32)
    for tile in range(image_cols // TILE_COLS):
        left = tile * TILE_COLS - half_width
        lo, hi = max(left, 0), min(left + span, image_cols)
        placed = jnp.pad(own[:, lo - left : hi - left], ((0, 0), (lo, image_cols - hi), (0, 0)))
        own_full = jnp.where(tile_index == tile, placed, own_full)
    grad_conv = lax.dynamic_update_slice_in_dim(
        jnp.zeros_like(image), grad_tile, first_col, axis=1
    )
    low, high = halo_rows(grad_conv, "row", half_width)
    edge = ((0, 0), (half_width, half_width), (0, 0))
    low = jnp.pad(low.astype(jnp.float32), edge)
    high = jnp.pad(high.astype(jnp.float32), edge)
    halo_out = []
    for out_row in range(image_rows):
        total = jnp.zeros((image_cols, channels), jnp.float32)
        for row_tap in range(KERNEL):
            source = out_row + row_tap
            if source < half_width:
                line = low[source]
            elif source >= half_width + image_rows:
                line = high[source - half_width - image_rows]
            else:
                continue
            for col_tap in range(KERNEL):
                total = total + line[col_tap : col_tap + image_cols] * flipped[row_tap, col_tap]
        halo_out.append(total)
    conv_back = own_full + jnp.stack(halo_out)
    grad_image = (cotangent.astype(jnp.float32) + conv_back).astype(jnp.bfloat16)
    return (block_out, grad_image, grad_w_in, grad_w_out, small_grads)


def solution(mesh):
    placed = (
        P(("group", "row"), None, None),
        P(("group", "row"), None),
        P(),
        P(),
        P(),
        P(),
        P(),
        P(("group", "row"), None, None),
    )
    return jax.shard_map(
        shards,
        mesh=mesh,
        in_specs=placed,
        out_specs=(
            P(("group", "row"), None, None),
            P(("group", "row"), None, None),
            P(("group", "row"), None),
            P(("group", "row"), None),
            P("group", None),
        ),
        check_vma=False,
    )
```

```python
import jax
import jax.numpy as jnp
from jax import lax
from jax.sharding import PartitionSpec as P

KERNEL = 7
TILE_ROWS = 4
TILE_COLS = 128


EPSILON = 1e-06
ROOT_TWO_PI = 0.7978845608028654
CUBIC_TERM = 0.044715


def padded_2(block, sides, width):
    for axis, dim in sides:
        count = lax.axis_size(axis)
        forward = [(i, i + 1) for i in range(count - 1)]
        backward = [(target, source) for source, target in forward]
        low = lax.ppermute(
            lax.slice_in_dim(block, block.shape[dim] - width, None, axis=dim), axis, forward
        )
        high = lax.ppermute(lax.slice_in_dim(block, 0, width, axis=dim), axis, backward)
        block = jnp.concatenate([low, block, high], axis=dim)
    return block


def bit_reversed(values, count, steps, axis):
    shape = values.shape
    values = values.reshape(shape[:axis] + (2,) * steps + (shape[axis] // count,) + shape[axis + 1 :])
    order = (
        tuple(range(axis))
        + tuple(axis + steps - 1 - i for i in range(steps))
        + tuple(range(axis + steps, values.ndim))
    )
    return values.transpose(order).reshape(shape)


def split_pair(values):
    high = values.astype(jnp.bfloat16)
    low = (values - high.astype(jnp.float32)).astype(jnp.bfloat16)
    return high, low


def four_way(quartered, rows, whole, axis, step):
    count = lax.axis_size(axis)
    me = lax.axis_index(axis)
    quarters, width = quartered.shape[0], quartered.shape[2]
    part_q = quartered.shape[1] // 4
    part_r = rows.shape[0] // 4
    mine = 2 * ((me >> step) & 1) + ((me >> (step + 1)) & 1)
    high, low = split_pair(whole)
    size = whole.shape[0]
    cut_q = quarters * part_q
    cut_r = cut_q + part_r
    quartered_new = lax.dynamic_slice_in_dim(quartered, mine * part_q, part_q, axis=1)
    rows_new = lax.dynamic_slice_in_dim(rows, mine * part_r, part_r, axis=0)
    decoded = [high.astype(jnp.float32) + low.astype(jnp.float32)]
    for offset in (1, 2, 3):
        mask = ((offset >> 1) << step) | ((offset & 1) << (step + 1))
        pairs = [(i, i ^ mask) for i in range(count)]
        other = mine ^ offset
        give_q = lax.dynamic_slice_in_dim(quartered, other * part_q, part_q, axis=1)
        give_r = lax.dynamic_slice_in_dim(rows, other * part_r, part_r, axis=0)
        sent = jnp.concatenate(
            [give_q.astype(jnp.bfloat16).reshape(-1, width), give_r.astype(jnp.bfloat16), high, low],
            axis=0,
        )
        got = lax.ppermute(sent, axis, pairs)
        quartered_new = quartered_new + got[:cut_q].reshape(quarters, part_q, width).astype(jnp.float32)
        rows_new = rows_new + got[cut_q:cut_r].astype(jnp.float32)
        decoded.append(
            got[cut_r : cut_r + size].astype(jnp.float32) + got[cut_r + size :].astype(jnp.float32)
        )
    ordered = jnp.stack(decoded)[jnp.bitwise_xor(jnp.arange(4), mine)]
    whole = ((ordered[0] + ordered[1]) + ordered[2]) + ordered[3]
    return lax.optimization_barrier((quartered_new, rows_new, whole))


def halving_reduce(quartered, rows, whole, axis):
    count = lax.axis_size(axis)
    steps = count.bit_length() - 1
    if (1 << steps) != count:
        return (
            lax.psum_scatter(quartered, axis, scatter_dimension=1, tiled=True),
            lax.psum_scatter(rows, axis, scatter_dimension=0, tiled=True),
            lax.psum(whole, axis),
        )
    me = lax.axis_index(axis)
    quartered = bit_reversed(quartered, count, steps, 1)
    rows = bit_reversed(rows, count, steps, 0)
    quarters, width = quartered.shape[0], quartered.shape[2]
    rounds, step = [[0]], 1
    while step < steps:
        rounds.append([step, step + 1] if step + 1 < steps else [step])
        step += len(rounds[-1])
    for bits in rounds:
        if len(bits) == 2:
            quartered, rows, whole = four_way(quartered, rows, whole, axis, bits[0])
            continue
        step = bits[0]
        bit = (me >> step) & 1
        pairs = [(i, i ^ (1 << step)) for i in range(count)]
        half_q = quartered.shape[1] // 2
        half_r = rows.shape[0] // 2
        keep_q = lax.dynamic_slice_in_dim(quartered, bit * half_q, half_q, axis=1)
        give_q = lax.dynamic_slice_in_dim(quartered, (1 - bit) * half_q, half_q, axis=1)
        keep_r = lax.dynamic_slice_in_dim(rows, bit * half_r, half_r, axis=0)
        give_r = lax.dynamic_slice_in_dim(rows, (1 - bit) * half_r, half_r, axis=0)
        if step == 0:
            got_q, got_r, got_whole = lax.ppermute((give_q, give_r, whole), axis, pairs)
            whole = whole + got_whole
        else:
            high, low = split_pair(whole)
            sent = jnp.concatenate(
                [give_q.astype(jnp.bfloat16).reshape(-1, width), give_r.astype(jnp.bfloat16), high, low],
                axis=0,
            )
            got = lax.ppermute(sent, axis, pairs)
            cut_q = quarters * half_q
            cut_r = cut_q + half_r
            size = whole.shape[0]
            got_q = got[:cut_q].reshape(quarters, half_q, width)
            got_r = got[cut_q:cut_r]
            mine = high.astype(jnp.float32) + low.astype(jnp.float32)
            theirs = got[cut_r : cut_r + size].astype(jnp.float32) + got[cut_r + size :].astype(
                jnp.float32
            )
            whole = mine + theirs
        quartered = keep_q + got_q.astype(jnp.float32)
        rows = keep_r + got_r.astype(jnp.float32)
        quartered, rows, whole = lax.optimization_barrier((quartered, rows, whole))
    return quartered, rows, whole


def halo_rows(block, axis, width):
    count = lax.axis_size(axis)
    forward = [(i, i + 1) for i in range(count - 1)]
    backward = [(target, source) for source, target in forward]
    low = lax.ppermute(lax.slice_in_dim(block, block.shape[0] - width, None, axis=0), axis, forward)
    high = lax.ppermute(lax.slice_in_dim(block, 0, width, axis=0), axis, backward)
    return low, high


def gelu_value(inputs):
    tangent = jnp.tanh(ROOT_TWO_PI * (inputs + CUBIC_TERM * inputs * inputs * inputs))
    return 0.5 * inputs * (1.0 + tangent)


def gelu_slope(inputs):
    tangent = jnp.tanh(ROOT_TWO_PI * (inputs + CUBIC_TERM * inputs * inputs * inputs))
    return 0.5 * (1.0 + tangent) + 0.5 * inputs * (1.0 - tangent * tangent) * ROOT_TWO_PI * (
        1.0 + 3.0 * CUBIC_TERM * inputs * inputs
    )


def depthwise(padded, kernel, image_rows, image_cols):
    total = jnp.zeros((image_rows, image_cols, kernel.shape[-1]), jnp.float32)
    for row_tap in range(KERNEL):
        for col_tap in range(KERNEL):
            total = (
                total
                + padded[row_tap : row_tap + image_rows, col_tap : col_tap + image_cols]
                * kernel[row_tap, col_tap]
            )
    return total


def kernel_terms(padded, grads, image_rows, image_cols):
    collected = []
    for row_tap in range(KERNEL):
        for col_tap in range(KERNEL):
            collected.append(
                jnp.sum(
                    padded[row_tap : row_tap + image_rows, col_tap : col_tap + image_cols] * grads,
                    axis=(0, 1),
                )
            )
    return jnp.stack(collected)


def shards(image, tissue, kernel, ln_gain, w_in, w_out, layer_scale, cotangent):
    half_width = KERNEL // 2
    image_rows, image_cols, channels = image.shape
    hidden = w_in.shape[1]
    span = TILE_COLS + 2 * half_width

    first_col = jnp.argmax(tissue.reshape(-1)).astype(jnp.int32) * TILE_COLS
    extended = padded_2(image, (("row", 0),), half_width)
    padded = jnp.pad(extended, ((0, 0), (half_width, half_width), (0, 0)))
    window = lax.dynamic_slice_in_dim(padded, first_col, span, axis=1).astype(jnp.float32)
    filtered = depthwise(window, kernel, image_rows, TILE_COLS)
    centre = jnp.mean(filtered, axis=-1, keepdims=True)
    centered = filtered - centre
    inv_std = lax.rsqrt(jnp.mean(centered * centered, axis=-1, keepdims=True) + EPSILON)
    standard = centered * inv_std
    normed = (standard * ln_gain).astype(jnp.bfloat16)
    upstream = lax.dynamic_slice_in_dim(cotangent, first_col, TILE_COLS, axis=1).astype(jnp.float32)
    grad_out = (1.0 * layer_scale * upstream).astype(jnp.bfloat16)

    normed_flat = normed.reshape(-1, channels)
    grad_flat = grad_out.reshape(-1, channels)
    pre_act = jnp.dot(normed_flat, w_in, preferred_element_type=jnp.float32)
    act_flat = gelu_value(pre_act).astype(jnp.bfloat16)
    branch = jnp.dot(act_flat, w_out, preferred_element_type=jnp.float32)
    grad_act = jnp.dot(grad_flat, w_out.T, preferred_element_type=jnp.float32)
    pre_flat = (grad_act * gelu_slope(pre_act)).astype(jnp.bfloat16)
    grad_norm = jnp.dot(pre_flat, w_in.T, preferred_element_type=jnp.float32)
    quarters = hidden // channels
    positions = pre_flat.shape[0]
    pre_quarters = pre_flat.reshape(positions, quarters, channels).transpose(1, 0, 2)
    normed_copies = jnp.broadcast_to(normed_flat[None], (quarters, positions, channels))
    partial_in = lax.dot_general(
        normed_copies,
        pre_quarters,
        (((1,), (1,)), ((0,), (0,))),
        preferred_element_type=jnp.float32,
    )
    partial_out = lax.dot_general(
        act_flat, grad_flat, (((0,), (0,)), ((), ())), preferred_element_type=jnp.float32
    )
    branch = branch.reshape(image_rows, TILE_COLS, channels)
    grad_norm = grad_norm.reshape(image_rows, TILE_COLS, channels)
    image_tile = lax.dynamic_slice_in_dim(image, first_col, TILE_COLS, axis=1)
    out_tile = (image_tile.astype(jnp.float32) + 1.0 * layer_scale * branch).astype(jnp.bfloat16)
    block_out = lax.dynamic_update_slice_in_dim(image, out_tile, first_col, axis=1)
    scale_grad = jnp.sum(1.0 * branch * upstream, axis=(0, 1))
    gain_grad = jnp.sum(grad_norm * standard, axis=(0, 1))
    grad_std = grad_norm * ln_gain
    grad_tile = (
        inv_std
        * (
            grad_std
            - jnp.mean(grad_std, axis=-1, keepdims=True)
            - standard * jnp.mean(grad_std * standard, axis=-1, keepdims=True)
        )
    ).astype(jnp.bfloat16)
    kernel_grad = kernel_terms(window, grad_tile.astype(jnp.float32), image_rows, TILE_COLS)
    packed = jnp.concatenate([kernel_grad, gain_grad[None], scale_grad[None]], axis=0)
    owned_in, grad_w_out, small_grads = halving_reduce(partial_in, partial_out, packed, "row")
    grad_w_in = owned_in.transpose(1, 0, 2).reshape(-1, hidden)
    flipped = kernel[::-1, ::-1]
    tile_padded = jnp.pad(
        grad_tile.astype(jnp.float32),
        ((half_width, half_width), (2 * half_width, 2 * half_width), (0, 0)),
    )
    own = depthwise(tile_padded, flipped, image_rows, span)
    tile_index = first_col // TILE_COLS
    own_full = jnp.zeros((image_rows, image_cols, channels), jnp.float32)
    for tile in range(image_cols // TILE_COLS):
        left = tile * TILE_COLS - half_width
        lo, hi = max(left, 0), min(left + span, image_cols)
        placed = jnp.pad(own[:, lo - left : hi - left], ((0, 0), (lo, image_cols - hi), (0, 0)))
        own_full = jnp.where(tile_index == tile, placed, own_full)
    grad_conv = lax.dynamic_update_slice_in_dim(
        jnp.zeros_like(image), grad_tile, first_col, axis=1
    )
    low, high = halo_rows(grad_conv, "row", half_width)
    edge = ((0, 0), (half_width, half_width), (0, 0))
    low = jnp.pad(low.astype(jnp.float32), edge)
    high = jnp.pad(high.astype(jnp.float32), edge)
    halo_out = []
    for out_row in range(image_rows):
        total = jnp.zeros((image_cols, channels), jnp.float32)
        for row_tap in range(KERNEL):
            source = out_row + row_tap
            if source < half_width:
                line = low[source]
            elif source >= half_width + image_rows:
                line = high[source - half_width - image_rows]
            else:
                continue
            for col_tap in range(KERNEL):
                total = total + line[col_tap : col_tap + image_cols] * flipped[row_tap, col_tap]
        halo_out.append(total)
    conv_back = own_full + jnp.stack(halo_out)
    grad_image = (cotangent.astype(jnp.float32) + conv_back).astype(jnp.bfloat16)
    return (block_out, grad_image, grad_w_in, grad_w_out, small_grads)


def solution(mesh):
    placed = (
        P(("group", "row"), None, None),
        P(("group", "row"), None),
        P(),
        P(),
        P(),
        P(),
        P(),
        P(("group", "row"), None, None),
    )
    return jax.shard_map(
        shards,
        mesh=mesh,
        in_specs=placed,
        out_specs=(
            P(("group", "row"), None, None),
            P(("group", "row"), None, None),
            P(("group", "row"), None),
            P(("group", "row"), None),
            P("group", None),
        ),
        check_vma=False,
    )
```

```python
import jax
import jax.numpy as jnp
from jax import lax
from jax.sharding import PartitionSpec as P

KERNEL = 7
TILE_ROWS = 4
TILE_COLS = 128


EPSILON = 1e-06
ROOT_TWO_PI = 0.7978845608028654
CUBIC_TERM = 0.044715


def padded_2(block, sides, width):
    for axis, dim in sides:
        count = lax.axis_size(axis)
        forward = [(i, i + 1) for i in range(count - 1)]
        backward = [(target, source) for source, target in forward]
        low = lax.ppermute(
            lax.slice_in_dim(block, block.shape[dim] - width, None, axis=dim), axis, forward
        )
        high = lax.ppermute(lax.slice_in_dim(block, 0, width, axis=dim), axis, backward)
        block = jnp.concatenate([low, block, high], axis=dim)
    return block


def bit_reversed(values, count, steps, axis):
    shape = values.shape
    values = values.reshape(shape[:axis] + (2,) * steps + (shape[axis] // count,) + shape[axis + 1 :])
    order = (
        tuple(range(axis))
        + tuple(axis + steps - 1 - i for i in range(steps))
        + tuple(range(axis + steps, values.ndim))
    )
    return values.transpose(order).reshape(shape)


def split_pair(values):
    high = values.astype(jnp.bfloat16)
    low = (values - high.astype(jnp.float32)).astype(jnp.bfloat16)
    return high, low


def halving_reduce(quartered, rows, whole, axis):
    count = lax.axis_size(axis)
    steps = count.bit_length() - 1
    if (1 << steps) != count:
        return (
            lax.psum_scatter(quartered, axis, scatter_dimension=1, tiled=True),
            lax.psum_scatter(rows, axis, scatter_dimension=0, tiled=True),
            lax.psum(whole, axis),
        )
    me = lax.axis_index(axis)
    quartered = bit_reversed(quartered, count, steps, 1)
    rows = bit_reversed(rows, count, steps, 0)
    quarters, width = quartered.shape[0], quartered.shape[2]
    for step in range(steps):
        bit = (me >> step) & 1
        pairs = [(i, i ^ (1 << step)) for i in range(count)]
        half_q = quartered.shape[1] // 2
        half_r = rows.shape[0] // 2
        keep_q = lax.dynamic_slice_in_dim(quartered, bit * half_q, half_q, axis=1)
        give_q = lax.dynamic_slice_in_dim(quartered, (1 - bit) * half_q, half_q, axis=1)
        keep_r = lax.dynamic_slice_in_dim(rows, bit * half_r, half_r, axis=0)
        give_r = lax.dynamic_slice_in_dim(rows, (1 - bit) * half_r, half_r, axis=0)
        if step == 0:
            got_q, got_r, got_whole = lax.ppermute((give_q, give_r, whole), axis, pairs)
            whole = whole + got_whole
        else:
            high, low = split_pair(whole)
            sent = jnp.concatenate(
                [give_q.astype(jnp.bfloat16).reshape(-1, width), give_r.astype(jnp.bfloat16), high, low],
                axis=0,
            )
            got = lax.ppermute(sent, axis, pairs)
            cut_q = quarters * half_q
            cut_r = cut_q + half_r
            size = whole.shape[0]
            got_q = got[:cut_q].reshape(quarters, half_q, width)
            got_r = got[cut_q:cut_r]
            mine = high.astype(jnp.float32) + low.astype(jnp.float32)
            theirs = got[cut_r : cut_r + size].astype(jnp.float32) + got[cut_r + size :].astype(
                jnp.float32
            )
            whole = mine + theirs
        quartered = keep_q + got_q.astype(jnp.float32)
        rows = keep_r + got_r.astype(jnp.float32)
        quartered, rows, whole = lax.optimization_barrier((quartered, rows, whole))
    return quartered, rows, whole


def halo_rows(block, axis, width):
    count = lax.axis_size(axis)
    forward = [(i, i + 1) for i in range(count - 1)]
    backward = [(target, source) for source, target in forward]
    low = lax.ppermute(lax.slice_in_dim(block, block.shape[0] - width, None, axis=0), axis, forward)
    high = lax.ppermute(lax.slice_in_dim(block, 0, width, axis=0), axis, backward)
    return low, high


def gelu_value(inputs):
    tangent = jnp.tanh(ROOT_TWO_PI * (inputs + CUBIC_TERM * inputs * inputs * inputs))
    return 0.5 * inputs * (1.0 + tangent)


def gelu_slope(inputs):
    tangent = jnp.tanh(ROOT_TWO_PI * (inputs + CUBIC_TERM * inputs * inputs * inputs))
    return 0.5 * (1.0 + tangent) + 0.5 * inputs * (1.0 - tangent * tangent) * ROOT_TWO_PI * (
        1.0 + 3.0 * CUBIC_TERM * inputs * inputs
    )


def depthwise(padded, kernel, image_rows, image_cols):
    total = jnp.zeros((image_rows, image_cols, kernel.shape[-1]), jnp.float32)
    for row_tap in range(KERNEL):
        for col_tap in range(KERNEL):
            total = (
                total
                + padded[row_tap : row_tap + image_rows, col_tap : col_tap + image_cols]
                * kernel[row_tap, col_tap]
            )
    return total


def kernel_terms(padded, grads, image_rows, image_cols):
    collected = []
    for row_tap in range(KERNEL):
        for col_tap in range(KERNEL):
            collected.append(
                jnp.sum(
                    padded[row_tap : row_tap + image_rows, col_tap : col_tap + image_cols] * grads,
                    axis=(0, 1),
                )
            )
    return jnp.stack(collected)


def shards(image, tissue, kernel, ln_gain, w_in, w_out, layer_scale, cotangent):
    half_width = KERNEL // 2
    image_rows, image_cols, channels = image.shape
    hidden = w_in.shape[1]
    span = TILE_COLS + 2 * half_width

    first_col = jnp.argmax(tissue.reshape(-1)).astype(jnp.int32) * TILE_COLS
    extended = padded_2(image, (("row", 0),), half_width)
    padded = jnp.pad(extended, ((0, 0), (half_width, half_width), (0, 0)))
    window = lax.dynamic_slice_in_dim(padded, first_col, span, axis=1).astype(jnp.float32)
    filtered = depthwise(window, kernel, image_rows, TILE_COLS)
    centre = jnp.mean(filtered, axis=-1, keepdims=True)
    centered = filtered - centre
    inv_std = lax.rsqrt(jnp.mean(centered * centered, axis=-1, keepdims=True) + EPSILON)
    standard = centered * inv_std
    normed = (standard * ln_gain).astype(jnp.bfloat16)
    upstream = lax.dynamic_slice_in_dim(cotangent, first_col, TILE_COLS, axis=1).astype(jnp.float32)
    grad_out = (1.0 * layer_scale * upstream).astype(jnp.bfloat16)

    normed_flat = normed.reshape(-1, channels)
    grad_flat = grad_out.reshape(-1, channels)
    pre_act = jnp.dot(normed_flat, w_in, preferred_element_type=jnp.float32)
    act_flat = gelu_value(pre_act).astype(jnp.bfloat16)
    branch = jnp.dot(act_flat, w_out, preferred_element_type=jnp.float32)
    grad_act = jnp.dot(grad_flat, w_out.T, preferred_element_type=jnp.float32)
    pre_flat = (grad_act * gelu_slope(pre_act)).astype(jnp.bfloat16)
    grad_norm = jnp.dot(pre_flat, w_in.T, preferred_element_type=jnp.float32)
    quarters = hidden // channels
    positions = pre_flat.shape[0]
    pre_quarters = pre_flat.reshape(positions, quarters, channels).transpose(1, 0, 2)
    normed_copies = jnp.broadcast_to(normed_flat[None], (quarters, positions, channels))
    partial_in = lax.dot_general(
        normed_copies,
        pre_quarters,
        (((1,), (1,)), ((0,), (0,))),
        preferred_element_type=jnp.float32,
    )
    partial_out = lax.dot_general(
        act_flat, grad_flat, (((0,), (0,)), ((), ())), preferred_element_type=jnp.float32
    )
    branch = branch.reshape(image_rows, TILE_COLS, channels)
    grad_norm = grad_norm.reshape(image_rows, TILE_COLS, channels)
    image_tile = lax.dynamic_slice_in_dim(image, first_col, TILE_COLS, axis=1)
    out_tile = (image_tile.astype(jnp.float32) + 1.0 * layer_scale * branch).astype(jnp.bfloat16)
    tile_index = first_col // TILE_COLS
    tiles = image_cols // TILE_COLS
    block_out = image
    for tile in range(tiles):
        placed = jnp.concatenate(
            [image[:, : tile * TILE_COLS], out_tile, image[:, (tile + 1) * TILE_COLS :]], axis=1
        )
        block_out = jnp.where(tile_index == tile, placed, block_out)
    scale_grad = jnp.sum(1.0 * branch * upstream, axis=(0, 1))
    gain_grad = jnp.sum(grad_norm * standard, axis=(0, 1))
    grad_std = grad_norm * ln_gain
    grad_tile = (
        inv_std
        * (
            grad_std
            - jnp.mean(grad_std, axis=-1, keepdims=True)
            - standard * jnp.mean(grad_std * standard, axis=-1, keepdims=True)
        )
    ).astype(jnp.bfloat16)
    kernel_grad = kernel_terms(window, grad_tile.astype(jnp.float32), image_rows, TILE_COLS)
    packed = jnp.concatenate([kernel_grad, gain_grad[None], scale_grad[None]], axis=0)
    owned_in, grad_w_out, small_grads = halving_reduce(partial_in, partial_out, packed, "row")
    grad_w_in = owned_in.transpose(1, 0, 2).reshape(-1, hidden)
    flipped = kernel[::-1, ::-1]
    tile_padded = jnp.pad(
        grad_tile.astype(jnp.float32),
        ((half_width, half_width), (2 * half_width, 2 * half_width), (0, 0)),
    )
    own = depthwise(tile_padded, flipped, image_rows, span)
    own_full = jnp.zeros((image_rows, image_cols, channels), jnp.float32)
    for tile in range(image_cols // TILE_COLS):
        left = tile * TILE_COLS - half_width
        lo, hi = max(left, 0), min(left + span, image_cols)
        placed = jnp.pad(own[:, lo - left : hi - left], ((0, 0), (lo, image_cols - hi), (0, 0)))
        own_full = jnp.where(tile_index == tile, placed, own_full)
    grad_conv = jnp.zeros_like(image)
    for tile in range(tiles):
        placed = jnp.pad(
            grad_tile, ((0, 0), (tile * TILE_COLS, image_cols - (tile + 1) * TILE_COLS), (0, 0))
        )
        grad_conv = jnp.where(tile_index == tile, placed, grad_conv)
    low, high = halo_rows(grad_conv, "row", half_width)
    edge = ((0, 0), (half_width, half_width), (0, 0))
    low = jnp.pad(low.astype(jnp.float32), edge)
    high = jnp.pad(high.astype(jnp.float32), edge)
    halo_out = []
    for out_row in range(image_rows):
        total = jnp.zeros((image_cols, channels), jnp.float32)
        for row_tap in range(KERNEL):
            source = out_row + row_tap
            if source < half_width:
                line = low[source]
            elif source >= half_width + image_rows:
                line = high[source - half_width - image_rows]
            else:
                continue
            for col_tap in range(KERNEL):
                total = total + line[col_tap : col_tap + image_cols] * flipped[row_tap, col_tap]
        halo_out.append(total)
    conv_back = own_full + jnp.stack(halo_out)
    grad_image = (cotangent.astype(jnp.float32) + conv_back).astype(jnp.bfloat16)
    return (block_out, grad_image, grad_w_in, grad_w_out, small_grads)


def solution(mesh):
    placed = (
        P(("group", "row"), None, None),
        P(("group", "row"), None),
        P(),
        P(),
        P(),
        P(),
        P(),
        P(("group", "row"), None, None),
    )
    return jax.shard_map(
        shards,
        mesh=mesh,
        in_specs=placed,
        out_specs=(
            P(("group", "row"), None, None),
            P(("group", "row"), None, None),
            P(("group", "row"), None),
            P(("group", "row"), None),
            P("group", None),
        ),
        check_vma=False,
    )
```

```python
import jax
import jax.numpy as jnp
from jax import lax
from jax.sharding import PartitionSpec as P

KERNEL = 7
TILE_ROWS = 4
TILE_COLS = 128


EPSILON = 1e-06
ROOT_TWO_PI = 0.7978845608028654
CUBIC_TERM = 0.044715


def padded_2(block, sides, width):
    for axis, dim in sides:
        count = lax.axis_size(axis)
        forward = [(i, i + 1) for i in range(count - 1)]
        backward = [(target, source) for source, target in forward]
        low = lax.ppermute(
            lax.slice_in_dim(block, block.shape[dim] - width, None, axis=dim), axis, forward
        )
        high = lax.ppermute(lax.slice_in_dim(block, 0, width, axis=dim), axis, backward)
        block = jnp.concatenate([low, block, high], axis=dim)
    return block


def bit_reversed(values, count, steps, axis):
    shape = values.shape
    values = values.reshape(shape[:axis] + (2,) * steps + (shape[axis] // count,) + shape[axis + 1 :])
    order = (
        tuple(range(axis))
        + tuple(axis + steps - 1 - i for i in range(steps))
        + tuple(range(axis + steps, values.ndim))
    )
    return values.transpose(order).reshape(shape)


def split_pair(values):
    high = values.astype(jnp.bfloat16)
    low = (values - high.astype(jnp.float32)).astype(jnp.bfloat16)
    return high, low


def halving_reduce(quartered, rows, whole, axis):
    count = lax.axis_size(axis)
    steps = count.bit_length() - 1
    if (1 << steps) != count:
        return (
            lax.psum_scatter(quartered, axis, scatter_dimension=1, tiled=True),
            lax.psum_scatter(rows, axis, scatter_dimension=0, tiled=True),
            lax.psum(whole, axis),
        )
    me = lax.axis_index(axis)
    quartered = bit_reversed(quartered, count, steps, 1)
    rows = bit_reversed(rows, count, steps, 0)
    quarters, width = quartered.shape[0], quartered.shape[2]
    for step in range(steps):
        bit = (me >> step) & 1
        pairs = [(i, i ^ (1 << step)) for i in range(count)]
        half_q = quartered.shape[1] // 2
        half_r = rows.shape[0] // 2
        keep_q = lax.dynamic_slice_in_dim(quartered, bit * half_q, half_q, axis=1)
        give_q = lax.dynamic_slice_in_dim(quartered, (1 - bit) * half_q, half_q, axis=1)
        keep_r = lax.dynamic_slice_in_dim(rows, bit * half_r, half_r, axis=0)
        give_r = lax.dynamic_slice_in_dim(rows, (1 - bit) * half_r, half_r, axis=0)
        if step == 0:
            got_q, got_r, got_whole = lax.ppermute((give_q, give_r, whole), axis, pairs)
            whole = whole + got_whole
        else:
            high, low = split_pair(whole)
            sent = jnp.concatenate(
                [give_q.astype(jnp.bfloat16).reshape(-1, width), give_r.astype(jnp.bfloat16), high, low],
                axis=0,
            )
            got = lax.ppermute(sent, axis, pairs)
            cut_q = quarters * half_q
            cut_r = cut_q + half_r
            size = whole.shape[0]
            got_q = got[:cut_q].reshape(quarters, half_q, width)
            got_r = got[cut_q:cut_r]
            mine = high.astype(jnp.float32) + low.astype(jnp.float32)
            theirs = got[cut_r : cut_r + size].astype(jnp.float32) + got[cut_r + size :].astype(
                jnp.float32
            )
            whole = mine + theirs
        quartered = keep_q + got_q.astype(jnp.float32)
        rows = keep_r + got_r.astype(jnp.float32)
        quartered, rows, whole = lax.optimization_barrier((quartered, rows, whole))
    return quartered, rows, whole


def halo_rows(block, axis, width):
    count = lax.axis_size(axis)
    forward = [(i, i + 1) for i in range(count - 1)]
    backward = [(target, source) for source, target in forward]
    low = lax.ppermute(lax.slice_in_dim(block, block.shape[0] - width, None, axis=0), axis, forward)
    high = lax.ppermute(lax.slice_in_dim(block, 0, width, axis=0), axis, backward)
    return low, high


def gelu_value(inputs):
    tangent = jnp.tanh(ROOT_TWO_PI * (inputs + CUBIC_TERM * inputs * inputs * inputs))
    return 0.5 * inputs * (1.0 + tangent)


def gelu_slope(inputs):
    tangent = jnp.tanh(ROOT_TWO_PI * (inputs + CUBIC_TERM * inputs * inputs * inputs))
    return 0.5 * (1.0 + tangent) + 0.5 * inputs * (1.0 - tangent * tangent) * ROOT_TWO_PI * (
        1.0 + 3.0 * CUBIC_TERM * inputs * inputs
    )


def depthwise(padded, kernel, image_rows, image_cols):
    total = jnp.zeros((image_rows, image_cols, kernel.shape[-1]), jnp.float32)
    for row_tap in range(KERNEL):
        for col_tap in range(KERNEL):
            total = (
                total
                + padded[row_tap : row_tap + image_rows, col_tap : col_tap + image_cols]
                * kernel[row_tap, col_tap]
            )
    return total


def kernel_terms(padded, grads, image_rows, image_cols):
    collected = []
    for row_tap in range(KERNEL):
        for col_tap in range(KERNEL):
            collected.append(
                jnp.sum(
                    padded[row_tap : row_tap + image_rows, col_tap : col_tap + image_cols] * grads,
                    axis=(0, 1),
                )
            )
    return jnp.stack(collected)


def shards(image, tissue, kernel, ln_gain, w_in, w_out, layer_scale, cotangent):
    half_width = KERNEL // 2
    image_rows, image_cols, channels = image.shape
    hidden = w_in.shape[1]
    span = TILE_COLS + 2 * half_width

    first_col = jnp.argmax(tissue.reshape(-1)).astype(jnp.int32) * TILE_COLS
    extended = padded_2(image, (("row", 0),), half_width)
    padded = jnp.pad(extended, ((0, 0), (half_width, half_width), (0, 0)))
    window = lax.dynamic_slice_in_dim(padded, first_col, span, axis=1).astype(jnp.float32)
    filtered = depthwise(window, kernel, image_rows, TILE_COLS)
    centre = jnp.mean(filtered, axis=-1, keepdims=True)
    centered = filtered - centre
    inv_std = lax.rsqrt(jnp.mean(centered * centered, axis=-1, keepdims=True) + EPSILON)
    standard = centered * inv_std
    normed = (standard * ln_gain).astype(jnp.bfloat16)
    upstream = lax.dynamic_slice_in_dim(cotangent, first_col, TILE_COLS, axis=1).astype(jnp.float32)
    grad_out = (1.0 * layer_scale * upstream).astype(jnp.bfloat16)

    normed_flat = normed.reshape(-1, channels)
    grad_flat = grad_out.reshape(-1, channels)
    pre_act = jnp.dot(normed_flat, w_in, preferred_element_type=jnp.float32)
    act_flat = gelu_value(pre_act).astype(jnp.bfloat16)
    branch = jnp.dot(act_flat, w_out, preferred_element_type=jnp.float32)
    grad_act = jnp.dot(grad_flat, w_out.T, preferred_element_type=jnp.float32)
    pre_flat = (grad_act * gelu_slope(pre_act)).astype(jnp.bfloat16)
    grad_norm = jnp.dot(pre_flat, w_in.T, preferred_element_type=jnp.float32)
    quarters = hidden // channels
    positions = pre_flat.shape[0]
    pre_quarters = pre_flat.reshape(positions, quarters, channels).transpose(1, 0, 2)
    normed_copies = jnp.broadcast_to(normed_flat[None], (quarters, positions, channels))
    partial_in = lax.dot_general(
        normed_copies,
        pre_quarters,
        (((1,), (1,)), ((0,), (0,))),
        preferred_element_type=jnp.float32,
    )
    partial_out = lax.dot_general(
        act_flat, grad_flat, (((0,), (0,)), ((), ())), preferred_element_type=jnp.float32
    )
    branch = branch.reshape(image_rows, TILE_COLS, channels)
    grad_norm = grad_norm.reshape(image_rows, TILE_COLS, channels)
    image_tile = lax.dynamic_slice_in_dim(image, first_col, TILE_COLS, axis=1)
    out_tile = (image_tile.astype(jnp.float32) + 1.0 * layer_scale * branch).astype(jnp.bfloat16)
    block_out = lax.dynamic_update_slice_in_dim(image, out_tile, first_col, axis=1)
    scale_grad = jnp.sum(1.0 * branch * upstream, axis=(0, 1))
    gain_grad = jnp.sum(grad_norm * standard, axis=(0, 1))
    grad_std = grad_norm * ln_gain
    grad_tile = (
        inv_std
        * (
            grad_std
            - jnp.mean(grad_std, axis=-1, keepdims=True)
            - standard * jnp.mean(grad_std * standard, axis=-1, keepdims=True)
        )
    ).astype(jnp.bfloat16)
    kernel_grad = kernel_terms(window, grad_tile.astype(jnp.float32), image_rows, TILE_COLS)
    packed = jnp.concatenate([kernel_grad, gain_grad[None], scale_grad[None]], axis=0)
    owned_in, grad_w_out, small_grads = halving_reduce(partial_in, partial_out, packed, "row")
    grad_w_in = owned_in.transpose(1, 0, 2).reshape(-1, hidden)
    flipped = kernel[::-1, ::-1]
    tile_padded = jnp.pad(
        grad_tile.astype(jnp.float32),
        ((half_width, half_width), (2 * half_width, 2 * half_width), (0, 0)),
    )
    own = depthwise(tile_padded, flipped, image_rows, span)
    tile_index = first_col // TILE_COLS
    own_full = jnp.zeros((image_rows, image_cols, channels), jnp.float32)
    for tile in range(image_cols // TILE_COLS):
        left = tile * TILE_COLS - half_width
        lo, hi = max(left, 0), min(left + span, image_cols)
        placed = jnp.pad(own[:, lo - left : hi - left], ((0, 0), (lo, image_cols - hi), (0, 0)))
        own_full = jnp.where(tile_index == tile, placed, own_full)
    tiles = image_cols // TILE_COLS
    marker = jnp.full((image_rows, 16, channels), first_col // TILE_COLS, jnp.bfloat16)
    tagged = jnp.concatenate([grad_tile, marker], axis=1)
    low_tagged, high_tagged = halo_rows(tagged, "row", half_width)

    def spread(rows_tagged):
        which = rows_tagged[0, TILE_COLS, 0]
        spread_rows = jnp.zeros((half_width, image_cols, channels), jnp.bfloat16)
        for tile in range(tiles):
            placed = jnp.pad(
                rows_tagged[:, :TILE_COLS],
                ((0, 0), (tile * TILE_COLS, image_cols - (tile + 1) * TILE_COLS), (0, 0)),
            )
            spread_rows = jnp.where(which == tile, placed, spread_rows)
        return spread_rows

    low, high = spread(low_tagged), spread(high_tagged)
    edge = ((0, 0), (half_width, half_width), (0, 0))
    low = jnp.pad(low.astype(jnp.float32), edge)
    high = jnp.pad(high.astype(jnp.float32), edge)
    halo_out = []
    for out_row in range(image_rows):
        total = jnp.zeros((image_cols, channels), jnp.float32)
        for row_tap in range(KERNEL):
            source = out_row + row_tap
            if source < half_width:
                line = low[source]
            elif source >= half_width + image_rows:
                line = high[source - half_width - image_rows]
            else:
                continue
            for col_tap in range(KERNEL):
                total = total + line[col_tap : col_tap + image_cols] * flipped[row_tap, col_tap]
        halo_out.append(total)
    conv_back = own_full + jnp.stack(halo_out)
    grad_image = (cotangent.astype(jnp.float32) + conv_back).astype(jnp.bfloat16)
    return (block_out, grad_image, grad_w_in, grad_w_out, small_grads)


def solution(mesh):
    placed = (
        P(("group", "row"), None, None),
        P(("group", "row"), None),
        P(),
        P(),
        P(),
        P(),
        P(),
        P(("group", "row"), None, None),
    )
    return jax.shard_map(
        shards,
        mesh=mesh,
        in_specs=placed,
        out_specs=(
            P(("group", "row"), None, None),
            P(("group", "row"), None, None),
            P(("group", "row"), None),
            P(("group", "row"), None),
            P("group", None),
        ),
        check_vma=False,
    )
```

```python
import jax
import jax.numpy as jnp
from jax import lax
from jax.sharding import PartitionSpec as P

KERNEL = 7
TILE_ROWS = 4
TILE_COLS = 128


EPSILON = 1e-06
ROOT_TWO_PI = 0.7978845608028654
CUBIC_TERM = 0.044715


def padded_2(block, sides, width):
    for axis, dim in sides:
        count = lax.axis_size(axis)
        forward = [(i, i + 1) for i in range(count - 1)]
        backward = [(target, source) for source, target in forward]
        low = lax.ppermute(
            lax.slice_in_dim(block, block.shape[dim] - width, None, axis=dim), axis, forward
        )
        high = lax.ppermute(lax.slice_in_dim(block, 0, width, axis=dim), axis, backward)
        block = jnp.concatenate([low, block, high], axis=dim)
    return block


def bit_reversed(values, count, steps, axis):
    shape = values.shape
    values = values.reshape(shape[:axis] + (2,) * steps + (shape[axis] // count,) + shape[axis + 1 :])
    order = (
        tuple(range(axis))
        + tuple(axis + steps - 1 - i for i in range(steps))
        + tuple(range(axis + steps, values.ndim))
    )
    return values.transpose(order).reshape(shape)


def split_pair(values):
    high = values.astype(jnp.bfloat16)
    low = (values - high.astype(jnp.float32)).astype(jnp.bfloat16)
    return high, low


def halving_reduce(quartered, rows, whole, axis):
    count = lax.axis_size(axis)
    steps = count.bit_length() - 1
    if (1 << steps) != count:
        return (
            lax.psum_scatter(quartered, axis, scatter_dimension=1, tiled=True),
            lax.psum_scatter(rows, axis, scatter_dimension=0, tiled=True),
            lax.psum(whole, axis),
        )
    me = lax.axis_index(axis)
    quartered = bit_reversed(quartered, count, steps, 1)
    rows = bit_reversed(rows, count, steps, 0)
    quarters, width = quartered.shape[0], quartered.shape[2]
    for step in range(steps):
        bit = (me >> step) & 1
        pairs = [(i, i ^ (1 << step)) for i in range(count)]
        half_q = quartered.shape[1] // 2
        half_r = rows.shape[0] // 2
        keep_q = lax.dynamic_slice_in_dim(quartered, bit * half_q, half_q, axis=1)
        give_q = lax.dynamic_slice_in_dim(quartered, (1 - bit) * half_q, half_q, axis=1)
        keep_r = lax.dynamic_slice_in_dim(rows, bit * half_r, half_r, axis=0)
        give_r = lax.dynamic_slice_in_dim(rows, (1 - bit) * half_r, half_r, axis=0)
        if step == 0:
            got_q, got_r, got_whole = lax.ppermute((give_q, give_r, whole), axis, pairs)
            whole = whole + got_whole
        else:
            high, low = split_pair(whole)
            sent = jnp.concatenate(
                [give_q.astype(jnp.bfloat16).reshape(-1, width), give_r.astype(jnp.bfloat16), high, low],
                axis=0,
            )
            got = lax.ppermute(sent, axis, pairs)
            cut_q = quarters * half_q
            cut_r = cut_q + half_r
            size = whole.shape[0]
            got_q = got[:cut_q].reshape(quarters, half_q, width)
            got_r = got[cut_q:cut_r]
            mine = high.astype(jnp.float32) + low.astype(jnp.float32)
            theirs = got[cut_r : cut_r + size].astype(jnp.float32) + got[cut_r + size :].astype(
                jnp.float32
            )
            whole = mine + theirs
        quartered = keep_q + got_q.astype(jnp.float32)
        rows = keep_r + got_r.astype(jnp.float32)
        quartered, rows, whole = lax.optimization_barrier((quartered, rows, whole))
    return quartered, rows, whole


def halo_rows(block, axis, width):
    count = lax.axis_size(axis)
    forward = [(i, i + 1) for i in range(count - 1)]
    backward = [(target, source) for source, target in forward]
    low = lax.ppermute(lax.slice_in_dim(block, block.shape[0] - width, None, axis=0), axis, forward)
    high = lax.ppermute(lax.slice_in_dim(block, 0, width, axis=0), axis, backward)
    return low, high


def pick_cols(values, tile_index, start_of, width):
    chosen = None
    for tile in range(start_of):
        piece = lax.slice_in_dim(values, tile * TILE_COLS, tile * TILE_COLS + width, axis=1)
        chosen = piece if chosen is None else jnp.where(tile_index == tile, piece, chosen)
    return chosen


def gelu_value(inputs):
    tangent = jnp.tanh(ROOT_TWO_PI * (inputs + CUBIC_TERM * inputs * inputs * inputs))
    return 0.5 * inputs * (1.0 + tangent)


def gelu_slope(inputs):
    tangent = jnp.tanh(ROOT_TWO_PI * (inputs + CUBIC_TERM * inputs * inputs * inputs))
    return 0.5 * (1.0 + tangent) + 0.5 * inputs * (1.0 - tangent * tangent) * ROOT_TWO_PI * (
        1.0 + 3.0 * CUBIC_TERM * inputs * inputs
    )


def depthwise(padded, kernel, image_rows, image_cols):
    total = jnp.zeros((image_rows, image_cols, kernel.shape[-1]), jnp.float32)
    for row_tap in range(KERNEL):
        for col_tap in range(KERNEL):
            total = (
                total
                + padded[row_tap : row_tap + image_rows, col_tap : col_tap + image_cols]
                * kernel[row_tap, col_tap]
            )
    return total


def kernel_terms(padded, grads, image_rows, image_cols):
    collected = []
    for row_tap in range(KERNEL):
        for col_tap in range(KERNEL):
            collected.append(
                jnp.sum(
                    padded[row_tap : row_tap + image_rows, col_tap : col_tap + image_cols] * grads,
                    axis=(0, 1),
                )
            )
    return jnp.stack(collected)


def shards(image, tissue, kernel, ln_gain, w_in, w_out, layer_scale, cotangent):
    half_width = KERNEL // 2
    image_rows, image_cols, channels = image.shape
    hidden = w_in.shape[1]
    span = TILE_COLS + 2 * half_width

    first_col = jnp.argmax(tissue.reshape(-1)).astype(jnp.int32) * TILE_COLS
    extended = padded_2(image, (("row", 0),), half_width)
    padded = jnp.pad(extended, ((0, 0), (half_width, half_width), (0, 0)))
    tile_count = image_cols // TILE_COLS
    tile_at = first_col // TILE_COLS
    window = pick_cols(padded, tile_at, tile_count, span).astype(jnp.float32)
    filtered = depthwise(window, kernel, image_rows, TILE_COLS)
    centre = jnp.mean(filtered, axis=-1, keepdims=True)
    centered = filtered - centre
    inv_std = lax.rsqrt(jnp.mean(centered * centered, axis=-1, keepdims=True) + EPSILON)
    standard = centered * inv_std
    normed = (standard * ln_gain).astype(jnp.bfloat16)
    upstream = pick_cols(cotangent, tile_at, tile_count, TILE_COLS).astype(jnp.float32)
    grad_out = (1.0 * layer_scale * upstream).astype(jnp.bfloat16)

    normed_flat = normed.reshape(-1, channels)
    grad_flat = grad_out.reshape(-1, channels)
    pre_act = jnp.dot(normed_flat, w_in, preferred_element_type=jnp.float32)
    act_flat = gelu_value(pre_act).astype(jnp.bfloat16)
    branch = jnp.dot(act_flat, w_out, preferred_element_type=jnp.float32)
    grad_act = jnp.dot(grad_flat, w_out.T, preferred_element_type=jnp.float32)
    pre_flat = (grad_act * gelu_slope(pre_act)).astype(jnp.bfloat16)
    grad_norm = jnp.dot(pre_flat, w_in.T, preferred_element_type=jnp.float32)
    quarters = hidden // channels
    positions = pre_flat.shape[0]
    pre_quarters = pre_flat.reshape(positions, quarters, channels).transpose(1, 0, 2)
    normed_copies = jnp.broadcast_to(normed_flat[None], (quarters, positions, channels))
    partial_in = lax.dot_general(
        normed_copies,
        pre_quarters,
        (((1,), (1,)), ((0,), (0,))),
        preferred_element_type=jnp.float32,
    )
    partial_out = lax.dot_general(
        act_flat, grad_flat, (((0,), (0,)), ((), ())), preferred_element_type=jnp.float32
    )
    branch = branch.reshape(image_rows, TILE_COLS, channels)
    grad_norm = grad_norm.reshape(image_rows, TILE_COLS, channels)
    image_tile = pick_cols(image, tile_at, tile_count, TILE_COLS)
    out_tile = (image_tile.astype(jnp.float32) + 1.0 * layer_scale * branch).astype(jnp.bfloat16)
    block_out = lax.dynamic_update_slice_in_dim(image, out_tile, first_col, axis=1)
    scale_grad = jnp.sum(1.0 * branch * upstream, axis=(0, 1))
    gain_grad = jnp.sum(grad_norm * standard, axis=(0, 1))
    grad_std = grad_norm * ln_gain
    grad_tile = (
        inv_std
        * (
            grad_std
            - jnp.mean(grad_std, axis=-1, keepdims=True)
            - standard * jnp.mean(grad_std * standard, axis=-1, keepdims=True)
        )
    ).astype(jnp.bfloat16)
    kernel_grad = kernel_terms(window, grad_tile.astype(jnp.float32), image_rows, TILE_COLS)
    packed = jnp.concatenate([kernel_grad, gain_grad[None], scale_grad[None]], axis=0)
    owned_in, grad_w_out, small_grads = halving_reduce(partial_in, partial_out, packed, "row")
    grad_w_in = owned_in.transpose(1, 0, 2).reshape(-1, hidden)
    flipped = kernel[::-1, ::-1]
    tile_padded = jnp.pad(
        grad_tile.astype(jnp.float32),
        ((half_width, half_width), (2 * half_width, 2 * half_width), (0, 0)),
    )
    own = depthwise(tile_padded, flipped, image_rows, span)
    tile_index = first_col // TILE_COLS
    own_full = jnp.zeros((image_rows, image_cols, channels), jnp.float32)
    for tile in range(image_cols // TILE_COLS):
        left = tile * TILE_COLS - half_width
        lo, hi = max(left, 0), min(left + span, image_cols)
        placed = jnp.pad(own[:, lo - left : hi - left], ((0, 0), (lo, image_cols - hi), (0, 0)))
        own_full = jnp.where(tile_index == tile, placed, own_full)
    grad_conv = lax.dynamic_update_slice_in_dim(
        jnp.zeros_like(image), grad_tile, first_col, axis=1
    )
    low, high = halo_rows(grad_conv, "row", half_width)
    edge = ((0, 0), (half_width, half_width), (0, 0))
    low = jnp.pad(low.astype(jnp.float32), edge)
    high = jnp.pad(high.astype(jnp.float32), edge)
    halo_out = []
    for out_row in range(image_rows):
        total = jnp.zeros((image_cols, channels), jnp.float32)
        for row_tap in range(KERNEL):
            source = out_row + row_tap
            if source < half_width:
                line = low[source]
            elif source >= half_width + image_rows:
                line = high[source - half_width - image_rows]
            else:
                continue
            for col_tap in range(KERNEL):
                total = total + line[col_tap : col_tap + image_cols] * flipped[row_tap, col_tap]
        halo_out.append(total)
    conv_back = own_full + jnp.stack(halo_out)
    grad_image = (cotangent.astype(jnp.float32) + conv_back).astype(jnp.bfloat16)
    return (block_out, grad_image, grad_w_in, grad_w_out, small_grads)


def solution(mesh):
    placed = (
        P(("group", "row"), None, None),
        P(("group", "row"), None),
        P(),
        P(),
        P(),
        P(),
        P(),
        P(("group", "row"), None, None),
    )
    return jax.shard_map(
        shards,
        mesh=mesh,
        in_specs=placed,
        out_specs=(
            P(("group", "row"), None, None),
            P(("group", "row"), None, None),
            P(("group", "row"), None),
            P(("group", "row"), None),
            P("group", None),
        ),
        check_vma=False,
    )
```

```python
import jax
import jax.numpy as jnp
from jax import lax
from jax.sharding import PartitionSpec as P

KERNEL = 7
TILE_ROWS = 4
TILE_COLS = 128


EPSILON = 1e-06
ROOT_TWO_PI = 0.7978845608028654
CUBIC_TERM = 0.044715


def padded_2(block, sides, width):
    for axis, dim in sides:
        count = lax.axis_size(axis)
        forward = [(i, i + 1) for i in range(count - 1)]
        backward = [(target, source) for source, target in forward]
        low = lax.ppermute(
            lax.slice_in_dim(block, block.shape[dim] - width, None, axis=dim), axis, forward
        )
        high = lax.ppermute(lax.slice_in_dim(block, 0, width, axis=dim), axis, backward)
        block = jnp.concatenate([low, block, high], axis=dim)
    return block


def bit_reversed(values, count, steps, axis):
    shape = values.shape
    values = values.reshape(shape[:axis] + (2,) * steps + (shape[axis] // count,) + shape[axis + 1 :])
    order = (
        tuple(range(axis))
        + tuple(axis + steps - 1 - i for i in range(steps))
        + tuple(range(axis + steps, values.ndim))
    )
    return values.transpose(order).reshape(shape)


def split_pair(values):
    high = values.astype(jnp.bfloat16)
    low = (values - high.astype(jnp.float32)).astype(jnp.bfloat16)
    return high, low


def halving_reduce(quartered, rows, whole, axis):
    count = lax.axis_size(axis)
    steps = count.bit_length() - 1
    if (1 << steps) != count:
        return (
            lax.psum_scatter(quartered, axis, scatter_dimension=1, tiled=True),
            lax.psum_scatter(rows, axis, scatter_dimension=0, tiled=True),
            lax.psum(whole, axis),
        )
    me = lax.axis_index(axis)
    quartered = bit_reversed(quartered, count, steps, 1)
    rows = bit_reversed(rows, count, steps, 0)
    quarters, width = quartered.shape[0], quartered.shape[2]
    for step in range(steps):
        bit = (me >> step) & 1
        pairs = [(i, i ^ (1 << step)) for i in range(count)]
        half_q = quartered.shape[1] // 2
        half_r = rows.shape[0] // 2
        keep_q = lax.dynamic_slice_in_dim(quartered, bit * half_q, half_q, axis=1)
        give_q = lax.dynamic_slice_in_dim(quartered, (1 - bit) * half_q, half_q, axis=1)
        keep_r = lax.dynamic_slice_in_dim(rows, bit * half_r, half_r, axis=0)
        give_r = lax.dynamic_slice_in_dim(rows, (1 - bit) * half_r, half_r, axis=0)
        if step == 0:
            got_q, got_r, got_whole = lax.ppermute((give_q, give_r, whole), axis, pairs)
            whole = whole + got_whole
        else:
            high, low = split_pair(whole)
            sent = jnp.concatenate(
                [give_q.astype(jnp.bfloat16).reshape(-1, width), give_r.astype(jnp.bfloat16), high, low],
                axis=0,
            )
            got = lax.ppermute(sent, axis, pairs)
            cut_q = quarters * half_q
            cut_r = cut_q + half_r
            size = whole.shape[0]
            got_q = got[:cut_q].reshape(quarters, half_q, width)
            got_r = got[cut_q:cut_r]
            mine = high.astype(jnp.float32) + low.astype(jnp.float32)
            theirs = got[cut_r : cut_r + size].astype(jnp.float32) + got[cut_r + size :].astype(
                jnp.float32
            )
            whole = mine + theirs
        quartered = keep_q + got_q.astype(jnp.float32)
        rows = keep_r + got_r.astype(jnp.float32)
        quartered, rows, whole = lax.optimization_barrier((quartered, rows, whole))
    return quartered, rows, whole


def halo_rows(block, axis, width):
    count = lax.axis_size(axis)
    forward = [(i, i + 1) for i in range(count - 1)]
    backward = [(target, source) for source, target in forward]
    low = lax.ppermute(lax.slice_in_dim(block, block.shape[0] - width, None, axis=0), axis, forward)
    high = lax.ppermute(lax.slice_in_dim(block, 0, width, axis=0), axis, backward)
    return low, high


def pick_cols(values, tile_index, start_of, width):
    chosen = None
    for tile in range(start_of):
        piece = lax.slice_in_dim(values, tile * TILE_COLS, tile * TILE_COLS + width, axis=1)
        chosen = piece if chosen is None else jnp.where(tile_index == tile, piece, chosen)
    return chosen


def gelu_value(inputs):
    tangent = jnp.tanh(ROOT_TWO_PI * (inputs + CUBIC_TERM * inputs * inputs * inputs))
    return 0.5 * inputs * (1.0 + tangent)


def gelu_slope(inputs):
    tangent = jnp.tanh(ROOT_TWO_PI * (inputs + CUBIC_TERM * inputs * inputs * inputs))
    return 0.5 * (1.0 + tangent) + 0.5 * inputs * (1.0 - tangent * tangent) * ROOT_TWO_PI * (
        1.0 + 3.0 * CUBIC_TERM * inputs * inputs
    )


def depthwise(padded, kernel, image_rows, image_cols):
    total = jnp.zeros((image_rows, image_cols, kernel.shape[-1]), jnp.float32)
    for row_tap in range(KERNEL):
        for col_tap in range(KERNEL):
            total = (
                total
                + padded[row_tap : row_tap + image_rows, col_tap : col_tap + image_cols]
                * kernel[row_tap, col_tap]
            )
    return total


def kernel_terms(padded, grads, image_rows, image_cols):
    collected = []
    for row_tap in range(KERNEL):
        for col_tap in range(KERNEL):
            collected.append(
                jnp.sum(
                    padded[row_tap : row_tap + image_rows, col_tap : col_tap + image_cols] * grads,
                    axis=(0, 1),
                )
            )
    return jnp.stack(collected)


def shards(image, tissue, kernel, ln_gain, w_in, w_out, layer_scale, cotangent):
    half_width = KERNEL // 2
    image_rows, image_cols, channels = image.shape
    hidden = w_in.shape[1]
    span = TILE_COLS + 2 * half_width

    first_col = jnp.argmax(tissue.reshape(-1)).astype(jnp.int32) * TILE_COLS
    extended = padded_2(image, (("row", 0),), half_width)
    padded = jnp.pad(extended, ((0, 0), (half_width, half_width), (0, 0)))
    tile_count = image_cols // TILE_COLS
    tile_at = first_col // TILE_COLS
    window = pick_cols(padded, tile_at, tile_count, span).astype(jnp.float32)
    filtered = depthwise(window, kernel, image_rows, TILE_COLS)
    centre = jnp.mean(filtered, axis=-1, keepdims=True)
    centered = filtered - centre
    inv_std = lax.rsqrt(jnp.mean(centered * centered, axis=-1, keepdims=True) + EPSILON)
    standard = centered * inv_std
    normed = (standard * ln_gain).astype(jnp.bfloat16)
    upstream = pick_cols(cotangent, tile_at, tile_count, TILE_COLS).astype(jnp.float32)
    grad_out = (1.0 * layer_scale * upstream).astype(jnp.bfloat16)

    normed_flat = normed.reshape(-1, channels)
    grad_flat = grad_out.reshape(-1, channels)
    pre_act = jnp.dot(normed_flat, w_in, preferred_element_type=jnp.float32)
    act_flat = gelu_value(pre_act).astype(jnp.bfloat16)
    branch = jnp.dot(act_flat, w_out, preferred_element_type=jnp.float32)
    grad_act = jnp.dot(grad_flat, w_out.T, preferred_element_type=jnp.float32)
    pre_flat = (grad_act * gelu_slope(pre_act)).astype(jnp.bfloat16)
    grad_norm = jnp.dot(pre_flat, w_in.T, preferred_element_type=jnp.float32)
    quarters = hidden // channels
    positions = pre_flat.shape[0]
    pre_quarters = pre_flat.reshape(positions, quarters, channels).transpose(1, 0, 2)
    normed_copies = jnp.broadcast_to(normed_flat[None], (quarters, positions, channels))
    partial_in = lax.dot_general(
        normed_copies,
        pre_quarters,
        (((1,), (1,)), ((0,), (0,))),
        preferred_element_type=jnp.float32,
    )
    partial_out = lax.dot_general(
        act_flat, grad_flat, (((0,), (0,)), ((), ())), preferred_element_type=jnp.float32
    )
    branch = branch.reshape(image_rows, TILE_COLS, channels)
    grad_norm = grad_norm.reshape(image_rows, TILE_COLS, channels)
    image_tile = pick_cols(image, tile_at, tile_count, TILE_COLS)
    out_tile = (image_tile.astype(jnp.float32) + 1.0 * layer_scale * branch).astype(jnp.bfloat16)
    block_out = image
    for tile in range(tile_count):
        placed = jnp.concatenate(
            [image[:, : tile * TILE_COLS], out_tile, image[:, (tile + 1) * TILE_COLS :]], axis=1
        )
        block_out = jnp.where(tile_at == tile, placed, block_out)
    scale_grad = jnp.sum(1.0 * branch * upstream, axis=(0, 1))
    gain_grad = jnp.sum(grad_norm * standard, axis=(0, 1))
    grad_std = grad_norm * ln_gain
    grad_tile = (
        inv_std
        * (
            grad_std
            - jnp.mean(grad_std, axis=-1, keepdims=True)
            - standard * jnp.mean(grad_std * standard, axis=-1, keepdims=True)
        )
    ).astype(jnp.bfloat16)
    kernel_grad = kernel_terms(window, grad_tile.astype(jnp.float32), image_rows, TILE_COLS)
    packed = jnp.concatenate([kernel_grad, gain_grad[None], scale_grad[None]], axis=0)
    owned_in, grad_w_out, small_grads = halving_reduce(partial_in, partial_out, packed, "row")
    grad_w_in = owned_in.transpose(1, 0, 2).reshape(-1, hidden)
    flipped = kernel[::-1, ::-1]
    tile_padded = jnp.pad(
        grad_tile.astype(jnp.float32),
        ((half_width, half_width), (2 * half_width, 2 * half_width), (0, 0)),
    )
    own = depthwise(tile_padded, flipped, image_rows, span)
    tile_index = first_col // TILE_COLS
    own_full = jnp.zeros((image_rows, image_cols, channels), jnp.float32)
    for tile in range(image_cols // TILE_COLS):
        left = tile * TILE_COLS - half_width
        lo, hi = max(left, 0), min(left + span, image_cols)
        placed = jnp.pad(own[:, lo - left : hi - left], ((0, 0), (lo, image_cols - hi), (0, 0)))
        own_full = jnp.where(tile_index == tile, placed, own_full)
    grad_conv = jnp.zeros_like(image)
    for tile in range(tile_count):
        placed = jnp.pad(
            grad_tile, ((0, 0), (tile * TILE_COLS, image_cols - (tile + 1) * TILE_COLS), (0, 0))
        )
        grad_conv = jnp.where(tile_at == tile, placed, grad_conv)
    low, high = halo_rows(grad_conv, "row", half_width)
    edge = ((0, 0), (half_width, half_width), (0, 0))
    low = jnp.pad(low.astype(jnp.float32), edge)
    high = jnp.pad(high.astype(jnp.float32), edge)
    halo_out = []
    for out_row in range(image_rows):
        total = jnp.zeros((image_cols, channels), jnp.float32)
        for row_tap in range(KERNEL):
            source = out_row + row_tap
            if source < half_width:
                line = low[source]
            elif source >= half_width + image_rows:
                line = high[source - half_width - image_rows]
            else:
                continue
            for col_tap in range(KERNEL):
                total = total + line[col_tap : col_tap + image_cols] * flipped[row_tap, col_tap]
        halo_out.append(total)
    conv_back = own_full + jnp.stack(halo_out)
    grad_image = (cotangent.astype(jnp.float32) + conv_back).astype(jnp.bfloat16)
    return (block_out, grad_image, grad_w_in, grad_w_out, small_grads)


def solution(mesh):
    placed = (
        P(("group", "row"), None, None),
        P(("group", "row"), None),
        P(),
        P(),
        P(),
        P(),
        P(),
        P(("group", "row"), None, None),
    )
    return jax.shard_map(
        shards,
        mesh=mesh,
        in_specs=placed,
        out_specs=(
            P(("group", "row"), None, None),
            P(("group", "row"), None, None),
            P(("group", "row"), None),
            P(("group", "row"), None),
            P("group", None),
        ),
        check_vma=False,
    )
```

```python
import jax
import jax.numpy as jnp
from jax import lax
from jax.sharding import PartitionSpec as P

KERNEL = 7
TILE_ROWS = 4
TILE_COLS = 128


EPSILON = 1e-06
ROOT_TWO_PI = 0.7978845608028654
CUBIC_TERM = 0.044715


def padded_2(block, sides, width):
    for axis, dim in sides:
        count = lax.axis_size(axis)
        forward = [(i, i + 1) for i in range(count - 1)]
        backward = [(target, source) for source, target in forward]
        low = lax.ppermute(
            lax.slice_in_dim(block, block.shape[dim] - width, None, axis=dim), axis, forward
        )
        high = lax.ppermute(lax.slice_in_dim(block, 0, width, axis=dim), axis, backward)
        block = jnp.concatenate([low, block, high], axis=dim)
    return block


def bit_reversed(values, count, steps, axis):
    shape = values.shape
    values = values.reshape(shape[:axis] + (2,) * steps + (shape[axis] // count,) + shape[axis + 1 :])
    order = (
        tuple(range(axis))
        + tuple(axis + steps - 1 - i for i in range(steps))
        + tuple(range(axis + steps, values.ndim))
    )
    return values.transpose(order).reshape(shape)


def split_pair(values):
    high = values.astype(jnp.bfloat16)
    low = (values - high.astype(jnp.float32)).astype(jnp.bfloat16)
    return high, low


def halving_reduce(quartered, rows, whole, axis):
    count = lax.axis_size(axis)
    steps = count.bit_length() - 1
    if (1 << steps) != count:
        return (
            lax.psum_scatter(quartered, axis, scatter_dimension=1, tiled=True),
            lax.psum_scatter(rows, axis, scatter_dimension=0, tiled=True),
            lax.psum(whole, axis),
        )
    me = lax.axis_index(axis)
    quartered = bit_reversed(quartered, count, steps, 1)
    rows = bit_reversed(rows, count, steps, 0)
    quarters, width = quartered.shape[0], quartered.shape[2]
    for step in range(steps):
        bit = (me >> step) & 1
        pairs = [(i, i ^ (1 << step)) for i in range(count)]
        half_q = quartered.shape[1] // 2
        half_r = rows.shape[0] // 2
        keep_q = lax.dynamic_slice_in_dim(quartered, bit * half_q, half_q, axis=1)
        give_q = lax.dynamic_slice_in_dim(quartered, (1 - bit) * half_q, half_q, axis=1)
        keep_r = lax.dynamic_slice_in_dim(rows, bit * half_r, half_r, axis=0)
        give_r = lax.dynamic_slice_in_dim(rows, (1 - bit) * half_r, half_r, axis=0)
        if step == 0:
            got_q, got_r, got_whole = lax.ppermute((give_q, give_r, whole), axis, pairs)
            whole = whole + got_whole
        else:
            high, low = split_pair(whole)
            sent = jnp.concatenate(
                [give_q.astype(jnp.bfloat16).reshape(-1, width), give_r.astype(jnp.bfloat16), high, low],
                axis=0,
            )
            got = lax.ppermute(sent, axis, pairs)
            cut_q = quarters * half_q
            cut_r = cut_q + half_r
            size = whole.shape[0]
            got_q = got[:cut_q].reshape(quarters, half_q, width)
            got_r = got[cut_q:cut_r]
            mine = high.astype(jnp.float32) + low.astype(jnp.float32)
            theirs = got[cut_r : cut_r + size].astype(jnp.float32) + got[cut_r + size :].astype(
                jnp.float32
            )
            whole = mine + theirs
        quartered = keep_q + got_q.astype(jnp.float32)
        rows = keep_r + got_r.astype(jnp.float32)
    return quartered, rows, whole


def halo_rows(block, axis, width):
    count = lax.axis_size(axis)
    forward = [(i, i + 1) for i in range(count - 1)]
    backward = [(target, source) for source, target in forward]
    low = lax.ppermute(lax.slice_in_dim(block, block.shape[0] - width, None, axis=0), axis, forward)
    high = lax.ppermute(lax.slice_in_dim(block, 0, width, axis=0), axis, backward)
    return low, high


def pick_cols(values, tile_index, start_of, width):
    chosen = None
    for tile in range(start_of):
        piece = lax.slice_in_dim(values, tile * TILE_COLS, tile * TILE_COLS + width, axis=1)
        chosen = piece if chosen is None else jnp.where(tile_index == tile, piece, chosen)
    return chosen


def gelu_value(inputs):
    tangent = jnp.tanh(ROOT_TWO_PI * (inputs + CUBIC_TERM * inputs * inputs * inputs))
    return 0.5 * inputs * (1.0 + tangent)


def gelu_slope(inputs):
    tangent = jnp.tanh(ROOT_TWO_PI * (inputs + CUBIC_TERM * inputs * inputs * inputs))
    return 0.5 * (1.0 + tangent) + 0.5 * inputs * (1.0 - tangent * tangent) * ROOT_TWO_PI * (
        1.0 + 3.0 * CUBIC_TERM * inputs * inputs
    )


def depthwise(padded, kernel, image_rows, image_cols):
    total = jnp.zeros((image_rows, image_cols, kernel.shape[-1]), jnp.float32)
    for row_tap in range(KERNEL):
        for col_tap in range(KERNEL):
            total = (
                total
                + padded[row_tap : row_tap + image_rows, col_tap : col_tap + image_cols]
                * kernel[row_tap, col_tap]
            )
    return total


def kernel_terms(padded, grads, image_rows, image_cols):
    collected = []
    for row_tap in range(KERNEL):
        for col_tap in range(KERNEL):
            collected.append(
                jnp.sum(
                    padded[row_tap : row_tap + image_rows, col_tap : col_tap + image_cols] * grads,
                    axis=(0, 1),
                )
            )
    return jnp.stack(collected)


def shards(image, tissue, kernel, ln_gain, w_in, w_out, layer_scale, cotangent):
    half_width = KERNEL // 2
    image_rows, image_cols, channels = image.shape
    hidden = w_in.shape[1]
    span = TILE_COLS + 2 * half_width

    first_col = jnp.argmax(tissue.reshape(-1)).astype(jnp.int32) * TILE_COLS
    extended = padded_2(image, (("row", 0),), half_width)
    padded = jnp.pad(extended, ((0, 0), (half_width, half_width), (0, 0)))
    tile_count = image_cols // TILE_COLS
    tile_at = first_col // TILE_COLS
    window = pick_cols(padded, tile_at, tile_count, span).astype(jnp.float32)
    filtered = depthwise(window, kernel, image_rows, TILE_COLS)
    centre = jnp.mean(filtered, axis=-1, keepdims=True)
    centered = filtered - centre
    inv_std = lax.rsqrt(jnp.mean(centered * centered, axis=-1, keepdims=True) + EPSILON)
    standard = centered * inv_std
    normed = (standard * ln_gain).astype(jnp.bfloat16)
    upstream = pick_cols(cotangent, tile_at, tile_count, TILE_COLS).astype(jnp.float32)
    grad_out = (1.0 * layer_scale * upstream).astype(jnp.bfloat16)

    normed_flat = normed.reshape(-1, channels)
    grad_flat = grad_out.reshape(-1, channels)
    pre_act = jnp.dot(normed_flat, w_in, preferred_element_type=jnp.float32)
    act_flat = gelu_value(pre_act).astype(jnp.bfloat16)
    branch = jnp.dot(act_flat, w_out, preferred_element_type=jnp.float32)
    grad_act = jnp.dot(grad_flat, w_out.T, preferred_element_type=jnp.float32)
    pre_flat = (grad_act * gelu_slope(pre_act)).astype(jnp.bfloat16)
    grad_norm = jnp.dot(pre_flat, w_in.T, preferred_element_type=jnp.float32)
    quarters = hidden // channels
    positions = pre_flat.shape[0]
    pre_quarters = pre_flat.reshape(positions, quarters, channels).transpose(1, 0, 2)
    normed_copies = jnp.broadcast_to(normed_flat[None], (quarters, positions, channels))
    partial_in = lax.dot_general(
        normed_copies,
        pre_quarters,
        (((1,), (1,)), ((0,), (0,))),
        preferred_element_type=jnp.float32,
    )
    partial_out = lax.dot_general(
        act_flat, grad_flat, (((0,), (0,)), ((), ())), preferred_element_type=jnp.float32
    )
    branch = branch.reshape(image_rows, TILE_COLS, channels)
    grad_norm = grad_norm.reshape(image_rows, TILE_COLS, channels)
    image_tile = pick_cols(image, tile_at, tile_count, TILE_COLS)
    out_tile = (image_tile.astype(jnp.float32) + 1.0 * layer_scale * branch).astype(jnp.bfloat16)
    block_out = lax.dynamic_update_slice_in_dim(image, out_tile, first_col, axis=1)
    scale_grad = jnp.sum(1.0 * branch * upstream, axis=(0, 1))
    gain_grad = jnp.sum(grad_norm * standard, axis=(0, 1))
    grad_std = grad_norm * ln_gain
    grad_tile = (
        inv_std
        * (
            grad_std
            - jnp.mean(grad_std, axis=-1, keepdims=True)
            - standard * jnp.mean(grad_std * standard, axis=-1, keepdims=True)
        )
    ).astype(jnp.bfloat16)
    kernel_grad = kernel_terms(window, grad_tile.astype(jnp.float32), image_rows, TILE_COLS)
    packed = jnp.concatenate([kernel_grad, gain_grad[None], scale_grad[None]], axis=0)
    owned_in, grad_w_out, small_grads = halving_reduce(partial_in, partial_out, packed, "row")
    grad_w_in = owned_in.transpose(1, 0, 2).reshape(-1, hidden)
    flipped = kernel[::-1, ::-1]
    tile_padded = jnp.pad(
        grad_tile.astype(jnp.float32),
        ((half_width, half_width), (2 * half_width, 2 * half_width), (0, 0)),
    )
    own = depthwise(tile_padded, flipped, image_rows, span)
    tile_index = first_col // TILE_COLS
    own_full = jnp.zeros((image_rows, image_cols, channels), jnp.float32)
    for tile in range(image_cols // TILE_COLS):
        left = tile * TILE_COLS - half_width
        lo, hi = max(left, 0), min(left + span, image_cols)
        placed = jnp.pad(own[:, lo - left : hi - left], ((0, 0), (lo, image_cols - hi), (0, 0)))
        own_full = jnp.where(tile_index == tile, placed, own_full)
    grad_conv = lax.dynamic_update_slice_in_dim(
        jnp.zeros_like(image), grad_tile, first_col, axis=1
    )
    low, high = halo_rows(grad_conv, "row", half_width)
    edge = ((0, 0), (half_width, half_width), (0, 0))
    low = jnp.pad(low.astype(jnp.float32), edge)
    high = jnp.pad(high.astype(jnp.float32), edge)
    halo_out = []
    for out_row in range(image_rows):
        total = jnp.zeros((image_cols, channels), jnp.float32)
        for row_tap in range(KERNEL):
            source = out_row + row_tap
            if source < half_width:
                line = low[source]
            elif source >= half_width + image_rows:
                line = high[source - half_width - image_rows]
            else:
                continue
            for col_tap in range(KERNEL):
                total = total + line[col_tap : col_tap + image_cols] * flipped[row_tap, col_tap]
        halo_out.append(total)
    conv_back = own_full + jnp.stack(halo_out)
    grad_image = (cotangent.astype(jnp.float32) + conv_back).astype(jnp.bfloat16)
    return (block_out, grad_image, grad_w_in, grad_w_out, small_grads)


def solution(mesh):
    placed = (
        P(("group", "row"), None, None),
        P(("group", "row"), None),
        P(),
        P(),
        P(),
        P(),
        P(),
        P(("group", "row"), None, None),
    )
    return jax.shard_map(
        shards,
        mesh=mesh,
        in_specs=placed,
        out_specs=(
            P(("group", "row"), None, None),
            P(("group", "row"), None, None),
            P(("group", "row"), None),
            P(("group", "row"), None),
            P("group", None),
        ),
        check_vma=False,
    )
```
